32 devices in a mesh: ctx: 4 (over x, core), ep: 8 (over z, y).
Axes of the slice: x: 2, y: 2, z: 4, core: 2. Of those that a mesh axis runs over, the one named last changes fastest.
Arguments:
- query_latent: bfloat16 [1, 512, 128, 512], P(None, 'ctx', 'ep'), may hold values from -6 to 6
- query_rope: bfloat16 [1, 128, 64, 512], P(None, 'ep', None, 'ctx'), may hold values from -12 to 12
- key_latent: bfloat16 [1, 512, 512], P(None, 'ctx'), may hold values from -6 to 6
- key_rope: bfloat16 [1, 64, 512], P(None, None, 'ctx'), may hold values from -14 to 14
- output_grad: bfloat16 [1, 512, 128, 512], P(None, 'ctx', 'ep'), may hold values from -6 to 6
Outputs:
- attended: bfloat16 [1, 512, 128, 512], P(None, 'ctx', 'ep')
- query_latent_grad: bfloat16 [1, 512, 128, 512], P(None, 'ctx', 'ep')
- query_rope_grad: bfloat16 [1, 128, 64, 512], P(None, 'ep', None, 'ctx')
- key_latent_grad: bfloat16 [1, 512, 512], P(None, 'ctx')
- key_rope_grad: bfloat16 [1, 64, 512], P(None, None, 'ctx')
The draws below stay inside these ranges and needn't reach their ends.
All inputs are finite; a program needn't handle non-finite values.
Results may differ from the reference program's by a relative error of at most 0.018.
Values may be sent and summed in bfloat16 or wider, within the bound.
No kernel may reach another device: no remote copies, remote signals or barrier semaphores. Data moves between devices by JAX's collectives and lax.ppermute only.
A program may use at most 64 MiB of HBM per device.

```python
import jax
import jax.numpy as jnp
from jax import lax

HEADS = 128
KVR = 512
ROPE = 64
SEQS = 1
TOK_DEV = 128
LEN = 512
N_CTX = 4
N_EP = 8


def draw_key_rope(key, part):
    field = jnp.clip(jax.random.normal(jax.random.fold_in(key, 1), (SEQS, ROPE, LEN), jnp.float32), -6.0, 6.0)
    return field.astype(jnp.bfloat16)


def draw_query_rope(key, part):
    field = jnp.clip(jax.random.normal(jax.random.fold_in(key, 2), (SEQS, HEADS, ROPE, LEN), jnp.float32), -6.0, 6.0)
    return field.astype(jnp.bfloat16)


def block_levels(key, shape, shards, least, high):
    def one(axis_at, blocks):
        steps = jax.random.uniform(jax.random.fold_in(jax.random.fold_in(key, 6), axis_at), (blocks,), jnp.float32, least / len(shards), high / len(shards))
        return jnp.repeat(jnp.exp(steps), shape[axis_at] // blocks).reshape((-1,) + (1,) * (len(shape) - axis_at - 1))

    loudness = one(*shards[0])
    for cut in shards[1:]:
        loudness = loudness * one(*cut)
    return loudness


def centred(stream_key, shape, width, most, cuts=(), kind=jnp.bfloat16):
    values = jax.random.normal(stream_key, shape, jnp.float32) * width
    if len(cuts) > 0:
        values = block_levels(stream_key, shape, cuts, -0.22, 0.18) * values
    return jnp.clip(values, min=-most, max=most).astype(kind)


def setup_inputs(seed: int = 0) -> dict:
    key_list = jax.random.split(jax.random.key(seed), 6)
    query_latent = centred(key_list[0], (SEQS, LEN, HEADS, KVR), 1.0, 6.0, ((1, 4), (2, 8)))
    query_rope = draw_query_rope(jax.random.fold_in(key_list[5], 71), 0)
    key_latent = centred(key_list[2], (SEQS, LEN, KVR), 1.0, 6.0, ((1, 4),))
    key_rope = draw_key_rope(jax.random.fold_in(key_list[5], 71), 0)
    output_grad = centred(key_list[4], (SEQS, LEN, HEADS, KVR), 1.0, 6.0, ((1, 4), (2, 8)))
    return {"query_latent": query_latent, "query_rope": query_rope, "key_latent": key_latent, "key_rope": key_rope, "output_grad": output_grad}


scale_factor = 192.0 ** -0.5


def round_half(values):
    return lax.optimization_barrier(values.astype(jnp.bfloat16)).astype(jnp.float32)


def reference(query_latent, query_rope, key_latent, key_rope, output_grad):
    group_heads = HEADS // N_EP
    positions = jnp.arange(LEN, dtype=jnp.int32)
    allowed = positions[None, :] <= positions[:, None]
    latent = key_latent.astype(jnp.float32)
    rope = key_rope.astype(jnp.float32)

    def group_terms(group):
        head_start = (group * group_heads).astype(jnp.int32)
        qlat = lax.dynamic_slice_in_dim(query_latent, head_start, group_heads, 2).astype(jnp.float32)
        qrot = lax.dynamic_slice_in_dim(query_rope, head_start, group_heads, 1).astype(jnp.float32)
        cotan = lax.dynamic_slice_in_dim(output_grad, head_start, group_heads, 2).astype(jnp.float32)
        scores = (jnp.einsum('sthd,sjd->shtj', qlat, latent) + jnp.einsum('shdt,sdj->shtj', qrot, rope)) * scale_factor
        scores = jnp.where(allowed, scores, jnp.float32(-1e30))
        row_max = jnp.max(scores, axis=-1, keepdims=True)
        powers = jnp.exp(scores - row_max)
        weights = powers / jnp.sum(powers, axis=-1, keepdims=True)
        rounded_weights = round_half(weights)
        attended = jnp.einsum('shtj,sjd->sthd', rounded_weights, latent).astype(jnp.bfloat16)
        row_dots = jnp.transpose(jnp.sum(cotan * attended.astype(jnp.float32), axis=-1), (0, 2, 1))
        weight_grad = jnp.einsum('sthd,sjd->shtj', cotan, latent)
        score_grad = round_half(weights * (weight_grad - row_dots[..., None]))
        qlat_grad = (scale_factor * jnp.einsum('shtj,sjd->sthd', score_grad, latent)).astype(jnp.bfloat16)
        qrot_grad = (scale_factor * jnp.einsum('shtj,sdj->shdt', score_grad, rope)).astype(jnp.bfloat16)
        grad_split = score_grad.reshape(SEQS, group_heads, N_CTX, TOK_DEV, LEN)
        weight_split = rounded_weights.reshape(SEQS, group_heads, N_CTX, TOK_DEV, LEN)
        qlat_split = qlat.reshape(SEQS, N_CTX, TOK_DEV, group_heads, KVR)
        cotan_split = cotan.reshape(SEQS, N_CTX, TOK_DEV, group_heads, KVR)
        qrot_split = qrot.reshape(SEQS, group_heads, ROPE, N_CTX, TOK_DEV)
        latent_terms = scale_factor * jnp.einsum('shbuj,sbuhd->sbjd', grad_split, qlat_split) + jnp.einsum('shbuj,sbuhd->sbjd', weight_split, cotan_split)
        rope_terms = scale_factor * jnp.einsum('shbuj,shdbu->sbdj', grad_split, qrot_split)
        latent_sum = jnp.sum(round_half(latent_terms), axis=1)
        rope_sum = jnp.sum(round_half(rope_terms), axis=1)
        return attended, qlat_grad, qrot_grad, latent_sum, rope_sum

    attended, qlat_grad, qrot_grad, latent_sum, rope_sum = lax.map(group_terms, jnp.arange(N_EP, dtype=jnp.int32))
    attended = jnp.transpose(attended, (1, 2, 0, 3, 4)).reshape(SEQS, LEN, HEADS, KVR)
    qlat_grad = jnp.transpose(qlat_grad, (1, 2, 0, 3, 4)).reshape(SEQS, LEN, HEADS, KVR)
    qrot_grad = jnp.transpose(qrot_grad, (1, 0, 2, 3, 4)).reshape(SEQS, HEADS, ROPE, LEN)
    key_latent_grad = jnp.sum(latent_sum, axis=0).astype(jnp.bfloat16)
    key_rope_grad = jnp.sum(rope_sum, axis=0).astype(jnp.bfloat16)
    return (attended, qlat_grad, qrot_grad, key_latent_grad, key_rope_grad)
```

```python
import jax
import jax.numpy as jnp
from jax import lax
from jax.sharding import PartitionSpec as P

scale_factor = 192.0 ** (-0.5)


def causal_reduce_ctx(blocks, n_ctx):
    here = lax.axis_index("ctx")
    total = jnp.take(blocks, here, axis=0).astype(jnp.float32)
    for shift in range(1, n_ctx):
        sent = jnp.take(blocks, jnp.maximum(here - shift, 0), axis=0)
        got = lax.ppermute(sent, "ctx", [(i, i - shift) for i in range(shift, n_ctx)])
        total = total + got.astype(jnp.float32)
    return total


def butterfly_sum_ep(total, n_ep):
    if n_ep & (n_ep - 1):
        return lax.psum(total.astype(jnp.bfloat16), "ep").astype(jnp.float32)
    bit = 1
    while bit < n_ep:
        mine = total.astype(jnp.bfloat16)
        theirs = lax.ppermute(mine, "ep", [(i, i ^ bit) for i in range(n_ep)])
        total = mine.astype(jnp.float32) + theirs.astype(jnp.float32)
        bit *= 2
    return total


def body(query_latent, query_rope, key_latent, key_rope, output_grad):
    n_ctx = lax.axis_size("ctx")
    n_ep = lax.axis_size("ep")
    block_len = query_latent.shape[1]
    kvr = key_latent.shape[2]
    local_keys = jnp.concatenate([key_latent[0], key_rope[0].T], axis=1)
    whole_keys = lax.all_gather(local_keys, "ctx", axis=0, tiled=True)
    whole_latent = whole_keys[None, :, :kvr]
    whole_rope = whole_keys[:, kvr:].T[None]
    length = whole_latent.shape[1]
    offset = lax.axis_index("ctx") * block_len
    query_place = offset + jnp.arange(block_len, dtype=jnp.int32)
    allowed = jnp.arange(length, dtype=jnp.int32)[None, :] <= query_place[:, None]
    scores = jnp.einsum(
        "sthd,sjd->shtj", query_latent, whole_latent, preferred_element_type=jnp.float32
    )
    scores = scores + jnp.einsum(
        "shdt,sdj->shtj", query_rope, whole_rope, preferred_element_type=jnp.float32
    )
    scores = jnp.where(allowed, scores * scale_factor, jnp.float32(-1e30))
    row_max = jnp.max(scores, axis=-1, keepdims=True)
    powers = jnp.exp(scores - row_max)
    weights = powers / jnp.sum(powers, axis=-1, keepdims=True)
    rounded_weights = weights.astype(jnp.bfloat16)
    attended = jnp.einsum(
        "shtj,sjd->sthd", rounded_weights, whole_latent, preferred_element_type=jnp.float32
    ).astype(jnp.bfloat16)
    row_dots = jnp.einsum(
        "sthd,sthd->sht", output_grad, attended, preferred_element_type=jnp.float32
    )
    weight_grad = jnp.einsum(
        "sthd,sjd->shtj", output_grad, whole_latent, preferred_element_type=jnp.float32
    )
    score_grad = (weights * (weight_grad - row_dots[..., None])).astype(jnp.bfloat16)
    latent_qgrad = (
        scale_factor
        * jnp.einsum("shtj,sjd->sthd", score_grad, whole_latent, preferred_element_type=jnp.float32)
    ).astype(jnp.bfloat16)
    rope_qgrad = (
        scale_factor
        * jnp.einsum("shtj,sdj->shdt", score_grad, whole_rope, preferred_element_type=jnp.float32)
    ).astype(jnp.bfloat16)
    latent_term = scale_factor * jnp.einsum(
        "shtj,sthd->jd", score_grad, query_latent, preferred_element_type=jnp.float32
    )
    latent_term = latent_term + jnp.einsum(
        "shtj,sthd->jd", rounded_weights, output_grad, preferred_element_type=jnp.float32
    )
    rope_term = scale_factor * jnp.einsum(
        "shtj,shdt->jd", score_grad, query_rope, preferred_element_type=jnp.float32
    )
    terms = jnp.concatenate([latent_term, rope_term], axis=1).astype(jnp.bfloat16)
    total = causal_reduce_ctx(terms.reshape(n_ctx, block_len, -1), n_ctx)
    total = butterfly_sum_ep(total, n_ep).astype(jnp.bfloat16)
    latent_kgrad = total[None, :, :kvr]
    rope_kgrad = total[:, kvr:].T[None]
    return (attended, latent_qgrad, rope_qgrad, latent_kgrad, rope_kgrad)


def solution(mesh):
    placed = (
        P(None, "ctx", "ep", None),
        P(None, "ep", None, "ctx"),
        P(None, "ctx", None),
        P(None, None, "ctx"),
        P(None, "ctx", "ep", None),
    )
    return jax.shard_map(
        body,
        mesh=mesh,
        in_specs=placed,
        out_specs=(
            P(None, "ctx", "ep", None),
            P(None, "ctx", "ep", None),
            P(None, "ep", None, "ctx"),
            P(None, "ctx", None),
            P(None, None, "ctx"),
        ),
        check_vma=False,
    )
```

```python
import jax
import jax.numpy as jnp
from jax import lax
from jax.sharding import PartitionSpec as P

scale_factor = 192.0 ** (-0.5)


def causal_reduce_ctx(blocks, n_ctx):
    here = lax.axis_index("ctx")
    total = jnp.take(blocks, here, axis=0).astype(jnp.float32)
    for shift in range(1, n_ctx):
        sent = jnp.take(blocks, jnp.maximum(here - shift, 0), axis=0)
        got = lax.ppermute(sent, "ctx", [(i, i - shift) for i in range(shift, n_ctx)])
        total = total + got.astype(jnp.float32)
    return total


def halving_sum_ep(total, n_ep):
    if n_ep & (n_ep - 1):
        return lax.psum(total.astype(jnp.bfloat16), "ep").astype(jnp.bfloat16)
    n_bits = n_ep.bit_length() - 1
    here = lax.axis_index("ep")
    rows, cols = total.shape
    parts = total.reshape((2,) * n_bits + (rows // n_ep, cols))
    for k in range(n_bits):
        axis = n_bits - 1 - k
        mine = (here >> k) & 1
        keep = jnp.take(parts, mine, axis=axis)
        sent = jnp.take(parts, 1 - mine, axis=axis).astype(jnp.bfloat16)
        got = lax.ppermute(sent, "ep", [(i, i ^ (1 << k)) for i in range(n_ep)])
        parts = keep + got.astype(jnp.float32)
        n_left = n_bits - 1 - k
        parts = parts.reshape((2,) * n_left + (rows // n_ep, cols)) if n_left else parts
    whole = parts.astype(jnp.bfloat16)
    for k in reversed(range(n_bits)):
        mine = (here >> k) & 1
        got = lax.ppermute(whole, "ep", [(i, i ^ (1 << k)) for i in range(n_ep)])
        low = jnp.where(mine == 0, whole, got)
        high = jnp.where(mine == 0, got, whole)
        whole = jnp.stack([low, high], axis=n_bits - 1 - k)
    return whole.reshape(rows, cols)


def body(query_latent, query_rope, key_latent, key_rope, output_grad):
    n_ctx = lax.axis_size("ctx")
    n_ep = lax.axis_size("ep")
    block_len = query_latent.shape[1]
    kvr = key_latent.shape[2]
    local_keys = jnp.concatenate([key_latent[0], key_rope[0].T], axis=1)
    whole_keys = lax.all_gather(local_keys, "ctx", axis=0, tiled=True)
    whole_latent = whole_keys[None, :, :kvr]
    whole_rope = whole_keys[:, kvr:].T[None]
    length = whole_latent.shape[1]
    offset = lax.axis_index("ctx") * block_len
    query_place = offset + jnp.arange(block_len, dtype=jnp.int32)
    allowed = jnp.arange(length, dtype=jnp.int32)[None, :] <= query_place[:, None]
    scores = jnp.einsum(
        "sthd,sjd->shtj", query_latent, whole_latent, preferred_element_type=jnp.float32
    )
    scores = scores + jnp.einsum(
        "shdt,sdj->shtj", query_rope, whole_rope, preferred_element_type=jnp.float32
    )
    scores = jnp.where(allowed, scores * scale_factor, jnp.float32(-1e30))
    row_max = jnp.max(scores, axis=-1, keepdims=True)
    powers = jnp.exp(scores - row_max)
    weights = powers / jnp.sum(powers, axis=-1, keepdims=True)
    rounded_weights = weights.astype(jnp.bfloat16)
    attended = jnp.einsum(
        "shtj,sjd->sthd", rounded_weights, whole_latent, preferred_element_type=jnp.float32
    ).astype(jnp.bfloat16)
    row_dots = jnp.einsum(
        "sthd,sthd->sht", output_grad, attended, preferred_element_type=jnp.float32
    )
    weight_grad = jnp.einsum(
        "sthd,sjd->shtj", output_grad, whole_latent, preferred_element_type=jnp.float32
    )
    score_grad = (weights * (weight_grad - row_dots[..., None])).astype(jnp.bfloat16)
    latent_qgrad = (
        scale_factor
        * jnp.einsum("shtj,sjd->sthd", score_grad, whole_latent, preferred_element_type=jnp.float32)
    ).astype(jnp.bfloat16)
    rope_qgrad = (
        scale_factor
        * jnp.einsum("shtj,sdj->shdt", score_grad, whole_rope, preferred_element_type=jnp.float32)
    ).astype(jnp.bfloat16)
    latent_term = scale_factor * jnp.einsum(
        "shtj,sthd->jd", score_grad, query_latent, preferred_element_type=jnp.float32
    )
    latent_term = latent_term + jnp.einsum(
        "shtj,sthd->jd", rounded_weights, output_grad, preferred_element_type=jnp.float32
    )
    rope_term = scale_factor * jnp.einsum(
        "shtj,shdt->jd", score_grad, query_rope, preferred_element_type=jnp.float32
    )
    terms = jnp.concatenate([latent_term, rope_term], axis=1).astype(jnp.bfloat16)
    total = causal_reduce_ctx(terms.reshape(n_ctx, block_len, -1), n_ctx)
    total = halving_sum_ep(total, n_ep)
    latent_kgrad = total[None, :, :kvr]
    rope_kgrad = total[:, kvr:].T[None]
    return (attended, latent_qgrad, rope_qgrad, latent_kgrad, rope_kgrad)


def solution(mesh):
    placed = (
        P(None, "ctx", "ep", None),
        P(None, "ep", None, "ctx"),
        P(None, "ctx", None),
        P(None, None, "ctx"),
        P(None, "ctx", "ep", None),
    )
    return jax.shard_map(
        body,
        mesh=mesh,
        in_specs=placed,
        out_specs=(
            P(None, "ctx", "ep", None),
            P(None, "ctx", "ep", None),
            P(None, "ep", None, "ctx"),
            P(None, "ctx", None),
            P(None, None, "ctx"),
        ),
        check_vma=False,
    )
```

```python
import jax
import jax.numpy as jnp
from jax import lax
from jax.experimental import pallas as pl
from jax.experimental.pallas import tpu as pltpu
from jax.sharding import PartitionSpec as P

scale_factor = 192.0 ** (-0.5)


def causal_reduce_ctx(blocks, n_ctx):
    here = lax.axis_index("ctx")
    total = jnp.take(blocks, here, axis=0).astype(jnp.float32)
    for shift in range(1, n_ctx):
        sent = jnp.take(blocks, jnp.maximum(here - shift, 0), axis=0)
        got = lax.ppermute(sent, "ctx", [(i, i - shift) for i in range(shift, n_ctx)])
        total = total + got.astype(jnp.float32)
    return total


def butterfly_sum_ep(total, n_ep):
    if n_ep & (n_ep - 1):
        return lax.psum(total.astype(jnp.bfloat16), "ep").astype(jnp.float32)
    bit = 1
    while bit < n_ep:
        mine = total.astype(jnp.bfloat16)
        theirs = lax.ppermute(mine, "ep", [(i, i ^ bit) for i in range(n_ep)])
        total = mine.astype(jnp.float32) + theirs.astype(jnp.float32)
        bit *= 2
    return total


def attention_kernel(ql_ref, qr_ref, qrt_ref, k_ref, kr_ref, do_ref, mask_ref,
                     att_ref, lqg_ref, rqg_ref, lt_ref, rt_ref):
    head = pl.program_id(0)
    f32 = jnp.float32
    nt = (((1,), (1,)), ((), ()))
    tn = (((0,), (0,)), ((), ()))
    q = ql_ref[...]
    k = k_ref[...]
    kr = kr_ref[...]
    dout = do_ref[...]
    scores = lax.dot_general(q, k, nt, preferred_element_type=f32)
    scores = scores + jnp.dot(qrt_ref[0], kr, preferred_element_type=f32)
    scores = jnp.where(mask_ref[...] != 0, scores * scale_factor, f32(-1e30))
    row_max = jnp.max(scores, axis=-1, keepdims=True)
    powers = jnp.exp(scores - row_max)
    weights = powers / jnp.sum(powers, axis=-1, keepdims=True)
    rounded = weights.astype(jnp.bfloat16)
    att = jnp.dot(rounded, k, preferred_element_type=f32).astype(jnp.bfloat16)
    att_ref[...] = att
    row_dots = jnp.sum(dout.astype(f32) * att.astype(f32), axis=-1, keepdims=True)
    weight_grad = lax.dot_general(dout, k, nt, preferred_element_type=f32)
    score_grad = (weights * (weight_grad - row_dots)).astype(jnp.bfloat16)
    lqg_ref[...] = (scale_factor * jnp.dot(score_grad, k, preferred_element_type=f32)).astype(jnp.bfloat16)
    rqg_ref[0] = (
        scale_factor * lax.dot_general(kr, score_grad, nt, preferred_element_type=f32)
    ).astype(jnp.bfloat16)
    lt = scale_factor * lax.dot_general(score_grad, q, tn, preferred_element_type=f32)
    lt = lt + lax.dot_general(rounded, dout, tn, preferred_element_type=f32)
    rt = scale_factor * jnp.dot(qr_ref[0], score_grad, preferred_element_type=f32)

    @pl.when(head == 0)
    def _():
        lt_ref[...] = lt
        rt_ref[...] = rt

    @pl.when(head > 0)
    def _():
        lt_ref[...] += lt
        rt_ref[...] += rt


def body(query_latent, query_rope, key_latent, key_rope, output_grad):
    n_ctx = lax.axis_size("ctx")
    n_ep = lax.axis_size("ep")
    _, block_len, heads, kvr = query_latent.shape
    rope = query_rope.shape[2]
    local_keys = jnp.concatenate([key_latent[0], key_rope[0].T], axis=1)
    whole_keys = lax.all_gather(local_keys, "ctx", axis=0, tiled=True)
    whole_latent = whole_keys[:, :kvr]
    whole_rope = whole_keys[:, kvr:].T
    length = whole_latent.shape[0]
    offset = lax.axis_index("ctx") * block_len
    query_place = offset + jnp.arange(block_len, dtype=jnp.int32)
    allowed = (jnp.arange(length, dtype=jnp.int32)[None, :] <= query_place[:, None]).astype(jnp.int32)
    ql = query_latent.reshape(block_len, heads * kvr)
    dout = output_grad.reshape(block_len, heads * kvr)
    qr = query_rope[0]
    qrt = jnp.swapaxes(qr, 1, 2)
    by_head = pl.BlockSpec((block_len, kvr), lambda h: (0, h))
    rope_head = pl.BlockSpec((1, rope, block_len), lambda h: (h, 0, 0))
    fixed = lambda shape: pl.BlockSpec(shape, lambda h: (0,) * len(shape))
    att, lqg, rqg, lt, rt = pl.pallas_call(
        attention_kernel,
        grid=(heads,),
        in_specs=[
            by_head,
            rope_head,
            pl.BlockSpec((1, block_len, rope), lambda h: (h, 0, 0)),
            fixed((length, kvr)),
            fixed((rope, length)),
            by_head,
            fixed((block_len, length)),
        ],
        out_specs=[
            by_head,
            by_head,
            rope_head,
            fixed((length, kvr)),
            fixed((rope, length)),
        ],
        out_shape=[
            jax.ShapeDtypeStruct((block_len, heads * kvr), jnp.bfloat16),
            jax.ShapeDtypeStruct((block_len, heads * kvr), jnp.bfloat16),
            jax.ShapeDtypeStruct((heads, rope, block_len), jnp.bfloat16),
            jax.ShapeDtypeStruct((length, kvr), jnp.float32),
            jax.ShapeDtypeStruct((rope, length), jnp.float32),
        ],
        compiler_params=pltpu.CompilerParams(dimension_semantics=("arbitrary",)),
    )(ql, qr, qrt, whole_latent, whole_rope, dout, allowed)
    attended = att.reshape(query_latent.shape)
    latent_qgrad = lqg.reshape(query_latent.shape)
    rope_qgrad = rqg[None]
    terms = jnp.concatenate([lt, rt.T], axis=1).astype(jnp.bfloat16)
    total = causal_reduce_ctx(terms.reshape(n_ctx, block_len, -1), n_ctx)
    total = butterfly_sum_ep(total, n_ep).astype(jnp.bfloat16)
    latent_kgrad = total[None, :, :kvr]
    rope_kgrad = total[:, kvr:].T[None]
    return (attended, latent_qgrad, rope_qgrad, latent_kgrad, rope_kgrad)


def solution(mesh):
    placed = (
        P(None, "ctx", "ep", None),
        P(None, "ep", None, "ctx"),
        P(None, "ctx", None),
        P(None, None, "ctx"),
        P(None, "ctx", "ep", None),
    )
    return jax.shard_map(
        body,
        mesh=mesh,
        in_specs=placed,
        out_specs=(
            P(None, "ctx", "ep", None),
            P(None, "ctx", "ep", None),
            P(None, "ep", None, "ctx"),
            P(None, "ctx", None),
            P(None, None, "ctx"),
        ),
        check_vma=False,
    )
```

```python
import jax
import jax.numpy as jnp
from jax import lax
from jax.experimental import pallas as pl
from jax.experimental.pallas import tpu as pltpu
from jax.sharding import PartitionSpec as P

scale_factor = 192.0 ** (-0.5)


def causal_reduce_ctx(blocks, n_ctx):
    here = lax.axis_index("ctx")
    total = jnp.take(blocks, here, axis=0).astype(jnp.float32)
    for shift in range(1, n_ctx):
        sent = jnp.take(blocks, jnp.maximum(here - shift, 0), axis=0)
        got = lax.ppermute(sent, "ctx", [(i, i - shift) for i in range(shift, n_ctx)])
        total = total + got.astype(jnp.float32)
    return total


def butterfly_sum_ep(total, n_ep):
    if n_ep & (n_ep - 1):
        return lax.psum(total.astype(jnp.bfloat16), "ep").astype(jnp.float32)
    bit = 1
    while bit < n_ep:
        mine = total.astype(jnp.bfloat16)
        theirs = lax.ppermute(mine, "ep", [(i, i ^ bit) for i in range(n_ep)])
        total = mine.astype(jnp.float32) + theirs.astype(jnp.float32)
        bit *= 2
    return total


def attention_kernel(offset_ref, ql_ref, qr_ref, k_ref, kr_ref, do_ref,
                     att_ref, lqg_ref, rqg_ref, lt_ref, rt_ref):
    step = pl.program_id(0)
    t_blk, heads, kvr = ql_ref.shape
    rope = qr_ref.shape[2]
    rows = t_blk * heads
    f32 = jnp.float32
    nt = (((1,), (1,)), ((), ()))
    tn = (((0,), (0,)), ((), ()))
    q = ql_ref[...].reshape(rows, kvr)
    qr = qr_ref[...].reshape(rows, rope)
    k = k_ref[...]
    kr = kr_ref[...]
    dout = do_ref[...].reshape(rows, kvr)
    length = k.shape[0]
    scores = lax.dot_general(q, k, nt, preferred_element_type=f32)
    scores = scores + jnp.dot(qr, kr, preferred_element_type=f32)
    row = lax.broadcasted_iota(jnp.int32, (rows, length), 0)
    col = lax.broadcasted_iota(jnp.int32, (rows, length), 1)
    allowed = row >= heads * (col - offset_ref[0] - step * t_blk)
    scores = jnp.where(allowed, scores * scale_factor, f32(-1e30))
    row_max = jnp.max(scores, axis=-1, keepdims=True)
    powers = jnp.exp(scores - row_max)
    weights = powers / jnp.sum(powers, axis=-1, keepdims=True)
    rounded = weights.astype(jnp.bfloat16)
    att = jnp.dot(rounded, k, preferred_element_type=f32).astype(jnp.bfloat16)
    att_ref[...] = att.reshape(t_blk, heads, kvr)
    row_dots = jnp.sum(dout.astype(f32) * att.astype(f32), axis=-1, keepdims=True)
    weight_grad = lax.dot_general(dout, k, nt, preferred_element_type=f32)
    score_grad = (weights * (weight_grad - row_dots)).astype(jnp.bfloat16)
    lqg = scale_factor * jnp.dot(score_grad, k, preferred_element_type=f32)
    lqg_ref[...] = lqg.astype(jnp.bfloat16).reshape(t_blk, heads, kvr)
    rqg = scale_factor * lax.dot_general(score_grad, kr, nt, preferred_element_type=f32)
    rqg_ref[...] = rqg.astype(jnp.bfloat16).reshape(t_blk, heads, rope)
    lt = scale_factor * lax.dot_general(score_grad, q, tn, preferred_element_type=f32)
    lt = lt + lax.dot_general(rounded, dout, tn, preferred_element_type=f32)
    rt = scale_factor * lax.dot_general(score_grad, qr, tn, preferred_element_type=f32)

    @pl.when(step == 0)
    def _():
        lt_ref[...] = lt
        rt_ref[...] = rt

    @pl.when(step > 0)
    def _():
        lt_ref[...] += lt
        rt_ref[...] += rt


def body(query_latent, query_rope, key_latent, key_rope, output_grad):
    n_ctx = lax.axis_size("ctx")
    n_ep = lax.axis_size("ep")
    _, block_len, heads, kvr = query_latent.shape
    rope = query_rope.shape[2]
    local_keys = jnp.concatenate([key_latent[0], key_rope[0].T], axis=1)
    whole_keys = lax.all_gather(local_keys, "ctx", axis=0, tiled=True)
    whole_latent = whole_keys[:, :kvr]
    whole_rope = whole_keys[:, kvr:].T
    length = whole_latent.shape[0]
    offset = (lax.axis_index("ctx") * block_len).astype(jnp.int32).reshape(1)
    qr = jnp.transpose(query_rope[0], (2, 0, 1))
    t_blk = max(1, min(block_len, 256 // heads))
    while block_len % t_blk:
        t_blk -= 1
    by_rows = pl.BlockSpec((t_blk, heads, kvr), lambda i, off: (i, 0, 0))
    rope_rows = pl.BlockSpec((t_blk, heads, rope), lambda i, off: (i, 0, 0))
    fixed = lambda shape: pl.BlockSpec(shape, lambda i, off: (0,) * len(shape))
    att, lqg, rqg, lt, rt = pl.pallas_call(
        attention_kernel,
        grid_spec=pltpu.PrefetchScalarGridSpec(
            num_scalar_prefetch=1,
            grid=(block_len // t_blk,),
            in_specs=[
                by_rows,
                rope_rows,
                fixed((length, kvr)),
                fixed((rope, length)),
                by_rows,
            ],
            out_specs=[
                by_rows,
                by_rows,
                rope_rows,
                fixed((length, kvr)),
                fixed((length, rope)),
            ],
        ),
        out_shape=[
            jax.ShapeDtypeStruct((block_len, heads, kvr), jnp.bfloat16),
            jax.ShapeDtypeStruct((block_len, heads, kvr), jnp.bfloat16),
            jax.ShapeDtypeStruct((block_len, heads, rope), jnp.bfloat16),
            jax.ShapeDtypeStruct((length, kvr), jnp.float32),
            jax.ShapeDtypeStruct((length, rope), jnp.float32),
        ],
        compiler_params=pltpu.CompilerParams(dimension_semantics=("arbitrary",)),
    )(offset, query_latent[0], qr, whole_latent, whole_rope, output_grad[0])
    attended = att[None]
    latent_qgrad = lqg[None]
    rope_qgrad = jnp.transpose(rqg, (1, 2, 0))[None]
    terms = jnp.concatenate([lt, rt], axis=1).astype(jnp.bfloat16)
    total = causal_reduce_ctx(terms.reshape(n_ctx, block_len, -1), n_ctx)
    total = butterfly_sum_ep(total, n_ep).astype(jnp.bfloat16)
    latent_kgrad = total[None, :, :kvr]
    rope_kgrad = total[:, kvr:].T[None]
    return (attended, latent_qgrad, rope_qgrad, latent_kgrad, rope_kgrad)


def solution(mesh):
    placed = (
        P(None, "ctx", "ep", None),
        P(None, "ep", None, "ctx"),
        P(None, "ctx", None),
        P(None, None, "ctx"),
        P(None, "ctx", "ep", None),
    )
    return jax.shard_map(
        body,
        mesh=mesh,
        in_specs=placed,
        out_specs=(
            P(None, "ctx", "ep", None),
            P(None, "ctx", "ep", None),
            P(None, "ep", None, "ctx"),
            P(None, "ctx", None),
            P(None, None, "ctx"),
        ),
        check_vma=False,
    )
```

```python
import jax
import jax.numpy as jnp
from jax import lax
from jax.experimental import pallas as pl
from jax.experimental.pallas import tpu as pltpu
from jax.sharding import PartitionSpec as P

scale_factor = 192.0 ** (-0.5)


def causal_reduce_ctx(blocks, n_ctx):
    here = lax.axis_index("ctx")
    total = jnp.take(blocks, here, axis=0).astype(jnp.float32)
    for shift in range(1, n_ctx):
        sent = jnp.take(blocks, jnp.maximum(here - shift, 0), axis=0)
        got = lax.ppermute(sent, "ctx", [(i, i - shift) for i in range(shift, n_ctx)])
        total = total + got.astype(jnp.float32)
    return total


def butterfly_sum_ep(total, n_ep):
    if n_ep & (n_ep - 1):
        return lax.psum(total.astype(jnp.bfloat16), "ep").astype(jnp.float32)
    bit = 1
    while bit < n_ep:
        mine = total.astype(jnp.bfloat16)
        theirs = lax.ppermute(mine, "ep", [(i, i ^ bit) for i in range(n_ep)])
        total = mine.astype(jnp.float32) + theirs.astype(jnp.float32)
        bit *= 2
    return total


def attention_kernel(offset_ref, ql_ref, qr_ref, keys_ref, do_ref,
                     att_ref, lqg_ref, rqg_ref, terms_ref, lt_acc, rt_acc):
    step = pl.program_id(0)
    t_blk, heads, kvr = ql_ref.shape
    rope = qr_ref.shape[2]
    rows = t_blk * heads
    f32 = jnp.float32
    nt = (((1,), (1,)), ((), ()))
    tn = (((0,), (0,)), ((), ()))
    q = ql_ref[...].reshape(rows, kvr)
    qr = qr_ref[...].reshape(rows, rope)
    k = keys_ref[:, :kvr]
    kr = keys_ref[:, kvr:]
    dout = do_ref[...].reshape(rows, kvr)
    length = k.shape[0]
    scores = lax.dot_general(q, k, nt, preferred_element_type=f32)
    scores = scores + lax.dot_general(qr, kr, nt, preferred_element_type=f32)
    row = lax.broadcasted_iota(jnp.int32, (rows, length), 0)
    col = lax.broadcasted_iota(jnp.int32, (rows, length), 1)
    allowed = row >= heads * (col - offset_ref[0] - step * t_blk)
    scores = jnp.where(allowed, scores * scale_factor, f32(-1e30))
    row_max = jnp.max(scores, axis=-1, keepdims=True)
    powers = jnp.exp(scores - row_max)
    weights = powers / jnp.sum(powers, axis=-1, keepdims=True)
    rounded = weights.astype(jnp.bfloat16)
    att = jnp.dot(rounded, k, preferred_element_type=f32).astype(jnp.bfloat16)
    att_ref[...] = att.reshape(t_blk, heads, kvr)
    row_dots = jnp.sum(dout.astype(f32) * att.astype(f32), axis=-1, keepdims=True)
    weight_grad = lax.dot_general(dout, k, nt, preferred_element_type=f32)
    score_grad = (weights * (weight_grad - row_dots)).astype(jnp.bfloat16)
    lqg = scale_factor * jnp.dot(score_grad, k, preferred_element_type=f32)
    lqg_ref[...] = lqg.astype(jnp.bfloat16).reshape(t_blk, heads, kvr)
    rqg = scale_factor * jnp.dot(score_grad, kr, preferred_element_type=f32)
    rqg_ref[...] = rqg.astype(jnp.bfloat16).reshape(t_blk, heads, rope)
    lt = scale_factor * lax.dot_general(score_grad, q, tn, preferred_element_type=f32)
    lt = lt + lax.dot_general(rounded, dout, tn, preferred_element_type=f32)
    rt = scale_factor * lax.dot_general(score_grad, qr, tn, preferred_element_type=f32)

    @pl.when(step == 0)
    def _():
        lt_acc[...] = lt
        rt_acc[...] = rt

    @pl.when(step > 0)
    def _():
        lt_acc[...] += lt
        rt_acc[...] += rt

    @pl.when(step == pl.num_programs(0) - 1)
    def _():
        terms_ref[:, :kvr] = lt_acc[...].astype(jnp.bfloat16)
        terms_ref[:, kvr:] = rt_acc[...].astype(jnp.bfloat16)


def body(query_latent, query_rope, key_latent, key_rope, output_grad):
    n_ctx = lax.axis_size("ctx")
    n_ep = lax.axis_size("ep")
    _, block_len, heads, kvr = query_latent.shape
    rope = query_rope.shape[2]
    local_keys = jnp.concatenate([key_latent[0], key_rope[0].T], axis=1)
    whole_keys = lax.all_gather(local_keys, "ctx", axis=0, tiled=True)
    length = whole_keys.shape[0]
    offset = (lax.axis_index("ctx") * block_len).astype(jnp.int32).reshape(1)
    qr = jnp.transpose(query_rope[0], (2, 0, 1))
    t_blk = max(1, min(block_len, 256 // heads))
    while block_len % t_blk:
        t_blk -= 1
    by_rows = pl.BlockSpec((t_blk, heads, kvr), lambda i, off: (i, 0, 0))
    rope_rows = pl.BlockSpec((t_blk, heads, rope), lambda i, off: (i, 0, 0))
    fixed = pl.BlockSpec((length, kvr + rope), lambda i, off: (0, 0))
    att, lqg, rqg, terms = pl.pallas_call(
        attention_kernel,
        grid_spec=pltpu.PrefetchScalarGridSpec(
            num_scalar_prefetch=1,
            grid=(block_len // t_blk,),
            in_specs=[by_rows, rope_rows, fixed, by_rows],
            out_specs=[by_rows, by_rows, rope_rows, fixed],
            scratch_shapes=[
                pltpu.VMEM((length, kvr), jnp.float32),
                pltpu.VMEM((length, rope), jnp.float32),
            ],
        ),
        out_shape=[
            jax.ShapeDtypeStruct((block_len, heads, kvr), jnp.bfloat16),
            jax.ShapeDtypeStruct((block_len, heads, kvr), jnp.bfloat16),
            jax.ShapeDtypeStruct((block_len, heads, rope), jnp.bfloat16),
            jax.ShapeDtypeStruct((length, kvr + rope), jnp.bfloat16),
        ],
        compiler_params=pltpu.CompilerParams(dimension_semantics=("arbitrary",)),
    )(offset, query_latent[0], qr, whole_keys, output_grad[0])
    attended = att[None]
    latent_qgrad = lqg[None]
    rope_qgrad = jnp.transpose(rqg, (1, 2, 0))[None]
    total = causal_reduce_ctx(terms.reshape(n_ctx, block_len, -1), n_ctx)
    total = butterfly_sum_ep(total, n_ep).astype(jnp.bfloat16)
    latent_kgrad = total[None, :, :kvr]
    rope_kgrad = total[:, kvr:].T[None]
    return (attended, latent_qgrad, rope_qgrad, latent_kgrad, rope_kgrad)


def solution(mesh):
    placed = (
        P(None, "ctx", "ep", None),
        P(None, "ep", None, "ctx"),
        P(None, "ctx", None),
        P(None, None, "ctx"),
        P(None, "ctx", "ep", None),
    )
    return jax.shard_map(
        body,
        mesh=mesh,
        in_specs=placed,
        out_specs=(
            P(None, "ctx", "ep", None),
            P(None, "ctx", "ep", None),
            P(None, "ep", None, "ctx"),
            P(None, "ctx", None),
            P(None, None, "ctx"),
        ),
        check_vma=False,
    )
```

```python
import jax
import jax.numpy as jnp
from jax import lax
from jax.experimental import pallas as pl
from jax.experimental.pallas import tpu as pltpu
from jax.sharding import PartitionSpec as P

scale_factor = 192.0 ** (-0.5)


def causal_reduce_ctx(blocks, n_ctx):
    here = lax.axis_index("ctx")
    if n_ctx % 2:
        total = jnp.take(blocks, here, axis=0).astype(jnp.float32)
        for shift in range(1, n_ctx):
            sent = jnp.take(blocks, jnp.maximum(here - shift, 0), axis=0)
            got = lax.ppermute(sent, "ctx", [(i, i - shift) for i in range(shift, n_ctx)])
            total = total + got.astype(jnp.float32)
        return total
    pairs = n_ctx // 2
    side = here % 2
    by_parity = blocks.reshape(pairs, 2, *blocks.shape[1:])
    mine = jnp.take(by_parity, side, axis=1)
    theirs = jnp.take(by_parity, 1 - side, axis=1)
    got = lax.ppermute(theirs, "ctx", [(i, i ^ 1) for i in range(n_ctx)])
    summed = (mine.astype(jnp.float32) + got.astype(jnp.float32)).astype(jnp.bfloat16)
    total = jnp.take(summed, here // 2, axis=0).astype(jnp.float32)
    for shift in range(1, pairs):
        sent = jnp.take(summed, jnp.maximum(here // 2 - shift, 0), axis=0)
        got = lax.ppermute(sent, "ctx", [(i, i - 2 * shift) for i in range(2 * shift, n_ctx)])
        total = total + got.astype(jnp.float32)
    return total


def butterfly_sum_ep(total, n_ep):
    if n_ep & (n_ep - 1):
        return lax.psum(total.astype(jnp.bfloat16), "ep").astype(jnp.float32)
    bit = 1
    while bit < n_ep:
        mine = total.astype(jnp.bfloat16)
        theirs = lax.ppermute(mine, "ep", [(i, i ^ bit) for i in range(n_ep)])
        total = mine.astype(jnp.float32) + theirs.astype(jnp.float32)
        bit *= 2
    return total


def attention_kernel(offset_ref, ql_ref, qr_ref, keys_ref, do_ref,
                     att_ref, lqg_ref, rqg_ref, terms_ref, lt_acc, rt_acc):
    step = pl.program_id(0)
    t_blk, heads, kvr = ql_ref.shape
    rope = qr_ref.shape[2]
    rows = t_blk * heads
    f32 = jnp.float32
    nt = (((1,), (1,)), ((), ()))
    tn = (((0,), (0,)), ((), ()))
    q = ql_ref[...].reshape(rows, kvr)
    qr = qr_ref[...].reshape(rows, rope)
    k = keys_ref[:, :kvr]
    kr = keys_ref[:, kvr:]
    dout = do_ref[...].reshape(rows, kvr)
    length = k.shape[0]
    scores = lax.dot_general(q, k, nt, preferred_element_type=f32)
    scores = scores + lax.dot_general(qr, kr, nt, preferred_element_type=f32)
    row = lax.broadcasted_iota(jnp.int32, (rows, length), 0)
    col = lax.broadcasted_iota(jnp.int32, (rows, length), 1)
    allowed = row >= heads * (col - offset_ref[0] - step * t_blk)
    scores = jnp.where(allowed, scores * scale_factor, f32(-1e30))
    row_max = jnp.max(scores, axis=-1, keepdims=True)
    powers = jnp.exp(scores - row_max)
    weights = powers / jnp.sum(powers, axis=-1, keepdims=True)
    rounded = weights.astype(jnp.bfloat16)
    att = jnp.dot(rounded, k, preferred_element_type=f32).astype(jnp.bfloat16)
    att_ref[...] = att.reshape(t_blk, heads, kvr)
    row_dots = jnp.sum(dout.astype(f32) * att.astype(f32), axis=-1, keepdims=True)
    weight_grad = lax.dot_general(dout, k, nt, preferred_element_type=f32)
    score_grad = (weights * (weight_grad - row_dots)).astype(jnp.bfloat16)
    lqg = scale_factor * jnp.dot(score_grad, k, preferred_element_type=f32)
    lqg_ref[...] = lqg.astype(jnp.bfloat16).reshape(t_blk, heads, kvr)
    rqg = scale_factor * jnp.dot(score_grad, kr, preferred_element_type=f32)
    rqg_ref[...] = rqg.astype(jnp.bfloat16).reshape(t_blk, heads, rope)
    lt = scale_factor * lax.dot_general(score_grad, q, tn, preferred_element_type=f32)
    lt = lt + lax.dot_general(rounded, dout, tn, preferred_element_type=f32)
    rt = scale_factor * lax.dot_general(score_grad, qr, tn, preferred_element_type=f32)

    @pl.when(step == 0)
    def _():
        lt_acc[...] = lt
        rt_acc[...] = rt

    @pl.when(step > 0)
    def _():
        lt_acc[...] += lt
        rt_acc[...] += rt

    @pl.when(step == pl.num_programs(0) - 1)
    def _():
        terms_ref[:, :kvr] = lt_acc[...].astype(jnp.bfloat16)
        terms_ref[:, kvr:] = rt_acc[...].astype(jnp.bfloat16)


def body(query_latent, query_rope, key_latent, key_rope, output_grad):
    n_ctx = lax.axis_size("ctx")
    n_ep = lax.axis_size("ep")
    _, block_len, heads, kvr = query_latent.shape
    rope = query_rope.shape[2]
    local_keys = jnp.concatenate([key_latent[0], key_rope[0].T], axis=1)
    whole_keys = lax.all_gather(local_keys, "ctx", axis=0, tiled=True)
    length = whole_keys.shape[0]
    offset = (lax.axis_index("ctx") * block_len).astype(jnp.int32).reshape(1)
    qr = jnp.transpose(query_rope[0], (2, 0, 1))
    t_blk = max(1, min(block_len, 256 // heads))
    while block_len % t_blk:
        t_blk -= 1
    by_rows = pl.BlockSpec((t_blk, heads, kvr), lambda i, off: (i, 0, 0))
    rope_rows = pl.BlockSpec((t_blk, heads, rope), lambda i, off: (i, 0, 0))
    fixed = pl.BlockSpec((length, kvr + rope), lambda i, off: (0, 0))
    att, lqg, rqg, terms = pl.pallas_call(
        attention_kernel,
        grid_spec=pltpu.PrefetchScalarGridSpec(
            num_scalar_prefetch=1,
            grid=(block_len // t_blk,),
            in_specs=[by_rows, rope_rows, fixed, by_rows],
            out_specs=[by_rows, by_rows, rope_rows, fixed],
            scratch_shapes=[
                pltpu.VMEM((length, kvr), jnp.float32),
                pltpu.VMEM((length, rope), jnp.float32),
            ],
        ),
        out_shape=[
            jax.ShapeDtypeStruct((block_len, heads, kvr), jnp.bfloat16),
            jax.ShapeDtypeStruct((block_len, heads, kvr), jnp.bfloat16),
            jax.ShapeDtypeStruct((block_len, heads, rope), jnp.bfloat16),
            jax.ShapeDtypeStruct((length, kvr + rope), jnp.bfloat16),
        ],
        compiler_params=pltpu.CompilerParams(dimension_semantics=("arbitrary",)),
    )(offset, query_latent[0], qr, whole_keys, output_grad[0])
    attended = att[None]
    latent_qgrad = lqg[None]
    rope_qgrad = jnp.transpose(rqg, (1, 2, 0))[None]
    total = causal_reduce_ctx(terms.reshape(n_ctx, block_len, -1), n_ctx)
    total = butterfly_sum_ep(total, n_ep).astype(jnp.bfloat16)
    latent_kgrad = total[None, :, :kvr]
    rope_kgrad = total[:, kvr:].T[None]
    return (attended, latent_qgrad, rope_qgrad, latent_kgrad, rope_kgrad)


def solution(mesh):
    placed = (
        P(None, "ctx", "ep", None),
        P(None, "ep", None, "ctx"),
        P(None, "ctx", None),
        P(None, None, "ctx"),
        P(None, "ctx", "ep", None),
    )
    return jax.shard_map(
        body,
        mesh=mesh,
        in_specs=placed,
        out_specs=(
            P(None, "ctx", "ep", None),
            P(None, "ctx", "ep", None),
            P(None, "ep", None, "ctx"),
            P(None, "ctx", None),
            P(None, None, "ctx"),
        ),
        check_vma=False,
    )
```

```python
import jax
import jax.numpy as jnp
from jax import lax
from jax.experimental import pallas as pl
from jax.experimental.pallas import tpu as pltpu
from jax.sharding import PartitionSpec as P

scale_factor = 192.0 ** (-0.5)


def causal_reduce_ctx(blocks, n_ctx):
    here = lax.axis_index("ctx")
    if n_ctx % 2:
        total = jnp.take(blocks, here, axis=0).astype(jnp.float32)
        for shift in range(1, n_ctx):
            sent = jnp.take(blocks, jnp.maximum(here - shift, 0), axis=0)
            got = lax.ppermute(sent, "ctx", [(i, i - shift) for i in range(shift, n_ctx)])
            total = total + got.astype(jnp.float32)
        return total
    pairs = n_ctx // 2
    side = here % 2
    by_parity = blocks.reshape(pairs, 2, *blocks.shape[1:])
    mine = jnp.take(by_parity, side, axis=1)
    theirs = jnp.take(by_parity, 1 - side, axis=1)
    got = lax.ppermute(theirs, "ctx", [(i, i ^ 1) for i in range(n_ctx)])
    summed = (mine.astype(jnp.float32) + got.astype(jnp.float32)).astype(jnp.bfloat16)
    total = jnp.take(summed, here // 2, axis=0).astype(jnp.float32)
    for shift in range(1, pairs):
        sent = jnp.take(summed, jnp.maximum(here // 2 - shift, 0), axis=0)
        got = lax.ppermute(sent, "ctx", [(i, i - 2 * shift) for i in range(2 * shift, n_ctx)])
        total = total + got.astype(jnp.float32)
    return total


def butterfly_sum_ep(total, n_ep):
    if n_ep & (n_ep - 1):
        return lax.psum(total.astype(jnp.bfloat16), "ep").astype(jnp.float32)
    bit = 1
    while bit < n_ep:
        mine = total.astype(jnp.bfloat16)
        theirs = lax.ppermute(mine, "ep", [(i, i ^ bit) for i in range(n_ep)])
        total = mine.astype(jnp.float32) + theirs.astype(jnp.float32)
        bit *= 2
    return total


def attention_kernel(offset_ref, ql_ref, qr_ref, keys_ref, do_ref,
                     att_ref, lqg_ref, rqg_ref, terms_ref, lt_acc, rt_acc):
    step = pl.program_id(0)
    t_blk, heads, kvr = ql_ref.shape
    rope = qr_ref.shape[2]
    rows = t_blk * heads
    f32 = jnp.float32
    nt = (((1,), (1,)), ((), ()))
    tn = (((0,), (0,)), ((), ()))
    q = ql_ref[...].reshape(rows, kvr)
    qr = qr_ref[...].reshape(rows, rope)
    k = keys_ref[:, :kvr]
    kr = keys_ref[:, kvr:]
    dout = do_ref[...].reshape(rows, kvr)
    length = k.shape[0]
    scores = lax.dot_general(q, k, nt, preferred_element_type=f32)
    scores = scores + lax.dot_general(qr, kr, nt, preferred_element_type=f32)
    row = lax.broadcasted_iota(jnp.int32, (rows, length), 0)
    col = lax.broadcasted_iota(jnp.int32, (rows, length), 1)
    allowed = row >= heads * (col - offset_ref[0] - step * t_blk)
    scores = jnp.where(allowed, scores * scale_factor, f32(-1e30))
    row_max = jnp.max(scores, axis=-1, keepdims=True)
    powers = jnp.exp(scores - row_max)
    weights = powers / jnp.sum(powers, axis=-1, keepdims=True)
    rounded = weights.astype(jnp.bfloat16)
    att = jnp.dot(rounded, k, preferred_element_type=f32).astype(jnp.bfloat16)
    att_ref[...] = att.reshape(t_blk, heads, kvr)
    row_dots = jnp.sum(dout.astype(f32) * att.astype(f32), axis=-1, keepdims=True)
    weight_grad = lax.dot_general(dout, k, nt, preferred_element_type=f32)
    score_grad = (weights * (weight_grad - row_dots)).astype(jnp.bfloat16)
    lqg = scale_factor * jnp.dot(score_grad, k, preferred_element_type=f32)
    lqg_ref[...] = lqg.astype(jnp.bfloat16).reshape(t_blk, heads, kvr)
    rqg = scale_factor * jnp.dot(score_grad, kr, preferred_element_type=f32)
    rqg_ref[...] = rqg.astype(jnp.bfloat16).reshape(t_blk, heads, rope)
    lt = scale_factor * lax.dot_general(score_grad, q, tn, preferred_element_type=f32)
    lt = lt + lax.dot_general(rounded, dout, tn, preferred_element_type=f32)
    rt = scale_factor * lax.dot_general(score_grad, qr, tn, preferred_element_type=f32)

    @pl.when(step == 0)
    def _():
        lt_acc[...] = lt
        rt_acc[...] = rt

    @pl.when(step > 0)
    def _():
        lt_acc[...] += lt
        rt_acc[...] += rt

    @pl.when(step == pl.num_programs(0) - 1)
    def _():
        terms_ref[:, :kvr] = lt_acc[...].astype(jnp.bfloat16)
        terms_ref[:, kvr:] = rt_acc[...].astype(jnp.bfloat16)


def body(query_latent, query_rope, key_latent, key_rope, output_grad):
    n_ctx = lax.axis_size("ctx")
    n_ep = lax.axis_size("ep")
    _, block_len, heads, kvr = query_latent.shape
    rope = query_rope.shape[2]
    local_keys = jnp.concatenate([key_latent[0], key_rope[0].T], axis=1)
    whole_keys = lax.all_gather(local_keys, "ctx", axis=0, tiled=True)
    length = whole_keys.shape[0]
    offset = (lax.axis_index("ctx") * block_len).astype(jnp.int32).reshape(1)
    qr = jnp.transpose(query_rope[0], (2, 0, 1))
    t_blk = max(1, min(block_len, 512 // heads))
    while block_len % t_blk:
        t_blk -= 1
    by_rows = pl.BlockSpec((t_blk, heads, kvr), lambda i, off: (i, 0, 0))
    rope_rows = pl.BlockSpec((t_blk, heads, rope), lambda i, off: (i, 0, 0))
    fixed = pl.BlockSpec((length, kvr + rope), lambda i, off: (0, 0))
    att, lqg, rqg, terms = pl.pallas_call(
        attention_kernel,
        grid_spec=pltpu.PrefetchScalarGridSpec(
            num_scalar_prefetch=1,
            grid=(block_len // t_blk,),
            in_specs=[by_rows, rope_rows, fixed, by_rows],
            out_specs=[by_rows, by_rows, rope_rows, fixed],
            scratch_shapes=[
                pltpu.VMEM((length, kvr), jnp.float32),
                pltpu.VMEM((length, rope), jnp.float32),
            ],
        ),
        out_shape=[
            jax.ShapeDtypeStruct((block_len, heads, kvr), jnp.bfloat16),
            jax.ShapeDtypeStruct((block_len, heads, kvr), jnp.bfloat16),
            jax.ShapeDtypeStruct((block_len, heads, rope), jnp.bfloat16),
            jax.ShapeDtypeStruct((length, kvr + rope), jnp.bfloat16),
        ],
        compiler_params=pltpu.CompilerParams(dimension_semantics=("arbitrary",)),
    )(offset, query_latent[0], qr, whole_keys, output_grad[0])
    attended = att[None]
    latent_qgrad = lqg[None]
    rope_qgrad = jnp.transpose(rqg, (1, 2, 0))[None]
    total = causal_reduce_ctx(terms.reshape(n_ctx, block_len, -1), n_ctx)
    total = butterfly_sum_ep(total, n_ep).astype(jnp.bfloat16)
    latent_kgrad = total[None, :, :kvr]
    rope_kgrad = total[:, kvr:].T[None]
    return (attended, latent_qgrad, rope_qgrad, latent_kgrad, rope_kgrad)


def solution(mesh):
    placed = (
        P(None, "ctx", "ep", None),
        P(None, "ep", None, "ctx"),
        P(None, "ctx", None),
        P(None, None, "ctx"),
        P(None, "ctx", "ep", None),
    )
    return jax.shard_map(
        body,
        mesh=mesh,
        in_specs=placed,
        out_specs=(
            P(None, "ctx", "ep", None),
            P(None, "ctx", "ep", None),
            P(None, "ep", None, "ctx"),
            P(None, "ctx", None),
            P(None, None, "ctx"),
        ),
        check_vma=False,
    )
```

```python
import jax
import jax.numpy as jnp
from jax import lax
from jax.experimental import pallas as pl
from jax.experimental.pallas import tpu as pltpu
from jax.sharding import PartitionSpec as P

scale_factor = 192.0 ** (-0.5)


def causal_reduce_ctx(blocks, n_ctx):
    here = lax.axis_index("ctx")
    if n_ctx % 2:
        total = jnp.take(blocks, here, axis=0).astype(jnp.float32)
        for shift in range(1, n_ctx):
            sent = jnp.take(blocks, jnp.maximum(here - shift, 0), axis=0)
            got = lax.ppermute(sent, "ctx", [(i, i - shift) for i in range(shift, n_ctx)])
            total = total + got.astype(jnp.float32)
        return total
    pairs = n_ctx // 2
    side = here % 2
    by_parity = blocks.reshape(pairs, 2, *blocks.shape[1:])
    mine = jnp.take(by_parity, side, axis=1)
    theirs = jnp.take(by_parity, 1 - side, axis=1)
    got = lax.ppermute(theirs, "ctx", [(i, i ^ 1) for i in range(n_ctx)])
    summed = (mine.astype(jnp.float32) + got.astype(jnp.float32)).astype(jnp.bfloat16)
    total = jnp.take(summed, here // 2, axis=0).astype(jnp.float32)
    for shift in range(1, pairs):
        sent = jnp.take(summed, jnp.maximum(here // 2 - shift, 0), axis=0)
        got = lax.ppermute(sent, "ctx", [(i, i - 2 * shift) for i in range(2 * shift, n_ctx)])
        total = total + got.astype(jnp.float32)
    return total


def butterfly_sum_ep(total, n_ep):
    if n_ep & (n_ep - 1):
        return lax.psum(total.astype(jnp.bfloat16), "ep").astype(jnp.float32)
    bit = 1
    while bit < n_ep:
        mine = total.astype(jnp.bfloat16)
        theirs = lax.ppermute(mine, "ep", [(i, i ^ bit) for i in range(n_ep)])
        total = mine.astype(jnp.float32) + theirs.astype(jnp.float32)
        bit *= 2
    return total


def attention_kernel(offset_ref, ql_ref, qr_ref, keys_ref, do_ref,
                     att_ref, lqg_ref, rqg_ref, terms_ref, lt_acc, rt_acc):
    step = pl.program_id(0)
    t_blk, heads, kvr = ql_ref.shape
    rope = qr_ref.shape[2]
    rows = t_blk * heads
    f32 = jnp.float32
    nt = (((1,), (1,)), ((), ()))
    tn = (((0,), (0,)), ((), ()))
    q = ql_ref[...].reshape(rows, kvr)
    qr = qr_ref[...].reshape(rows, rope)
    k = keys_ref[:, :kvr]
    kr = keys_ref[:, kvr:]
    dout = do_ref[...].reshape(rows, kvr)
    length = k.shape[0]
    scores = lax.dot_general(q, k, nt, preferred_element_type=f32)
    scores = scores + lax.dot_general(qr, kr, nt, preferred_element_type=f32)
    row = lax.broadcasted_iota(jnp.int32, (rows, length), 0)
    col = lax.broadcasted_iota(jnp.int32, (rows, length), 1)
    allowed = row >= heads * (col - offset_ref[0] - step * t_blk)
    scores = jnp.where(allowed, scores * scale_factor, f32(-1e30))
    row_max = jnp.max(scores, axis=-1, keepdims=True)
    powers = jnp.exp(scores - row_max)
    weights = powers / jnp.sum(powers, axis=-1, keepdims=True)
    rounded = weights.astype(jnp.bfloat16)
    att = jnp.dot(rounded, k, preferred_element_type=f32).astype(jnp.bfloat16)
    att_ref[...] = att.reshape(t_blk, heads, kvr)
    row_dots = jnp.sum(dout.astype(f32) * att.astype(f32), axis=-1, keepdims=True)
    weight_grad = lax.dot_general(dout, k, nt, preferred_element_type=f32)
    score_grad = (weights * (weight_grad - row_dots)).astype(jnp.bfloat16)
    lqg = scale_factor * jnp.dot(score_grad, k, preferred_element_type=f32)
    lqg_ref[...] = lqg.astype(jnp.bfloat16).reshape(t_blk, heads, kvr)
    rqg = scale_factor * jnp.dot(score_grad, kr, preferred_element_type=f32)
    rqg_ref[...] = rqg.astype(jnp.bfloat16).reshape(t_blk, heads, rope)
    lt = scale_factor * lax.dot_general(score_grad, q, tn, preferred_element_type=f32)
    lt = lt + lax.dot_general(rounded, dout, tn, preferred_element_type=f32)
    rt = scale_factor * lax.dot_general(score_grad, qr, tn, preferred_element_type=f32)

    @pl.when(step == 0)
    def _():
        lt_acc[...] = lt
        rt_acc[...] = rt

    @pl.when(step > 0)
    def _():
        lt_acc[...] += lt
        rt_acc[...] += rt

    @pl.when(step == pl.num_programs(0) - 1)
    def _():
        terms_ref[:, :kvr] = lt_acc[...].astype(jnp.bfloat16)
        terms_ref[:, kvr:] = rt_acc[...].astype(jnp.bfloat16)


def body(query_latent, query_rope, key_latent, key_rope, output_grad):
    n_ctx = lax.axis_size("ctx")
    n_ep = lax.axis_size("ep")
    _, block_len, heads, kvr = query_latent.shape
    rope = query_rope.shape[2]
    local_keys = jnp.concatenate([key_latent[0], key_rope[0].T], axis=1)
    whole_keys = lax.all_gather(local_keys, "ctx", axis=0, tiled=True)
    length = whole_keys.shape[0]
    offset = (lax.axis_index("ctx") * block_len).astype(jnp.int32).reshape(1)
    qr = jnp.transpose(query_rope[0], (2, 0, 1))
    t_blk = max(1, min(block_len, 1024 // heads))
    while block_len % t_blk:
        t_blk -= 1
    by_rows = pl.BlockSpec((t_blk, heads, kvr), lambda i, off: (i, 0, 0))
    rope_rows = pl.BlockSpec((t_blk, heads, rope), lambda i, off: (i, 0, 0))
    fixed = pl.BlockSpec((length, kvr + rope), lambda i, off: (0, 0))
    att, lqg, rqg, terms = pl.pallas_call(
        attention_kernel,
        grid_spec=pltpu.PrefetchScalarGridSpec(
            num_scalar_prefetch=1,
            grid=(block_len // t_blk,),
            in_specs=[by_rows, rope_rows, fixed, by_rows],
            out_specs=[by_rows, by_rows, rope_rows, fixed],
            scratch_shapes=[
                pltpu.VMEM((length, kvr), jnp.float32),
                pltpu.VMEM((length, rope), jnp.float32),
            ],
        ),
        out_shape=[
            jax.ShapeDtypeStruct((block_len, heads, kvr), jnp.bfloat16),
            jax.ShapeDtypeStruct((block_len, heads, kvr), jnp.bfloat16),
            jax.ShapeDtypeStruct((block_len, heads, rope), jnp.bfloat16),
            jax.ShapeDtypeStruct((length, kvr + rope), jnp.bfloat16),
        ],
        compiler_params=pltpu.CompilerParams(dimension_semantics=("arbitrary",)),
    )(offset, query_latent[0], qr, whole_keys, output_grad[0])
    attended = att[None]
    latent_qgrad = lqg[None]
    rope_qgrad = jnp.transpose(rqg, (1, 2, 0))[None]
    total = causal_reduce_ctx(terms.reshape(n_ctx, block_len, -1), n_ctx)
    total = butterfly_sum_ep(total, n_ep).astype(jnp.bfloat16)
    latent_kgrad = total[None, :, :kvr]
    rope_kgrad = total[:, kvr:].T[None]
    return (attended, latent_qgrad, rope_qgrad, latent_kgrad, rope_kgrad)


def solution(mesh):
    placed = (
        P(None, "ctx", "ep", None),
        P(None, "ep", None, "ctx"),
        P(None, "ctx", None),
        P(None, None, "ctx"),
        P(None, "ctx", "ep", None),
    )
    return jax.shard_map(
        body,
        mesh=mesh,
        in_specs=placed,
        out_specs=(
            P(None, "ctx", "ep", None),
            P(None, "ctx", "ep", None),
            P(None, "ep", None, "ctx"),
            P(None, "ctx", None),
            P(None, None, "ctx"),
        ),
        check_vma=False,
    )
```

```python
import jax
import jax.numpy as jnp
from jax import lax
from jax.experimental import pallas as pl
from jax.experimental.pallas import tpu as pltpu
from jax.sharding import PartitionSpec as P

scale_factor = 192.0 ** (-0.5)


def causal_reduce_ctx(blocks, n_ctx):
    here = lax.axis_index("ctx")
    if n_ctx % 2:
        total = jnp.take(blocks, here, axis=0).astype(jnp.float32)
        for shift in range(1, n_ctx):
            sent = jnp.take(blocks, jnp.maximum(here - shift, 0), axis=0)
            got = lax.ppermute(sent, "ctx", [(i, i - shift) for i in range(shift, n_ctx)])
            total = total + got.astype(jnp.float32)
        return total
    pairs = n_ctx // 2
    side = here % 2
    by_parity = blocks.reshape(pairs, 2, *blocks.shape[1:])
    mine = jnp.take(by_parity, side, axis=1)
    theirs = jnp.take(by_parity, 1 - side, axis=1)
    got = lax.ppermute(theirs, "ctx", [(i, i ^ 1) for i in range(n_ctx)])
    summed = (mine.astype(jnp.float32) + got.astype(jnp.float32)).astype(jnp.bfloat16)
    total = jnp.take(summed, here // 2, axis=0).astype(jnp.float32)
    for shift in range(1, pairs):
        sent = jnp.take(summed, jnp.maximum(here // 2 - shift, 0), axis=0)
        got = lax.ppermute(sent, "ctx", [(i, i - 2 * shift) for i in range(2 * shift, n_ctx)])
        total = total + got.astype(jnp.float32)
    return total


def butterfly_sum_ep(total, n_ep):
    if n_ep & (n_ep - 1):
        return lax.psum(total.astype(jnp.bfloat16), "ep").astype(jnp.float32)
    bit = 1
    while bit < n_ep:
        mine = total.astype(jnp.bfloat16)
        theirs = lax.ppermute(mine, "ep", [(i, i ^ bit) for i in range(n_ep)])
        total = mine.astype(jnp.float32) + theirs.astype(jnp.float32)
        bit *= 2
    return total


def attention_kernel(offset_ref, ql_ref, qr_ref, keys_ref, do_ref,
                     att_ref, sg_ref, terms_ref, lt_acc, rt_acc):
    step = pl.program_id(0)
    t_blk, heads, kvr = ql_ref.shape
    rope = qr_ref.shape[2]
    rows = t_blk * heads
    f32 = jnp.float32
    nt = (((1,), (1,)), ((), ()))
    tn = (((0,), (0,)), ((), ()))
    q = ql_ref[...].reshape(rows, kvr)
    qr = qr_ref[...].reshape(rows, rope)
    k = keys_ref[:, :kvr]
    kr = keys_ref[:, kvr:]
    dout = do_ref[...].reshape(rows, kvr)
    length = k.shape[0]
    scores = lax.dot_general(q, k, nt, preferred_element_type=f32)
    scores = scores + lax.dot_general(qr, kr, nt, preferred_element_type=f32)
    row = lax.broadcasted_iota(jnp.int32, (rows, length), 0)
    col = lax.broadcasted_iota(jnp.int32, (rows, length), 1)
    allowed = row >= heads * (col - offset_ref[0] - step * t_blk)
    scores = jnp.where(allowed, scores * scale_factor, f32(-1e30))
    row_max = jnp.max(scores, axis=-1, keepdims=True)
    powers = jnp.exp(scores - row_max)
    weights = powers / jnp.sum(powers, axis=-1, keepdims=True)
    rounded = weights.astype(jnp.bfloat16)
    att = jnp.dot(rounded, k, preferred_element_type=f32).astype(jnp.bfloat16)
    att_ref[...] = att.reshape(t_blk, heads, kvr)
    row_dots = jnp.sum(dout.astype(f32) * att.astype(f32), axis=-1, keepdims=True)
    weight_grad = lax.dot_general(dout, k, nt, preferred_element_type=f32)
    score_grad = (weights * (weight_grad - row_dots)).astype(jnp.bfloat16)
    sg_ref[...] = score_grad.reshape(t_blk, heads, length)
    lt = scale_factor * lax.dot_general(score_grad, q, tn, preferred_element_type=f32)
    lt = lt + lax.dot_general(rounded, dout, tn, preferred_element_type=f32)
    rt = scale_factor * lax.dot_general(score_grad, qr, tn, preferred_element_type=f32)

    @pl.when(step == 0)
    def _():
        lt_acc[...] = lt
        rt_acc[...] = rt

    @pl.when(step > 0)
    def _():
        lt_acc[...] += lt
        rt_acc[...] += rt

    @pl.when(step == pl.num_programs(0) - 1)
    def _():
        terms_ref[:, :kvr] = lt_acc[...].astype(jnp.bfloat16)
        terms_ref[:, kvr:] = rt_acc[...].astype(jnp.bfloat16)


def query_grad_kernel(sg_ref, keys_ref, lqg_ref, rqg_ref):
    t_blk, heads, length = sg_ref.shape
    kvr = lqg_ref.shape[2]
    rope = rqg_ref.shape[2]
    score_grad = sg_ref[...].reshape(t_blk * heads, length)
    lqg = scale_factor * jnp.dot(score_grad, keys_ref[:, :kvr], preferred_element_type=jnp.float32)
    lqg_ref[...] = lqg.astype(jnp.bfloat16).reshape(t_blk, heads, kvr)
    rqg = scale_factor * jnp.dot(score_grad, keys_ref[:, kvr:], preferred_element_type=jnp.float32)
    rqg_ref[...] = rqg.astype(jnp.bfloat16).reshape(t_blk, heads, rope)


def body(query_latent, query_rope, key_latent, key_rope, output_grad):
    n_ctx = lax.axis_size("ctx")
    n_ep = lax.axis_size("ep")
    _, block_len, heads, kvr = query_latent.shape
    rope = query_rope.shape[2]
    local_keys = jnp.concatenate([key_latent[0], key_rope[0].T], axis=1)
    whole_keys = lax.all_gather(local_keys, "ctx", axis=0, tiled=True)
    length = whole_keys.shape[0]
    offset = (lax.axis_index("ctx") * block_len).astype(jnp.int32).reshape(1)
    qr = jnp.transpose(query_rope[0], (2, 0, 1))
    t_blk = max(1, min(block_len, 1024 // heads))
    while block_len % t_blk:
        t_blk -= 1
    by_rows = pl.BlockSpec((t_blk, heads, kvr), lambda i, off: (i, 0, 0))
    rope_rows = pl.BlockSpec((t_blk, heads, rope), lambda i, off: (i, 0, 0))
    fixed = pl.BlockSpec((length, kvr + rope), lambda i, off: (0, 0))
    sg_rows = pl.BlockSpec((t_blk, heads, length), lambda i, off: (i, 0, 0))
    att, score_grad, terms = pl.pallas_call(
        attention_kernel,
        grid_spec=pltpu.PrefetchScalarGridSpec(
            num_scalar_prefetch=1,
            grid=(block_len // t_blk,),
            in_specs=[by_rows, rope_rows, fixed, by_rows],
            out_specs=[by_rows, sg_rows, fixed],
            scratch_shapes=[
                pltpu.VMEM((length, kvr), jnp.float32),
                pltpu.VMEM((length, rope), jnp.float32),
            ],
        ),
        out_shape=[
            jax.ShapeDtypeStruct((block_len, heads, kvr), jnp.bfloat16),
            jax.ShapeDtypeStruct((block_len, heads, length), jnp.bfloat16),
            jax.ShapeDtypeStruct((length, kvr + rope), jnp.bfloat16),
        ],
        compiler_params=pltpu.CompilerParams(dimension_semantics=("arbitrary",)),
    )(offset, query_latent[0], qr, whole_keys, output_grad[0])
    lqg, rqg = pl.pallas_call(
        query_grad_kernel,
        grid=(block_len // t_blk,),
        in_specs=[
            pl.BlockSpec((t_blk, heads, length), lambda i: (i, 0, 0)),
            pl.BlockSpec((length, kvr + rope), lambda i: (0, 0)),
        ],
        out_specs=[
            pl.BlockSpec((t_blk, heads, kvr), lambda i: (i, 0, 0)),
            pl.BlockSpec((t_blk, heads, rope), lambda i: (i, 0, 0)),
        ],
        out_shape=[
            jax.ShapeDtypeStruct((block_len, heads, kvr), jnp.bfloat16),
            jax.ShapeDtypeStruct((block_len, heads, rope), jnp.bfloat16),
        ],
        compiler_params=pltpu.CompilerParams(dimension_semantics=("arbitrary",)),
    )(score_grad, whole_keys)
    attended = att[None]
    latent_qgrad = lqg[None]
    rope_qgrad = jnp.transpose(rqg, (1, 2, 0))[None]
    total = causal_reduce_ctx(terms.reshape(n_ctx, block_len, -1), n_ctx)
    total = butterfly_sum_ep(total, n_ep).astype(jnp.bfloat16)
    latent_kgrad = total[None, :, :kvr]
    rope_kgrad = total[:, kvr:].T[None]
    return (attended, latent_qgrad, rope_qgrad, latent_kgrad, rope_kgrad)


def solution(mesh):
    placed = (
        P(None, "ctx", "ep", None),
        P(None, "ep", None, "ctx"),
        P(None, "ctx", None),
        P(None, None, "ctx"),
        P(None, "ctx", "ep", None),
    )
    return jax.shard_map(
        body,
        mesh=mesh,
        in_specs=placed,
        out_specs=(
            P(None, "ctx", "ep", None),
            P(None, "ctx", "ep", None),
            P(None, "ep", None, "ctx"),
            P(None, "ctx", None),
            P(None, None, "ctx"),
        ),
        check_vma=False,
    )
```

```python
import jax
import jax.numpy as jnp
from jax import lax
from jax.experimental import pallas as pl
from jax.experimental.pallas import tpu as pltpu
from jax.sharding import PartitionSpec as P

scale_factor = 192.0 ** (-0.5)


def causal_reduce_ctx(blocks, n_ctx):
    here = lax.axis_index("ctx")
    if n_ctx % 2:
        total = jnp.take(blocks, here, axis=0).astype(jnp.float32)
        for shift in range(1, n_ctx):
            sent = jnp.take(blocks, jnp.maximum(here - shift, 0), axis=0)
            got = lax.ppermute(sent, "ctx", [(i, i - shift) for i in range(shift, n_ctx)])
            total = total + got.astype(jnp.float32)
        return total
    pairs = n_ctx // 2
    side = here % 2
    by_parity = blocks.reshape(pairs, 2, *blocks.shape[1:])
    mine = jnp.take(by_parity, side, axis=1)
    theirs = jnp.take(by_parity, 1 - side, axis=1)
    got = lax.ppermute(theirs, "ctx", [(i, i ^ 1) for i in range(n_ctx)])
    summed = (mine.astype(jnp.float32) + got.astype(jnp.float32)).astype(jnp.bfloat16)
    total = jnp.take(summed, here // 2, axis=0).astype(jnp.float32)
    for shift in range(1, pairs):
        sent = jnp.take(summed, jnp.maximum(here // 2 - shift, 0), axis=0)
        got = lax.ppermute(sent, "ctx", [(i, i - 2 * shift) for i in range(2 * shift, n_ctx)])
        total = total + got.astype(jnp.float32)
    return total


def butterfly_sum_ep(total, n_ep):
    if n_ep & (n_ep - 1):
        return lax.psum(total.astype(jnp.bfloat16), "ep").astype(jnp.float32)
    bit = 1
    while bit < n_ep:
        mine = total.astype(jnp.bfloat16)
        theirs = lax.ppermute(mine, "ep", [(i, i ^ bit) for i in range(n_ep)])
        total = mine.astype(jnp.float32) + theirs.astype(jnp.float32)
        bit *= 2
    return total


def attention_kernel(offset_ref, ql_ref, qr_ref, keys_ref, do_ref,
                     att_ref, lqg_ref, rqg_ref, terms_ref, lt_acc, rt_acc):
    step = pl.program_id(0)
    t_blk, heads, kvr = ql_ref.shape
    rope = qr_ref.shape[2]
    rows = t_blk * heads
    f32 = jnp.float32
    nt = (((1,), (1,)), ((), ()))
    tn = (((0,), (0,)), ((), ()))
    q = ql_ref[...].reshape(rows, kvr)
    qr = qr_ref[...].reshape(rows, rope)
    k = keys_ref[:, :kvr]
    kr = keys_ref[:, kvr:]
    dout = do_ref[...].reshape(rows, kvr)
    length = k.shape[0]
    scores = lax.dot_general(q, k, nt, preferred_element_type=f32)
    scores = scores + lax.dot_general(qr, kr, nt, preferred_element_type=f32)
    row = lax.broadcasted_iota(jnp.int32, (rows, 1), 0)
    last_key = offset_ref[0] + step * t_blk + row // heads
    col = lax.broadcasted_iota(jnp.int32, (1, length), 1)
    scores = jnp.where(col <= last_key, scores * scale_factor, f32(-1e30))
    row_max = jnp.max(scores, axis=-1, keepdims=True)
    powers = jnp.exp(scores - row_max)
    weights = powers * (1.0 / jnp.sum(powers, axis=-1, keepdims=True))
    rounded = weights.astype(jnp.bfloat16)
    att = jnp.dot(rounded, k, preferred_element_type=f32).astype(jnp.bfloat16)
    att_ref[...] = att.reshape(t_blk, heads, kvr)
    row_dots = jnp.sum(dout.astype(f32) * att.astype(f32), axis=-1, keepdims=True)
    weight_grad = lax.dot_general(dout, k, nt, preferred_element_type=f32)
    score_grad = (weights * (weight_grad - row_dots)).astype(jnp.bfloat16)
    lqg = scale_factor * jnp.dot(score_grad, k, preferred_element_type=f32)
    lqg_ref[...] = lqg.astype(jnp.bfloat16).reshape(t_blk, heads, kvr)
    rqg = scale_factor * jnp.dot(score_grad, kr, preferred_element_type=f32)
    rqg_ref[...] = rqg.astype(jnp.bfloat16).reshape(t_blk, heads, rope)
    lt = scale_factor * lax.dot_general(score_grad, q, tn, preferred_element_type=f32)
    lt = lt + lax.dot_general(rounded, dout, tn, preferred_element_type=f32)
    rt = scale_factor * lax.dot_general(score_grad, qr, tn, preferred_element_type=f32)

    @pl.when(step == 0)
    def _():
        lt_acc[...] = lt
        rt_acc[...] = rt

    @pl.when(step > 0)
    def _():
        lt_acc[...] += lt
        rt_acc[...] += rt

    @pl.when(step == pl.num_programs(0) - 1)
    def _():
        terms_ref[:, :kvr] = lt_acc[...].astype(jnp.bfloat16)
        terms_ref[:, kvr:] = rt_acc[...].astype(jnp.bfloat16)


def body(query_latent, query_rope, key_latent, key_rope, output_grad):
    n_ctx = lax.axis_size("ctx")
    n_ep = lax.axis_size("ep")
    _, block_len, heads, kvr = query_latent.shape
    rope = query_rope.shape[2]
    local_keys = jnp.concatenate([key_latent[0], key_rope[0].T], axis=1)
    whole_keys = lax.all_gather(local_keys, "ctx", axis=0, tiled=True)
    length = whole_keys.shape[0]
    offset = (lax.axis_index("ctx") * block_len).astype(jnp.int32).reshape(1)
    qr = jnp.transpose(query_rope[0], (2, 0, 1))
    t_blk = max(1, min(block_len, 1024 // heads))
    while block_len % t_blk:
        t_blk -= 1
    by_rows = pl.BlockSpec((t_blk, heads, kvr), lambda i, off: (i, 0, 0))
    rope_rows = pl.BlockSpec((t_blk, heads, rope), lambda i, off: (i, 0, 0))
    fixed = pl.BlockSpec((length, kvr + rope), lambda i, off: (0, 0))
    att, lqg, rqg, terms = pl.pallas_call(
        attention_kernel,
        grid_spec=pltpu.PrefetchScalarGridSpec(
            num_scalar_prefetch=1,
            grid=(block_len // t_blk,),
            in_specs=[by_rows, rope_rows, fixed, by_rows],
            out_specs=[by_rows, by_rows, rope_rows, fixed],
            scratch_shapes=[
                pltpu.VMEM((length, kvr), jnp.float32),
                pltpu.VMEM((length, rope), jnp.float32),
            ],
        ),
        out_shape=[
            jax.ShapeDtypeStruct((block_len, heads, kvr), jnp.bfloat16),
            jax.ShapeDtypeStruct((block_len, heads, kvr), jnp.bfloat16),
            jax.ShapeDtypeStruct((block_len, heads, rope), jnp.bfloat16),
            jax.ShapeDtypeStruct((length, kvr + rope), jnp.bfloat16),
        ],
        compiler_params=pltpu.CompilerParams(dimension_semantics=("arbitrary",)),
    )(offset, query_latent[0], qr, whole_keys, output_grad[0])
    attended = att[None]
    latent_qgrad = lqg[None]
    rope_qgrad = jnp.transpose(rqg, (1, 2, 0))[None]
    total = causal_reduce_ctx(terms.reshape(n_ctx, block_len, -1), n_ctx)
    total = butterfly_sum_ep(total, n_ep).astype(jnp.bfloat16)
    latent_kgrad = total[None, :, :kvr]
    rope_kgrad = total[:, kvr:].T[None]
    return (attended, latent_qgrad, rope_qgrad, latent_kgrad, rope_kgrad)


def solution(mesh):
    placed = (
        P(None, "ctx", "ep", None),
        P(None, "ep", None, "ctx"),
        P(None, "ctx", None),
        P(None, None, "ctx"),
        P(None, "ctx", "ep", None),
    )
    return jax.shard_map(
        body,
        mesh=mesh,
        in_specs=placed,
        out_specs=(
            P(None, "ctx", "ep", None),
            P(None, "ctx", "ep", None),
            P(None, "ep", None, "ctx"),
            P(None, "ctx", None),
            P(None, None, "ctx"),
        ),
        check_vma=False,
    )
```

```python
import jax
import jax.numpy as jnp
from jax import lax
from jax.experimental import pallas as pl
from jax.experimental.pallas import tpu as pltpu
from jax.sharding import PartitionSpec as P

scale_factor = 192.0 ** (-0.5)


def causal_reduce_ctx(blocks, n_ctx):
    here = lax.axis_index("ctx")
    if n_ctx % 2:
        total = jnp.take(blocks, here, axis=0).astype(jnp.float32)
        for shift in range(1, n_ctx):
            sent = jnp.take(blocks, jnp.maximum(here - shift, 0), axis=0)
            got = lax.ppermute(sent, "ctx", [(i, i - shift) for i in range(shift, n_ctx)])
            total = total + got.astype(jnp.float32)
        return total
    pairs = n_ctx // 2
    mine, theirs = blocks[:pairs], blocks[pairs:]
    got = lax.ppermute(theirs, "ctx", [(i, i ^ 1) for i in range(n_ctx)])
    summed = (mine.astype(jnp.float32) + got.astype(jnp.float32)).astype(jnp.bfloat16)
    total = jnp.take(summed, here // 2, axis=0).astype(jnp.float32)
    for shift in range(1, pairs):
        sent = jnp.take(summed, jnp.maximum(here // 2 - shift, 0), axis=0)
        got = lax.ppermute(sent, "ctx", [(i, i - 2 * shift) for i in range(2 * shift, n_ctx)])
        total = total + got.astype(jnp.float32)
    return total


def butterfly_sum_ep(total, n_ep):
    if n_ep & (n_ep - 1):
        return lax.psum(total.astype(jnp.bfloat16), "ep").astype(jnp.float32)
    bit = 1
    while bit < n_ep:
        mine = total.astype(jnp.bfloat16)
        theirs = lax.ppermute(mine, "ep", [(i, i ^ bit) for i in range(n_ep)])
        total = mine.astype(jnp.float32) + theirs.astype(jnp.float32)
        bit *= 2
    return total


def attention_kernel(offset_ref, ql_ref, qr_ref, keys_ref, do_ref,
                     att_ref, lqg_ref, rqg_ref, terms_ref, lt_acc, rt_acc):
    step = pl.program_id(0)
    t_blk, heads, kvr = ql_ref.shape
    rope = qr_ref.shape[2]
    rows = t_blk * heads
    f32 = jnp.float32
    nt = (((1,), (1,)), ((), ()))
    tn = (((0,), (0,)), ((), ()))
    q = ql_ref[...].reshape(rows, kvr)
    qr = qr_ref[...].reshape(rows, rope)
    k = keys_ref[:, :kvr]
    kr = keys_ref[:, kvr:]
    dout = do_ref[...].reshape(rows, kvr)
    length = k.shape[0]
    scores = lax.dot_general(q, k, nt, preferred_element_type=f32)
    scores = scores + lax.dot_general(qr, kr, nt, preferred_element_type=f32)
    row = lax.broadcasted_iota(jnp.int32, (rows, 1), 0)
    last_key = offset_ref[0] + step * t_blk + row // heads
    col = lax.broadcasted_iota(jnp.int32, (1, length), 1)
    scores = jnp.where(col <= last_key, scores * scale_factor, f32(-1e30))
    row_max = jnp.max(scores, axis=-1, keepdims=True)
    powers = jnp.exp(scores - row_max)
    weights = powers * (1.0 / jnp.sum(powers, axis=-1, keepdims=True))
    rounded = weights.astype(jnp.bfloat16)
    att = jnp.dot(rounded, k, preferred_element_type=f32).astype(jnp.bfloat16)
    att_ref[...] = att.reshape(t_blk, heads, kvr)
    row_dots = jnp.sum(dout.astype(f32) * att.astype(f32), axis=-1, keepdims=True)
    weight_grad = lax.dot_general(dout, k, nt, preferred_element_type=f32)
    score_grad = (weights * (weight_grad - row_dots)).astype(jnp.bfloat16)
    lqg = scale_factor * jnp.dot(score_grad, k, preferred_element_type=f32)
    lqg_ref[...] = lqg.astype(jnp.bfloat16).reshape(t_blk, heads, kvr)
    rqg = scale_factor * jnp.dot(score_grad, kr, preferred_element_type=f32)
    rqg_ref[...] = rqg.astype(jnp.bfloat16).reshape(t_blk, heads, rope)
    lt = scale_factor * lax.dot_general(score_grad, q, tn, preferred_element_type=f32)
    lt = lt + lax.dot_general(rounded, dout, tn, preferred_element_type=f32)
    rt = scale_factor * lax.dot_general(score_grad, qr, tn, preferred_element_type=f32)

    @pl.when(step == 0)
    def _():
        lt_acc[...] = lt
        rt_acc[...] = rt

    @pl.when(step > 0)
    def _():
        lt_acc[...] += lt
        rt_acc[...] += rt

    @pl.when(step == pl.num_programs(0) - 1)
    def _():
        n_blocks, block_len = terms_ref.shape[0], terms_ref.shape[1]
        pairs = n_blocks // 2
        side = (offset_ref[0] // block_len) % 2 if n_blocks % 2 == 0 else 0
        for slot in range(n_blocks):
            if n_blocks % 2:
                start = slot * block_len
            elif slot < pairs:
                start = (2 * slot + side) * block_len
            else:
                start = (2 * (slot - pairs) + 1 - side) * block_len
            start = pl.multiple_of(start, block_len)
            terms_ref[slot, :, :kvr] = lt_acc[pl.ds(start, block_len), :].astype(jnp.bfloat16)
            terms_ref[slot, :, kvr:] = rt_acc[pl.ds(start, block_len), :].astype(jnp.bfloat16)


def body(query_latent, query_rope, key_latent, key_rope, output_grad):
    n_ctx = lax.axis_size("ctx")
    n_ep = lax.axis_size("ep")
    _, block_len, heads, kvr = query_latent.shape
    rope = query_rope.shape[2]
    local_keys = jnp.concatenate([key_latent[0], key_rope[0].T], axis=1)
    whole_keys = lax.all_gather(local_keys, "ctx", axis=0, tiled=True)
    length = whole_keys.shape[0]
    offset = (lax.axis_index("ctx") * block_len).astype(jnp.int32).reshape(1)
    qr = jnp.transpose(query_rope[0], (2, 0, 1))
    t_blk = max(1, min(block_len, 1024 // heads))
    while block_len % t_blk:
        t_blk -= 1
    by_rows = pl.BlockSpec((t_blk, heads, kvr), lambda i, off: (i, 0, 0))
    rope_rows = pl.BlockSpec((t_blk, heads, rope), lambda i, off: (i, 0, 0))
    fixed = pl.BlockSpec((length, kvr + rope), lambda i, off: (0, 0))
    term_blocks = pl.BlockSpec((n_ctx, block_len, kvr + rope), lambda i, off: (0, 0, 0))
    att, lqg, rqg, terms = pl.pallas_call(
        attention_kernel,
        grid_spec=pltpu.PrefetchScalarGridSpec(
            num_scalar_prefetch=1,
            grid=(block_len // t_blk,),
            in_specs=[by_rows, rope_rows, fixed, by_rows],
            out_specs=[by_rows, by_rows, rope_rows, term_blocks],
            scratch_shapes=[
                pltpu.VMEM((length, kvr), jnp.float32),
                pltpu.VMEM((length, rope), jnp.float32),
            ],
        ),
        out_shape=[
            jax.ShapeDtypeStruct((block_len, heads, kvr), jnp.bfloat16),
            jax.ShapeDtypeStruct((block_len, heads, kvr), jnp.bfloat16),
            jax.ShapeDtypeStruct((block_len, heads, rope), jnp.bfloat16),
            jax.ShapeDtypeStruct((n_ctx, block_len, kvr + rope), jnp.bfloat16),
        ],
        compiler_params=pltpu.CompilerParams(dimension_semantics=("arbitrary",)),
    )(offset, query_latent[0], qr, whole_keys, output_grad[0])
    attended = att[None]
    latent_qgrad = lqg[None]
    rope_qgrad = jnp.transpose(rqg, (1, 2, 0))[None]
    total = causal_reduce_ctx(terms, n_ctx)
    total = butterfly_sum_ep(total, n_ep).astype(jnp.bfloat16)
    latent_kgrad = total[None, :, :kvr]
    rope_kgrad = total[:, kvr:].T[None]
    return (attended, latent_qgrad, rope_qgrad, latent_kgrad, rope_kgrad)


def solution(mesh):
    placed = (
        P(None, "ctx", "ep", None),
        P(None, "ep", None, "ctx"),
        P(None, "ctx", None),
        P(None, None, "ctx"),
        P(None, "ctx", "ep", None),
    )
    return jax.shard_map(
        body,
        mesh=mesh,
        in_specs=placed,
        out_specs=(
            P(None, "ctx", "ep", None),
            P(None, "ctx", "ep", None),
            P(None, "ep", None, "ctx"),
            P(None, "ctx", None),
            P(None, None, "ctx"),
        ),
        check_vma=False,
    )
```

```python
import jax
import jax.numpy as jnp
from jax import lax
from jax.experimental import pallas as pl
from jax.experimental.pallas import tpu as pltpu
from jax.sharding import PartitionSpec as P

scale_factor = 192.0 ** (-0.5)


def causal_reduce_ctx(blocks, theirs, n_ctx):
    here = lax.axis_index("ctx")
    if n_ctx % 2:
        total = jnp.take(blocks, here, axis=0).astype(jnp.float32)
        for shift in range(1, n_ctx):
            sent = jnp.take(blocks, jnp.maximum(here - shift, 0), axis=0)
            got = lax.ppermute(sent, "ctx", [(i, i - shift) for i in range(shift, n_ctx)])
            total = total + got.astype(jnp.float32)
        return total
    pairs = n_ctx // 2
    mine = blocks
    got = lax.ppermute(theirs, "ctx", [(i, i ^ 1) for i in range(n_ctx)])
    summed = (mine.astype(jnp.float32) + got.astype(jnp.float32)).astype(jnp.bfloat16)
    total = jnp.take(summed, here // 2, axis=0).astype(jnp.float32)
    for shift in range(1, pairs):
        sent = jnp.take(summed, jnp.maximum(here // 2 - shift, 0), axis=0)
        got = lax.ppermute(sent, "ctx", [(i, i - 2 * shift) for i in range(2 * shift, n_ctx)])
        total = total + got.astype(jnp.float32)
    return total


def butterfly_sum_ep(total, n_ep):
    if n_ep & (n_ep - 1):
        return lax.psum(total.astype(jnp.bfloat16), "ep").astype(jnp.float32)
    bit = 1
    while bit < n_ep:
        mine = total.astype(jnp.bfloat16)
        theirs = lax.ppermute(mine, "ep", [(i, i ^ bit) for i in range(n_ep)])
        total = mine.astype(jnp.float32) + theirs.astype(jnp.float32)
        bit *= 2
    return total


def attention_kernel(offset_ref, ql_ref, qr_ref, keys_ref, do_ref,
                     att_ref, lqg_ref, rqg_ref, mine_ref, theirs_ref, lt_acc, rt_acc):
    step = pl.program_id(0)
    t_blk, heads, kvr = ql_ref.shape
    rope = qr_ref.shape[2]
    rows = t_blk * heads
    f32 = jnp.float32
    nt = (((1,), (1,)), ((), ()))
    tn = (((0,), (0,)), ((), ()))
    q = ql_ref[...].reshape(rows, kvr)
    qr = qr_ref[...].reshape(rows, rope)
    k = keys_ref[:, :kvr]
    kr = keys_ref[:, kvr:]
    dout = do_ref[...].reshape(rows, kvr)
    length = k.shape[0]
    scores = lax.dot_general(q, k, nt, preferred_element_type=f32)
    scores = scores + lax.dot_general(qr, kr, nt, preferred_element_type=f32)
    row = lax.broadcasted_iota(jnp.int32, (rows, 1), 0)
    last_key = offset_ref[0] + step * t_blk + row // heads
    col = lax.broadcasted_iota(jnp.int32, (1, length), 1)
    scores = jnp.where(col <= last_key, scores * scale_factor, f32(-1e30))
    row_max = jnp.max(scores, axis=-1, keepdims=True)
    powers = jnp.exp(scores - row_max)
    weights = powers * (1.0 / jnp.sum(powers, axis=-1, keepdims=True))
    rounded = weights.astype(jnp.bfloat16)
    att = jnp.dot(rounded, k, preferred_element_type=f32).astype(jnp.bfloat16)
    att_ref[...] = att.reshape(t_blk, heads, kvr)
    row_dots = jnp.sum(dout.astype(f32) * att.astype(f32), axis=-1, keepdims=True)
    weight_grad = lax.dot_general(dout, k, nt, preferred_element_type=f32)
    score_grad = (weights * (weight_grad - row_dots)).astype(jnp.bfloat16)
    lqg = scale_factor * jnp.dot(score_grad, k, preferred_element_type=f32)
    lqg_ref[...] = lqg.astype(jnp.bfloat16).reshape(t_blk, heads, kvr)
    rqg = scale_factor * jnp.dot(score_grad, kr, preferred_element_type=f32)
    rqg_ref[...] = rqg.astype(jnp.bfloat16).reshape(t_blk, heads, rope)
    lt = scale_factor * lax.dot_general(score_grad, q, tn, preferred_element_type=f32)
    lt = lt + lax.dot_general(rounded, dout, tn, preferred_element_type=f32)
    rt = scale_factor * lax.dot_general(score_grad, qr, tn, preferred_element_type=f32)

    @pl.when(step == 0)
    def _():
        lt_acc[...] = lt
        rt_acc[...] = rt

    @pl.when(step > 0)
    def _():
        lt_acc[...] += lt
        rt_acc[...] += rt

    @pl.when(step == pl.num_programs(0) - 1)
    def _():
        block_len = mine_ref.shape[1]
        n_blocks = lt_acc.shape[0] // block_len
        even = n_blocks % 2 == 0
        side = (offset_ref[0] // block_len) % 2 if even else 0
        for slot in range(mine_ref.shape[0]):
            start = (2 * slot + side) * block_len if even else slot * block_len
            start = pl.multiple_of(start, block_len)
            mine_ref[slot, :, :kvr] = lt_acc[pl.ds(start, block_len), :].astype(jnp.bfloat16)
            mine_ref[slot, :, kvr:] = rt_acc[pl.ds(start, block_len), :].astype(jnp.bfloat16)
        for slot in range(theirs_ref.shape[0]):
            if even:
                start = pl.multiple_of((2 * slot + 1 - side) * block_len, block_len)
                theirs_ref[slot, :, :kvr] = lt_acc[pl.ds(start, block_len), :].astype(jnp.bfloat16)
                theirs_ref[slot, :, kvr:] = rt_acc[pl.ds(start, block_len), :].astype(jnp.bfloat16)
            else:
                theirs_ref[slot] = jnp.zeros(theirs_ref.shape[1:], jnp.bfloat16)


def body(query_latent, query_rope, key_latent, key_rope, output_grad):
    n_ctx = lax.axis_size("ctx")
    n_ep = lax.axis_size("ep")
    _, block_len, heads, kvr = query_latent.shape
    rope = query_rope.shape[2]
    local_keys = jnp.concatenate([key_latent[0], key_rope[0].T], axis=1)
    whole_keys = lax.all_gather(local_keys, "ctx", axis=0, tiled=True)
    length = whole_keys.shape[0]
    offset = (lax.axis_index("ctx") * block_len).astype(jnp.int32).reshape(1)
    qr = jnp.transpose(query_rope[0], (2, 0, 1))
    t_blk = max(1, min(block_len, 1024 // heads))
    while block_len % t_blk:
        t_blk -= 1
    by_rows = pl.BlockSpec((t_blk, heads, kvr), lambda i, off: (i, 0, 0))
    rope_rows = pl.BlockSpec((t_blk, heads, rope), lambda i, off: (i, 0, 0))
    fixed = pl.BlockSpec((length, kvr + rope), lambda i, off: (0, 0))
    n_mine = n_ctx // 2 if n_ctx % 2 == 0 else n_ctx
    n_theirs = n_ctx // 2 if n_ctx % 2 == 0 else 1
    mine_blocks = pl.BlockSpec((n_mine, block_len, kvr + rope), lambda i, off: (0, 0, 0))
    their_blocks = pl.BlockSpec((n_theirs, block_len, kvr + rope), lambda i, off: (0, 0, 0))
    att, lqg, rqg, mine, theirs = pl.pallas_call(
        attention_kernel,
        grid_spec=pltpu.PrefetchScalarGridSpec(
            num_scalar_prefetch=1,
            grid=(block_len // t_blk,),
            in_specs=[by_rows, rope_rows, fixed, by_rows],
            out_specs=[by_rows, by_rows, rope_rows, mine_blocks, their_blocks],
            scratch_shapes=[
                pltpu.VMEM((length, kvr), jnp.float32),
                pltpu.VMEM((length, rope), jnp.float32),
            ],
        ),
        out_shape=[
            jax.ShapeDtypeStruct((block_len, heads, kvr), jnp.bfloat16),
            jax.ShapeDtypeStruct((block_len, heads, kvr), jnp.bfloat16),
            jax.ShapeDtypeStruct((block_len, heads, rope), jnp.bfloat16),
            jax.ShapeDtypeStruct((n_mine, block_len, kvr + rope), jnp.bfloat16),
            jax.ShapeDtypeStruct((n_theirs, block_len, kvr + rope), jnp.bfloat16),
        ],
        compiler_params=pltpu.CompilerParams(dimension_semantics=("arbitrary",)),
    )(offset, query_latent[0], qr, whole_keys, output_grad[0])
    attended = att[None]
    latent_qgrad = lqg[None]
    rope_qgrad = jnp.transpose(rqg, (1, 2, 0))[None]
    total = causal_reduce_ctx(mine, theirs, n_ctx)
    total = butterfly_sum_ep(total, n_ep).astype(jnp.bfloat16)
    latent_kgrad = total[None, :, :kvr]
    rope_kgrad = total[:, kvr:].T[None]
    return (attended, latent_qgrad, rope_qgrad, latent_kgrad, rope_kgrad)


def solution(mesh):
    placed = (
        P(None, "ctx", "ep", None),
        P(None, "ep", None, "ctx"),
        P(None, "ctx", None),
        P(None, None, "ctx"),
        P(None, "ctx", "ep", None),
    )
    return jax.shard_map(
        body,
        mesh=mesh,
        in_specs=placed,
        out_specs=(
            P(None, "ctx", "ep", None),
            P(None, "ctx", "ep", None),
            P(None, "ep", None, "ctx"),
            P(None, "ctx", None),
            P(None, None, "ctx"),
        ),
        check_vma=False,
    )
```

```python
import jax
import jax.numpy as jnp
from jax import lax
from jax.experimental import pallas as pl
from jax.experimental.pallas import tpu as pltpu
from jax.sharding import PartitionSpec as P

scale_factor = 192.0 ** (-0.5)


def causal_reduce_ctx(blocks, theirs, n_ctx):
    here = lax.axis_index("ctx")
    if n_ctx % 2:
        total = jnp.take(blocks, here, axis=0).astype(jnp.float32)
        for shift in range(1, n_ctx):
            sent = jnp.take(blocks, jnp.maximum(here - shift, 0), axis=0)
            got = lax.ppermute(sent, "ctx", [(i, i - shift) for i in range(shift, n_ctx)])
            total = total + got.astype(jnp.float32)
        return total
    pairs = n_ctx // 2
    mine = blocks
    got = lax.ppermute(theirs, "ctx", [(i, i ^ 1) for i in range(n_ctx)])
    summed = (mine.astype(jnp.float32) + got.astype(jnp.float32)).astype(jnp.bfloat16)
    total = jnp.take(summed, here // 2, axis=0).astype(jnp.float32)
    for shift in range(1, pairs):
        sent = jnp.take(summed, jnp.maximum(here // 2 - shift, 0), axis=0)
        got = lax.ppermute(sent, "ctx", [(i, i - 2 * shift) for i in range(2 * shift, n_ctx)])
        total = total + got.astype(jnp.float32)
    return total


def butterfly_sum_ep(total, n_ctx, n_ep):
    if n_ep & (n_ep - 1):
        return lax.psum(total.astype(jnp.bfloat16), "ep").astype(jnp.float32)
    bits = [1 << k for k in range(n_ep.bit_length() - 1)]
    orders = [bits, bits[1:] + bits[:1]]
    for step in range(len(bits)):
        pairs = [
            (c * n_ep + e, c * n_ep + (e ^ orders[c % 2][step]))
            for c in range(n_ctx)
            for e in range(n_ep)
        ]
        mine = total.astype(jnp.bfloat16)
        theirs = lax.ppermute(mine, ("ctx", "ep"), pairs)
        total = mine.astype(jnp.float32) + theirs.astype(jnp.float32)
    return total


def attention_kernel(offset_ref, ql_ref, qr_ref, keys_ref, do_ref,
                     att_ref, lqg_ref, rqg_ref, mine_ref, theirs_ref, lt_acc, rt_acc):
    step = pl.program_id(0)
    t_blk, heads, kvr = ql_ref.shape
    rope = qr_ref.shape[2]
    rows = t_blk * heads
    f32 = jnp.float32
    nt = (((1,), (1,)), ((), ()))
    tn = (((0,), (0,)), ((), ()))
    q = ql_ref[...].reshape(rows, kvr)
    qr = qr_ref[...].reshape(rows, rope)
    k = keys_ref[:, :kvr]
    kr = keys_ref[:, kvr:]
    dout = do_ref[...].reshape(rows, kvr)
    length = k.shape[0]
    scores = lax.dot_general(q, k, nt, preferred_element_type=f32)
    scores = scores + lax.dot_general(qr, kr, nt, preferred_element_type=f32)
    row = lax.broadcasted_iota(jnp.int32, (rows, 1), 0)
    last_key = offset_ref[0] + step * t_blk + row // heads
    col = lax.broadcasted_iota(jnp.int32, (1, length), 1)
    scores = jnp.where(col <= last_key, scores * scale_factor, f32(-1e30))
    row_max = jnp.max(scores, axis=-1, keepdims=True)
    powers = jnp.exp(scores - row_max)
    weights = powers * (1.0 / jnp.sum(powers, axis=-1, keepdims=True))
    rounded = weights.astype(jnp.bfloat16)
    att = jnp.dot(rounded, k, preferred_element_type=f32).astype(jnp.bfloat16)
    att_ref[...] = att.reshape(t_blk, heads, kvr)
    row_dots = jnp.sum(dout.astype(f32) * att.astype(f32), axis=-1, keepdims=True)
    weight_grad = lax.dot_general(dout, k, nt, preferred_element_type=f32)
    score_grad = (weights * (weight_grad - row_dots)).astype(jnp.bfloat16)
    lqg = scale_factor * jnp.dot(score_grad, k, preferred_element_type=f32)
    lqg_ref[...] = lqg.astype(jnp.bfloat16).reshape(t_blk, heads, kvr)
    rqg = scale_factor * jnp.dot(score_grad, kr, preferred_element_type=f32)
    rqg_ref[...] = rqg.astype(jnp.bfloat16).reshape(t_blk, heads, rope)
    lt = scale_factor * lax.dot_general(score_grad, q, tn, preferred_element_type=f32)
    lt = lt + lax.dot_general(rounded, dout, tn, preferred_element_type=f32)
    rt = scale_factor * lax.dot_general(score_grad, qr, tn, preferred_element_type=f32)

    @pl.when(step == 0)
    def _():
        lt_acc[...] = lt
        rt_acc[...] = rt

    @pl.when(step > 0)
    def _():
        lt_acc[...] += lt
        rt_acc[...] += rt

    @pl.when(step == pl.num_programs(0) - 1)
    def _():
        block_len = mine_ref.shape[1]
        n_blocks = lt_acc.shape[0] // block_len
        even = n_blocks % 2 == 0
        side = (offset_ref[0] // block_len) % 2 if even else 0
        for slot in range(mine_ref.shape[0]):
            start = (2 * slot + side) * block_len if even else slot * block_len
            start = pl.multiple_of(start, block_len)
            mine_ref[slot, :, :kvr] = lt_acc[pl.ds(start, block_len), :].astype(jnp.bfloat16)
            mine_ref[slot, :, kvr:] = rt_acc[pl.ds(start, block_len), :].astype(jnp.bfloat16)
        for slot in range(theirs_ref.shape[0]):
            if even:
                start = pl.multiple_of((2 * slot + 1 - side) * block_len, block_len)
                theirs_ref[slot, :, :kvr] = lt_acc[pl.ds(start, block_len), :].astype(jnp.bfloat16)
                theirs_ref[slot, :, kvr:] = rt_acc[pl.ds(start, block_len), :].astype(jnp.bfloat16)
            else:
                theirs_ref[slot] = jnp.zeros(theirs_ref.shape[1:], jnp.bfloat16)


def body(query_latent, query_rope, key_latent, key_rope, output_grad):
    n_ctx = lax.axis_size("ctx")
    n_ep = lax.axis_size("ep")
    _, block_len, heads, kvr = query_latent.shape
    rope = query_rope.shape[2]
    local_keys = jnp.concatenate([key_latent[0], key_rope[0].T], axis=1)
    whole_keys = lax.all_gather(local_keys, "ctx", axis=0, tiled=True)
    length = whole_keys.shape[0]
    offset = (lax.axis_index("ctx") * block_len).astype(jnp.int32).reshape(1)
    qr = jnp.transpose(query_rope[0], (2, 0, 1))
    t_blk = max(1, min(block_len, 1024 // heads))
    while block_len % t_blk:
        t_blk -= 1
    by_rows = pl.BlockSpec((t_blk, heads, kvr), lambda i, off: (i, 0, 0))
    rope_rows = pl.BlockSpec((t_blk, heads, rope), lambda i, off: (i, 0, 0))
    fixed = pl.BlockSpec((length, kvr + rope), lambda i, off: (0, 0))
    n_mine = n_ctx // 2 if n_ctx % 2 == 0 else n_ctx
    n_theirs = n_ctx // 2 if n_ctx % 2 == 0 else 1
    mine_blocks = pl.BlockSpec((n_mine, block_len, kvr + rope), lambda i, off: (0, 0, 0))
    their_blocks = pl.BlockSpec((n_theirs, block_len, kvr + rope), lambda i, off: (0, 0, 0))
    att, lqg, rqg, mine, theirs = pl.pallas_call(
        attention_kernel,
        grid_spec=pltpu.PrefetchScalarGridSpec(
            num_scalar_prefetch=1,
            grid=(block_len // t_blk,),
            in_specs=[by_rows, rope_rows, fixed, by_rows],
            out_specs=[by_rows, by_rows, rope_rows, mine_blocks, their_blocks],
            scratch_shapes=[
                pltpu.VMEM((length, kvr), jnp.float32),
                pltpu.VMEM((length, rope), jnp.float32),
            ],
        ),
        out_shape=[
            jax.ShapeDtypeStruct((block_len, heads, kvr), jnp.bfloat16),
            jax.ShapeDtypeStruct((block_len, heads, kvr), jnp.bfloat16),
            jax.ShapeDtypeStruct((block_len, heads, rope), jnp.bfloat16),
            jax.ShapeDtypeStruct((n_mine, block_len, kvr + rope), jnp.bfloat16),
            jax.ShapeDtypeStruct((n_theirs, block_len, kvr + rope), jnp.bfloat16),
        ],
        compiler_params=pltpu.CompilerParams(dimension_semantics=("arbitrary",)),
    )(offset, query_latent[0], qr, whole_keys, output_grad[0])
    attended = att[None]
    latent_qgrad = lqg[None]
    rope_qgrad = jnp.transpose(rqg, (1, 2, 0))[None]
    total = causal_reduce_ctx(mine, theirs, n_ctx)
    total = butterfly_sum_ep(total, n_ctx, n_ep).astype(jnp.bfloat16)
    latent_kgrad = total[None, :, :kvr]
    rope_kgrad = total[:, kvr:].T[None]
    return (attended, latent_qgrad, rope_qgrad, latent_kgrad, rope_kgrad)


def solution(mesh):
    placed = (
        P(None, "ctx", "ep", None),
        P(None, "ep", None, "ctx"),
        P(None, "ctx", None),
        P(None, None, "ctx"),
        P(None, "ctx", "ep", None),
    )
    return jax.shard_map(
        body,
        mesh=mesh,
        in_specs=placed,
        out_specs=(
            P(None, "ctx", "ep", None),
            P(None, "ctx", "ep", None),
            P(None, "ep", None, "ctx"),
            P(None, "ctx", None),
            P(None, None, "ctx"),
        ),
        check_vma=False,
    )
```

```python
import jax
import jax.numpy as jnp
from jax import lax
from jax.experimental import pallas as pl
from jax.experimental.pallas import tpu as pltpu
from jax.sharding import PartitionSpec as P

scale_factor = 192.0 ** (-0.5)


def causal_reduce_ctx(blocks, theirs, n_ctx):
    here = lax.axis_index("ctx")
    if n_ctx % 2:
        total = jnp.take(blocks, here, axis=0).astype(jnp.float32)
        for shift in range(1, n_ctx):
            sent = jnp.take(blocks, jnp.maximum(here - shift, 0), axis=0)
            got = lax.ppermute(sent, "ctx", [(i, i - shift) for i in range(shift, n_ctx)])
            total = total + got.astype(jnp.float32)
        return total
    pairs = n_ctx // 2
    mine = blocks
    got = lax.ppermute(theirs, "ctx", [(i, i ^ 1) for i in range(n_ctx)])
    summed = (mine.astype(jnp.float32) + got.astype(jnp.float32)).astype(jnp.bfloat16)
    total = jnp.take(summed, here // 2, axis=0).astype(jnp.float32)
    for shift in range(1, pairs):
        sent = jnp.take(summed, jnp.maximum(here // 2 - shift, 0), axis=0)
        got = lax.ppermute(sent, "ctx", [(i, i - 2 * shift) for i in range(2 * shift, n_ctx)])
        total = total + got.astype(jnp.float32)
    return total


def butterfly_sum_ep(total, n_ctx, n_ep):
    if n_ep & (n_ep - 1):
        return lax.psum(total.astype(jnp.bfloat16), "ep").astype(jnp.float32)
    bits = [1 << k for k in range(n_ep.bit_length() - 1)]
    orders = [bits, bits[1:] + bits[:1]]
    for step in range(len(bits)):
        pairs = [
            (c * n_ep + e, c * n_ep + (e ^ orders[c % 2][step]))
            for c in range(n_ctx)
            for e in range(n_ep)
        ]
        mine = total.astype(jnp.bfloat16)
        theirs = lax.ppermute(mine, ("ctx", "ep"), pairs)
        total = mine.astype(jnp.float32) + theirs.astype(jnp.float32)
    return total


def attention_kernel(offset_ref, ql_ref, qr_ref, keys_ref, do_ref,
                     att_ref, lqg_ref, rqg_ref, mine_ref, theirs_ref, lt_acc, rt_acc):
    step = pl.program_id(0)
    t_blk, heads, kvr = ql_ref.shape
    rope = qr_ref.shape[2]
    rows = t_blk * heads
    f32 = jnp.float32
    nt = (((1,), (1,)), ((), ()))
    tn = (((0,), (0,)), ((), ()))
    q = ql_ref[...].reshape(rows, kvr)
    qr = qr_ref[...].reshape(rows, rope)
    k = keys_ref[:, :kvr]
    kr = keys_ref[:, kvr:]
    dout = do_ref[...].reshape(rows, kvr)
    length = k.shape[0]
    scores = lax.dot_general(q, k, nt, preferred_element_type=f32)
    scores = scores + lax.dot_general(qr, kr, nt, preferred_element_type=f32)
    row = lax.broadcasted_iota(jnp.int32, (rows, 1), 0)
    last_key = offset_ref[0] + step * t_blk + row // heads
    col = lax.broadcasted_iota(jnp.int32, (1, length), 1)
    scores = jnp.where(col <= last_key, scores * scale_factor, f32(-1e30))
    row_max = jnp.max(scores, axis=-1, keepdims=True)
    powers = jnp.exp(scores - row_max)
    weights = powers * (1.0 / jnp.sum(powers, axis=-1, keepdims=True))
    rounded = weights.astype(jnp.bfloat16)
    att = jnp.dot(rounded, k, preferred_element_type=f32).astype(jnp.bfloat16)
    att_ref[...] = att.reshape(t_blk, heads, kvr)
    row_dots = jnp.sum(dout.astype(f32) * att.astype(f32), axis=-1, keepdims=True)
    weight_grad = lax.dot_general(dout, k, nt, preferred_element_type=f32)
    score_grad = (weights * (weight_grad - row_dots)).astype(jnp.bfloat16)
    lqg = scale_factor * jnp.dot(score_grad, k, preferred_element_type=f32)
    lqg_ref[...] = lqg.astype(jnp.bfloat16).reshape(t_blk, heads, kvr)
    rqg = scale_factor * jnp.dot(score_grad, kr, preferred_element_type=f32)
    rqg_ref[...] = rqg.astype(jnp.bfloat16).reshape(t_blk, heads, rope)
    lt = scale_factor * lax.dot_general(score_grad, q, tn, preferred_element_type=f32)
    lt = lt + lax.dot_general(rounded, dout, tn, preferred_element_type=f32)
    rt = scale_factor * lax.dot_general(score_grad, qr, tn, preferred_element_type=f32)

    @pl.when(step == 0)
    def _():
        lt_acc[...] = lt
        rt_acc[...] = rt

    @pl.when(step > 0)
    def _():
        lt_acc[...] += lt
        rt_acc[...] += rt

    @pl.when(step == pl.num_programs(0) - 1)
    def _():
        block_len = mine_ref.shape[1]
        n_blocks = lt_acc.shape[0] // block_len
        even = n_blocks % 2 == 0
        side = (offset_ref[0] // block_len) % 2 if even else 0
        for slot in range(mine_ref.shape[0]):
            start = (2 * slot + side) * block_len if even else slot * block_len
            start = pl.multiple_of(start, block_len)
            mine_ref[slot, :, :kvr] = lt_acc[pl.ds(start, block_len), :].astype(jnp.bfloat16)
            mine_ref[slot, :, kvr:] = rt_acc[pl.ds(start, block_len), :].astype(jnp.bfloat16)
        for slot in range(theirs_ref.shape[0]):
            if even:
                start = pl.multiple_of((2 * slot + 1 - side) * block_len, block_len)
                theirs_ref[slot, :, :kvr] = lt_acc[pl.ds(start, block_len), :].astype(jnp.bfloat16)
                theirs_ref[slot, :, kvr:] = rt_acc[pl.ds(start, block_len), :].astype(jnp.bfloat16)
            else:
                theirs_ref[slot] = jnp.zeros(theirs_ref.shape[1:], jnp.bfloat16)


def prep_kernel(kl_ref, kr_ref, qr_ref, keys_ref, qrows_ref):
    kvr = kl_ref.shape[1]
    keys_ref[:, :kvr] = kl_ref[...]
    keys_ref[:, kvr:] = kr_ref[...].astype(jnp.float32).T.astype(jnp.bfloat16)
    for head in range(qr_ref.shape[0]):
        qrows_ref[:, head, :] = qr_ref[head].astype(jnp.float32).T.astype(jnp.bfloat16)


def body(query_latent, query_rope, key_latent, key_rope, output_grad):
    n_ctx = lax.axis_size("ctx")
    n_ep = lax.axis_size("ep")
    _, block_len, heads, kvr = query_latent.shape
    rope = query_rope.shape[2]
    local_keys, qr = pl.pallas_call(
        prep_kernel,
        out_shape=[
            jax.ShapeDtypeStruct((block_len, kvr + rope), jnp.bfloat16),
            jax.ShapeDtypeStruct((block_len, heads, rope), jnp.bfloat16),
        ],
    )(key_latent[0], key_rope[0], query_rope[0])
    whole_keys = lax.all_gather(local_keys, "ctx", axis=0, tiled=True)
    length = whole_keys.shape[0]
    offset = (lax.axis_index("ctx") * block_len).astype(jnp.int32).reshape(1)
    t_blk = max(1, min(block_len, 1024 // heads))
    while block_len % t_blk:
        t_blk -= 1
    by_rows = pl.BlockSpec((t_blk, heads, kvr), lambda i, off: (i, 0, 0))
    rope_rows = pl.BlockSpec((t_blk, heads, rope), lambda i, off: (i, 0, 0))
    fixed = pl.BlockSpec((length, kvr + rope), lambda i, off: (0, 0))
    n_mine = n_ctx // 2 if n_ctx % 2 == 0 else n_ctx
    n_theirs = n_ctx // 2 if n_ctx % 2 == 0 else 1
    mine_blocks = pl.BlockSpec((n_mine, block_len, kvr + rope), lambda i, off: (0, 0, 0))
    their_blocks = pl.BlockSpec((n_theirs, block_len, kvr + rope), lambda i, off: (0, 0, 0))
    att, lqg, rqg, mine, theirs = pl.pallas_call(
        attention_kernel,
        grid_spec=pltpu.PrefetchScalarGridSpec(
            num_scalar_prefetch=1,
            grid=(block_len // t_blk,),
            in_specs=[by_rows, rope_rows, fixed, by_rows],
            out_specs=[by_rows, by_rows, rope_rows, mine_blocks, their_blocks],
            scratch_shapes=[
                pltpu.VMEM((length, kvr), jnp.float32),
                pltpu.VMEM((length, rope), jnp.float32),
            ],
        ),
        out_shape=[
            jax.ShapeDtypeStruct((block_len, heads, kvr), jnp.bfloat16),
            jax.ShapeDtypeStruct((block_len, heads, kvr), jnp.bfloat16),
            jax.ShapeDtypeStruct((block_len, heads, rope), jnp.bfloat16),
            jax.ShapeDtypeStruct((n_mine, block_len, kvr + rope), jnp.bfloat16),
            jax.ShapeDtypeStruct((n_theirs, block_len, kvr + rope), jnp.bfloat16),
        ],
        compiler_params=pltpu.CompilerParams(dimension_semantics=("arbitrary",)),
    )(offset, query_latent[0], qr, whole_keys, output_grad[0])
    attended = att[None]
    latent_qgrad = lqg[None]
    rope_qgrad = jnp.transpose(rqg, (1, 2, 0))[None]
    total = causal_reduce_ctx(mine, theirs, n_ctx)
    total = butterfly_sum_ep(total, n_ctx, n_ep).astype(jnp.bfloat16)
    latent_kgrad = total[None, :, :kvr]
    rope_kgrad = total[:, kvr:].T[None]
    return (attended, latent_qgrad, rope_qgrad, latent_kgrad, rope_kgrad)


def solution(mesh):
    placed = (
        P(None, "ctx", "ep", None),
        P(None, "ep", None, "ctx"),
        P(None, "ctx", None),
        P(None, None, "ctx"),
        P(None, "ctx", "ep", None),
    )
    return jax.shard_map(
        body,
        mesh=mesh,
        in_specs=placed,
        out_specs=(
            P(None, "ctx", "ep", None),
            P(None, "ctx", "ep", None),
            P(None, "ep", None, "ctx"),
            P(None, "ctx", None),
            P(None, None, "ctx"),
        ),
        check_vma=False,
    )
```

```python
import jax
import jax.numpy as jnp
from jax import lax
from jax.experimental import pallas as pl
from jax.experimental.pallas import tpu as pltpu
from jax.sharding import PartitionSpec as P

scale_factor = 192.0 ** (-0.5)


def causal_reduce_ctx(blocks, theirs, n_ctx):
    here = lax.axis_index("ctx")
    if n_ctx % 2:
        total = jnp.take(blocks, here, axis=0).astype(jnp.float32)
        for shift in range(1, n_ctx):
            sent = jnp.take(blocks, jnp.maximum(here - shift, 0), axis=0)
            got = lax.ppermute(sent, "ctx", [(i, i - shift) for i in range(shift, n_ctx)])
            total = total + got.astype(jnp.float32)
        return total
    pairs = n_ctx // 2
    mine = blocks
    got = lax.ppermute(theirs, "ctx", [(i, i ^ 1) for i in range(n_ctx)])
    summed = (mine.astype(jnp.float32) + got.astype(jnp.float32)).astype(jnp.bfloat16)
    total = jnp.take(summed, here // 2, axis=0).astype(jnp.float32)
    for shift in range(1, pairs):
        sent = jnp.take(summed, jnp.maximum(here // 2 - shift, 0), axis=0)
        got = lax.ppermute(sent, "ctx", [(i, i - 2 * shift) for i in range(2 * shift, n_ctx)])
        total = total + got.astype(jnp.float32)
    return total


def butterfly_sum_ep(total, n_ctx, n_ep):
    if n_ep & (n_ep - 1):
        return lax.psum(total.astype(jnp.bfloat16), "ep").astype(jnp.float32)
    bits = [1 << k for k in range(n_ep.bit_length() - 1)]
    orders = [bits, bits[-1:] + bits[:-1]]
    for step in range(len(bits)):
        pairs = [
            (c * n_ep + e, c * n_ep + (e ^ orders[c % 2][step]))
            for c in range(n_ctx)
            for e in range(n_ep)
        ]
        mine = total.astype(jnp.bfloat16)
        theirs = lax.ppermute(mine, ("ctx", "ep"), pairs)
        total = mine.astype(jnp.float32) + theirs.astype(jnp.float32)
    return total


def attention_kernel(offset_ref, ql_ref, qr_ref, keys_ref, do_ref,
                     att_ref, lqg_ref, rqg_ref, mine_ref, theirs_ref, lt_acc, rt_acc):
    step = pl.program_id(0)
    t_blk, heads, kvr = ql_ref.shape
    rope = qr_ref.shape[2]
    rows = t_blk * heads
    f32 = jnp.float32
    nt = (((1,), (1,)), ((), ()))
    tn = (((0,), (0,)), ((), ()))
    q = ql_ref[...].reshape(rows, kvr)
    qr = qr_ref[...].reshape(rows, rope)
    k = keys_ref[:, :kvr]
    kr = keys_ref[:, kvr:]
    dout = do_ref[...].reshape(rows, kvr)
    length = k.shape[0]
    scores = lax.dot_general(q, k, nt, preferred_element_type=f32)
    scores = scores + lax.dot_general(qr, kr, nt, preferred_element_type=f32)
    row = lax.broadcasted_iota(jnp.int32, (rows, 1), 0)
    last_key = offset_ref[0] + step * t_blk + row // heads
    col = lax.broadcasted_iota(jnp.int32, (1, length), 1)
    scores = jnp.where(col <= last_key, scores * scale_factor, f32(-1e30))
    row_max = jnp.max(scores, axis=-1, keepdims=True)
    powers = jnp.exp(scores - row_max)
    weights = powers * (1.0 / jnp.sum(powers, axis=-1, keepdims=True))
    rounded = weights.astype(jnp.bfloat16)
    att = jnp.dot(rounded, k, preferred_element_type=f32).astype(jnp.bfloat16)
    att_ref[...] = att.reshape(t_blk, heads, kvr)
    row_dots = jnp.sum(dout.astype(f32) * att.astype(f32), axis=-1, keepdims=True)
    weight_grad = lax.dot_general(dout, k, nt, preferred_element_type=f32)
    score_grad = (weights * (weight_grad - row_dots)).astype(jnp.bfloat16)
    lqg = scale_factor * jnp.dot(score_grad, k, preferred_element_type=f32)
    lqg_ref[...] = lqg.astype(jnp.bfloat16).reshape(t_blk, heads, kvr)
    rqg = scale_factor * jnp.dot(score_grad, kr, preferred_element_type=f32)
    rqg_ref[...] = rqg.astype(jnp.bfloat16).reshape(t_blk, heads, rope)
    lt = scale_factor * lax.dot_general(score_grad, q, tn, preferred_element_type=f32)
    lt = lt + lax.dot_general(rounded, dout, tn, preferred_element_type=f32)
    rt = scale_factor * lax.dot_general(score_grad, qr, tn, preferred_element_type=f32)

    @pl.when(step == 0)
    def _():
        lt_acc[...] = lt
        rt_acc[...] = rt

    @pl.when(step > 0)
    def _():
        lt_acc[...] += lt
        rt_acc[...] += rt

    @pl.when(step == pl.num_programs(0) - 1)
    def _():
        block_len = mine_ref.shape[1]
        n_blocks = lt_acc.shape[0] // block_len
        even = n_blocks % 2 == 0
        side = (offset_ref[0] // block_len) % 2 if even else 0
        for slot in range(mine_ref.shape[0]):
            start = (2 * slot + side) * block_len if even else slot * block_len
            start = pl.multiple_of(start, block_len)
            mine_ref[slot, :, :kvr] = lt_acc[pl.ds(start, block_len), :].astype(jnp.bfloat16)
            mine_ref[slot, :, kvr:] = rt_acc[pl.ds(start, block_len), :].astype(jnp.bfloat16)
        for slot in range(theirs_ref.shape[0]):
            if even:
                start = pl.multiple_of((2 * slot + 1 - side) * block_len, block_len)
                theirs_ref[slot, :, :kvr] = lt_acc[pl.ds(start, block_len), :].astype(jnp.bfloat16)
                theirs_ref[slot, :, kvr:] = rt_acc[pl.ds(start, block_len), :].astype(jnp.bfloat16)
            else:
                theirs_ref[slot] = jnp.zeros(theirs_ref.shape[1:], jnp.bfloat16)


def body(query_latent, query_rope, key_latent, key_rope, output_grad):
    n_ctx = lax.axis_size("ctx")
    n_ep = lax.axis_size("ep")
    _, block_len, heads, kvr = query_latent.shape
    rope = query_rope.shape[2]
    local_keys = jnp.concatenate([key_latent[0], key_rope[0].T], axis=1)
    whole_keys = lax.all_gather(local_keys, "ctx", axis=0, tiled=True)
    length = whole_keys.shape[0]
    offset = (lax.axis_index("ctx") * block_len).astype(jnp.int32).reshape(1)
    qr = jnp.transpose(query_rope[0], (2, 0, 1))
    t_blk = max(1, min(block_len, 1024 // heads))
    while block_len % t_blk:
        t_blk -= 1
    by_rows = pl.BlockSpec((t_blk, heads, kvr), lambda i, off: (i, 0, 0))
    rope_rows = pl.BlockSpec((t_blk, heads, rope), lambda i, off: (i, 0, 0))
    fixed = pl.BlockSpec((length, kvr + rope), lambda i, off: (0, 0))
    n_mine = n_ctx // 2 if n_ctx % 2 == 0 else n_ctx
    n_theirs = n_ctx // 2 if n_ctx % 2 == 0 else 1
    mine_blocks = pl.BlockSpec((n_mine, block_len, kvr + rope), lambda i, off: (0, 0, 0))
    their_blocks = pl.BlockSpec((n_theirs, block_len, kvr + rope), lambda i, off: (0, 0, 0))
    att, lqg, rqg, mine, theirs = pl.pallas_call(
        attention_kernel,
        grid_spec=pltpu.PrefetchScalarGridSpec(
            num_scalar_prefetch=1,
            grid=(block_len // t_blk,),
            in_specs=[by_rows, rope_rows, fixed, by_rows],
            out_specs=[by_rows, by_rows, rope_rows, mine_blocks, their_blocks],
            scratch_shapes=[
                pltpu.VMEM((length, kvr), jnp.float32),
                pltpu.VMEM((length, rope), jnp.float32),
            ],
        ),
        out_shape=[
            jax.ShapeDtypeStruct((block_len, heads, kvr), jnp.bfloat16),
            jax.ShapeDtypeStruct((block_len, heads, kvr), jnp.bfloat16),
            jax.ShapeDtypeStruct((block_len, heads, rope), jnp.bfloat16),
            jax.ShapeDtypeStruct((n_mine, block_len, kvr + rope), jnp.bfloat16),
            jax.ShapeDtypeStruct((n_theirs, block_len, kvr + rope), jnp.bfloat16),
        ],
        compiler_params=pltpu.CompilerParams(dimension_semantics=("arbitrary",)),
    )(offset, query_latent[0], qr, whole_keys, output_grad[0])
    attended = att[None]
    latent_qgrad = lqg[None]
    rope_qgrad = jnp.transpose(rqg, (1, 2, 0))[None]
    total = causal_reduce_ctx(mine, theirs, n_ctx)
    total = butterfly_sum_ep(total, n_ctx, n_ep).astype(jnp.bfloat16)
    latent_kgrad = total[None, :, :kvr]
    rope_kgrad = total[:, kvr:].T[None]
    return (attended, latent_qgrad, rope_qgrad, latent_kgrad, rope_kgrad)


def solution(mesh):
    placed = (
        P(None, "ctx", "ep", None),
        P(None, "ep", None, "ctx"),
        P(None, "ctx", None),
        P(None, None, "ctx"),
        P(None, "ctx", "ep", None),
    )
    return jax.shard_map(
        body,
        mesh=mesh,
        in_specs=placed,
        out_specs=(
            P(None, "ctx", "ep", None),
            P(None, "ctx", "ep", None),
            P(None, "ep", None, "ctx"),
            P(None, "ctx", None),
            P(None, None, "ctx"),
        ),
        check_vma=False,
    )
```

```python
import jax
import jax.numpy as jnp
from jax import lax
from jax.experimental import pallas as pl
from jax.experimental.pallas import tpu as pltpu
from jax.sharding import PartitionSpec as P

scale_factor = 192.0 ** (-0.5)


def causal_reduce_ctx(blocks, theirs, n_ctx):
    here = lax.axis_index("ctx")
    if n_ctx % 2:
        total = jnp.take(blocks, here, axis=0).astype(jnp.float32)
        for shift in range(1, n_ctx):
            sent = jnp.take(blocks, jnp.maximum(here - shift, 0), axis=0)
            got = lax.ppermute(sent, "ctx", [(i, i - shift) for i in range(shift, n_ctx)])
            total = total + got.astype(jnp.float32)
        return total
    pairs = n_ctx // 2
    mine = blocks
    got = lax.ppermute(theirs, "ctx", [(i, i ^ 1) for i in range(n_ctx)])

    def pair_sum(slot):
        both = jnp.take(mine, slot, axis=0).astype(jnp.float32) + jnp.take(got, slot, axis=0).astype(jnp.float32)
        return both.astype(jnp.bfloat16)

    total = pair_sum(here // 2).astype(jnp.float32)
    for shift in range(1, pairs):
        sent = pair_sum(jnp.maximum(here // 2 - shift, 0))
        got = lax.ppermute(sent, "ctx", [(i, i - 2 * shift) for i in range(2 * shift, n_ctx)])
        total = total + got.astype(jnp.float32)
    return total


def butterfly_sum_ep(total, n_ctx, n_ep):
    if n_ep & (n_ep - 1):
        return lax.psum(total.astype(jnp.bfloat16), "ep").astype(jnp.float32)
    bits = [1 << k for k in range(n_ep.bit_length() - 1)]
    orders = [bits, bits[-1:] + bits[:-1]]
    for step in range(len(bits)):
        pairs = [
            (c * n_ep + e, c * n_ep + (e ^ orders[c % 2][step]))
            for c in range(n_ctx)
            for e in range(n_ep)
        ]
        mine = total.astype(jnp.bfloat16)
        theirs = lax.ppermute(mine, ("ctx", "ep"), pairs)
        total = mine.astype(jnp.float32) + theirs.astype(jnp.float32)
    return total


def attention_kernel(offset_ref, ql_ref, qr_ref, keys_ref, do_ref,
                     att_ref, lqg_ref, rqg_ref, mine_ref, theirs_ref, lt_acc, rt_acc):
    step = pl.program_id(0)
    t_blk, heads, kvr = ql_ref.shape
    rope = qr_ref.shape[2]
    rows = t_blk * heads
    f32 = jnp.float32
    nt = (((1,), (1,)), ((), ()))
    tn = (((0,), (0,)), ((), ()))
    q = ql_ref[...].reshape(rows, kvr)
    qr = qr_ref[...].reshape(rows, rope)
    k = keys_ref[:, :kvr]
    kr = keys_ref[:, kvr:]
    dout = do_ref[...].reshape(rows, kvr)
    length = k.shape[0]
    scores = lax.dot_general(q, k, nt, preferred_element_type=f32)
    scores = scores + lax.dot_general(qr, kr, nt, preferred_element_type=f32)
    row = lax.broadcasted_iota(jnp.int32, (rows, 1), 0)
    last_key = offset_ref[0] + step * t_blk + row // heads
    col = lax.broadcasted_iota(jnp.int32, (1, length), 1)
    scores = jnp.where(col <= last_key, scores * scale_factor, f32(-1e30))
    row_max = jnp.max(scores, axis=-1, keepdims=True)
    powers = jnp.exp(scores - row_max)
    weights = powers * (1.0 / jnp.sum(powers, axis=-1, keepdims=True))
    rounded = weights.astype(jnp.bfloat16)
    att = jnp.dot(rounded, k, preferred_element_type=f32).astype(jnp.bfloat16)
    att_ref[...] = att.reshape(t_blk, heads, kvr)
    row_dots = jnp.sum(dout.astype(f32) * att.astype(f32), axis=-1, keepdims=True)
    weight_grad = lax.dot_general(dout, k, nt, preferred_element_type=f32)
    score_grad = (weights * (weight_grad - row_dots)).astype(jnp.bfloat16)
    lqg = scale_factor * jnp.dot(score_grad, k, preferred_element_type=f32)
    lqg_ref[...] = lqg.astype(jnp.bfloat16).reshape(t_blk, heads, kvr)
    rqg = scale_factor * jnp.dot(score_grad, kr, preferred_element_type=f32)
    rqg_ref[...] = rqg.astype(jnp.bfloat16).reshape(t_blk, heads, rope)
    lt = scale_factor * lax.dot_general(score_grad, q, tn, preferred_element_type=f32)
    lt = lt + lax.dot_general(rounded, dout, tn, preferred_element_type=f32)
    rt = scale_factor * lax.dot_general(score_grad, qr, tn, preferred_element_type=f32)

    @pl.when(step == 0)
    def _():
        lt_acc[...] = lt
        rt_acc[...] = rt

    @pl.when(step > 0)
    def _():
        lt_acc[...] += lt
        rt_acc[...] += rt

    @pl.when(step == pl.num_programs(0) - 1)
    def _():
        block_len = mine_ref.shape[1]
        n_blocks = lt_acc.shape[0] // block_len
        even = n_blocks % 2 == 0
        side = (offset_ref[0] // block_len) % 2 if even else 0
        for slot in range(mine_ref.shape[0]):
            start = (2 * slot + side) * block_len if even else slot * block_len
            start = pl.multiple_of(start, block_len)
            mine_ref[slot, :, :kvr] = lt_acc[pl.ds(start, block_len), :].astype(jnp.bfloat16)
            mine_ref[slot, :, kvr:] = rt_acc[pl.ds(start, block_len), :].astype(jnp.bfloat16)
        for slot in range(theirs_ref.shape[0]):
            if even:
                start = pl.multiple_of((2 * slot + 1 - side) * block_len, block_len)
                theirs_ref[slot, :, :kvr] = lt_acc[pl.ds(start, block_len), :].astype(jnp.bfloat16)
                theirs_ref[slot, :, kvr:] = rt_acc[pl.ds(start, block_len), :].astype(jnp.bfloat16)
            else:
                theirs_ref[slot] = jnp.zeros(theirs_ref.shape[1:], jnp.bfloat16)


def body(query_latent, query_rope, key_latent, key_rope, output_grad):
    n_ctx = lax.axis_size("ctx")
    n_ep = lax.axis_size("ep")
    _, block_len, heads, kvr = query_latent.shape
    rope = query_rope.shape[2]
    local_keys = jnp.concatenate([key_latent[0], key_rope[0].T], axis=1)
    whole_keys = lax.all_gather(local_keys, "ctx", axis=0, tiled=True)
    length = whole_keys.shape[0]
    offset = (lax.axis_index("ctx") * block_len).astype(jnp.int32).reshape(1)
    qr = jnp.transpose(query_rope[0], (2, 0, 1))
    t_blk = max(1, min(block_len, 1024 // heads))
    while block_len % t_blk:
        t_blk -= 1
    by_rows = pl.BlockSpec((t_blk, heads, kvr), lambda i, off: (i, 0, 0))
    rope_rows = pl.BlockSpec((t_blk, heads, rope), lambda i, off: (i, 0, 0))
    fixed = pl.BlockSpec((length, kvr + rope), lambda i, off: (0, 0))
    n_mine = n_ctx // 2 if n_ctx % 2 == 0 else n_ctx
    n_theirs = n_ctx // 2 if n_ctx % 2 == 0 else 1
    mine_blocks = pl.BlockSpec((n_mine, block_len, kvr + rope), lambda i, off: (0, 0, 0))
    their_blocks = pl.BlockSpec((n_theirs, block_len, kvr + rope), lambda i, off: (0, 0, 0))
    att, lqg, rqg, mine, theirs = pl.pallas_call(
        attention_kernel,
        grid_spec=pltpu.PrefetchScalarGridSpec(
            num_scalar_prefetch=1,
            grid=(block_len // t_blk,),
            in_specs=[by_rows, rope_rows, fixed, by_rows],
            out_specs=[by_rows, by_rows, rope_rows, mine_blocks, their_blocks],
            scratch_shapes=[
                pltpu.VMEM((length, kvr), jnp.float32),
                pltpu.VMEM((length, rope), jnp.float32),
            ],
        ),
        out_shape=[
            jax.ShapeDtypeStruct((block_len, heads, kvr), jnp.bfloat16),
            jax.ShapeDtypeStruct((block_len, heads, kvr), jnp.bfloat16),
            jax.ShapeDtypeStruct((block_len, heads, rope), jnp.bfloat16),
            jax.ShapeDtypeStruct((n_mine, block_len, kvr + rope), jnp.bfloat16),
            jax.ShapeDtypeStruct((n_theirs, block_len, kvr + rope), jnp.bfloat16),
        ],
        compiler_params=pltpu.CompilerParams(dimension_semantics=("arbitrary",)),
    )(offset, query_latent[0], qr, whole_keys, output_grad[0])
    attended = att[None]
    latent_qgrad = lqg[None]
    rope_qgrad = jnp.transpose(rqg, (1, 2, 0))[None]
    total = causal_reduce_ctx(mine, theirs, n_ctx)
    total = butterfly_sum_ep(total, n_ctx, n_ep)
    latent_kgrad = total[None, :, :kvr].astype(jnp.bfloat16)
    rope_kgrad = total[:, kvr:].T[None].astype(jnp.bfloat16)
    return (attended, latent_qgrad, rope_qgrad, latent_kgrad, rope_kgrad)


def solution(mesh):
    placed = (
        P(None, "ctx", "ep", None),
        P(None, "ep", None, "ctx"),
        P(None, "ctx", None),
        P(None, None, "ctx"),
        P(None, "ctx", "ep", None),
    )
    return jax.shard_map(
        body,
        mesh=mesh,
        in_specs=placed,
        out_specs=(
            P(None, "ctx", "ep", None),
            P(None, "ctx", "ep", None),
            P(None, "ep", None, "ctx"),
            P(None, "ctx", None),
            P(None, None, "ctx"),
        ),
        check_vma=False,
    )
```

```python
import jax
import jax.numpy as jnp
from jax import lax
from jax.experimental import pallas as pl
from jax.experimental.pallas import tpu as pltpu
from jax.sharding import PartitionSpec as P

scale_factor = 192.0 ** (-0.5)


def causal_reduce_ctx(blocks, theirs, n_ctx):
    here = lax.axis_index("ctx")
    if n_ctx % 2:
        total = jnp.take(blocks, here, axis=0).astype(jnp.float32)
        for shift in range(1, n_ctx):
            sent = jnp.take(blocks, jnp.maximum(here - shift, 0), axis=0)
            got = lax.ppermute(sent, "ctx", [(i, i - shift) for i in range(shift, n_ctx)])
            total = total + got.astype(jnp.float32)
        return total
    pairs = n_ctx // 2
    mine = blocks
    got = lax.ppermute(theirs, "ctx", [(i, i ^ 1) for i in range(n_ctx)])
    summed = (mine.astype(jnp.float32) + got.astype(jnp.float32)).astype(jnp.bfloat16)
    total = jnp.take(summed, here // 2, axis=0).astype(jnp.float32)
    for shift in range(1, pairs):
        sent = jnp.take(summed, jnp.maximum(here // 2 - shift, 0), axis=0)
        got = lax.ppermute(sent, "ctx", [(i, i - 2 * shift) for i in range(2 * shift, n_ctx)])
        total = total + got.astype(jnp.float32)
    return total


def butterfly_sum_ep(total, n_ctx, n_ep):
    if n_ep & (n_ep - 1):
        return lax.psum(total.astype(jnp.bfloat16), "ep").astype(jnp.float32)
    bits = [1 << k for k in range(n_ep.bit_length() - 1)]
    orders = [bits, bits[-1:] + bits[:-1]]
    for step in range(len(bits)):
        pairs = [
            (c * n_ep + e, c * n_ep + (e ^ orders[c % 2][step]))
            for c in range(n_ctx)
            for e in range(n_ep)
        ]
        mine = total.astype(jnp.bfloat16)
        theirs = lax.ppermute(mine, ("ctx", "ep"), pairs)
        total = mine.astype(jnp.float32) + theirs.astype(jnp.float32)
    return total


def attention_kernel(offset_ref, ql_ref, qr_ref, keys_ref, do_ref,
                     att_ref, lqg_ref, rqg_ref, mine_ref, theirs_ref, lt_acc, rt_acc):
    step = pl.program_id(0)
    t_blk, heads, kvr = ql_ref.shape
    rope = qr_ref.shape[2]
    f32 = jnp.float32
    nt = (((1,), (1,)), ((), ()))
    tn = (((0,), (0,)), ((), ()))
    k = keys_ref[:, :kvr]
    kr = keys_ref[:, kvr:]
    length = k.shape[0]
    n_sub = 2 if t_blk % 2 == 0 else 1
    t_sub = t_blk // n_sub
    rows = t_sub * heads
    lt = None
    for sub in range(n_sub):
        part = pl.ds(sub * t_sub, t_sub)
        q = ql_ref[part].reshape(rows, kvr)
        qr = qr_ref[part].reshape(rows, rope)
        dout = do_ref[part].reshape(rows, kvr)
        scores = lax.dot_general(q, k, nt, preferred_element_type=f32)
        scores = scores + lax.dot_general(qr, kr, nt, preferred_element_type=f32)
        row = lax.broadcasted_iota(jnp.int32, (rows, 1), 0)
        last_key = offset_ref[0] + step * t_blk + sub * t_sub + row // heads
        col = lax.broadcasted_iota(jnp.int32, (1, length), 1)
        scores = jnp.where(col <= last_key, scores * scale_factor, f32(-1e30))
        row_max = jnp.max(scores, axis=-1, keepdims=True)
        powers = jnp.exp(scores - row_max)
        weights = powers * (1.0 / jnp.sum(powers, axis=-1, keepdims=True))
        rounded = weights.astype(jnp.bfloat16)
        att = jnp.dot(rounded, k, preferred_element_type=f32).astype(jnp.bfloat16)
        att_ref[part] = att.reshape(t_sub, heads, kvr)
        row_dots = jnp.sum(dout.astype(f32) * att.astype(f32), axis=-1, keepdims=True)
        weight_grad = lax.dot_general(dout, k, nt, preferred_element_type=f32)
        score_grad = (weights * (weight_grad - row_dots)).astype(jnp.bfloat16)
        lqg = scale_factor * jnp.dot(score_grad, k, preferred_element_type=f32)
        lqg_ref[part] = lqg.astype(jnp.bfloat16).reshape(t_sub, heads, kvr)
        rqg = scale_factor * jnp.dot(score_grad, kr, preferred_element_type=f32)
        rqg_ref[part] = rqg.astype(jnp.bfloat16).reshape(t_sub, heads, rope)
        lt_part = scale_factor * lax.dot_general(score_grad, q, tn, preferred_element_type=f32)
        lt_part = lt_part + lax.dot_general(rounded, dout, tn, preferred_element_type=f32)
        rt_part = scale_factor * lax.dot_general(score_grad, qr, tn, preferred_element_type=f32)
        lt = lt_part if lt is None else lt + lt_part
        rt = rt_part if sub == 0 else rt + rt_part

    @pl.when(step == 0)
    def _():
        lt_acc[...] = lt
        rt_acc[...] = rt

    @pl.when(step > 0)
    def _():
        lt_acc[...] += lt
        rt_acc[...] += rt


    @pl.when(step == pl.num_programs(0) - 1)
    def _():
        block_len = mine_ref.shape[1]
        n_blocks = lt_acc.shape[0] // block_len
        even = n_blocks % 2 == 0
        side = (offset_ref[0] // block_len) % 2 if even else 0
        for slot in range(mine_ref.shape[0]):
            start = (2 * slot + side) * block_len if even else slot * block_len
            start = pl.multiple_of(start, block_len)
            mine_ref[slot, :, :kvr] = lt_acc[pl.ds(start, block_len), :].astype(jnp.bfloat16)
            mine_ref[slot, :, kvr:] = rt_acc[pl.ds(start, block_len), :].astype(jnp.bfloat16)
        for slot in range(theirs_ref.shape[0]):
            if even:
                start = pl.multiple_of((2 * slot + 1 - side) * block_len, block_len)
                theirs_ref[slot, :, :kvr] = lt_acc[pl.ds(start, block_len), :].astype(jnp.bfloat16)
                theirs_ref[slot, :, kvr:] = rt_acc[pl.ds(start, block_len), :].astype(jnp.bfloat16)
            else:
                theirs_ref[slot] = jnp.zeros(theirs_ref.shape[1:], jnp.bfloat16)


def body(query_latent, query_rope, key_latent, key_rope, output_grad):
    n_ctx = lax.axis_size("ctx")
    n_ep = lax.axis_size("ep")
    _, block_len, heads, kvr = query_latent.shape
    rope = query_rope.shape[2]
    local_keys = jnp.concatenate([key_latent[0], key_rope[0].T], axis=1)
    whole_keys = lax.all_gather(local_keys, "ctx", axis=0, tiled=True)
    length = whole_keys.shape[0]
    offset = (lax.axis_index("ctx") * block_len).astype(jnp.int32).reshape(1)
    qr = jnp.transpose(query_rope[0], (2, 0, 1))
    t_blk = max(1, min(block_len, 1024 // heads))
    while block_len % t_blk:
        t_blk -= 1
    by_rows = pl.BlockSpec((t_blk, heads, kvr), lambda i, off: (i, 0, 0))
    rope_rows = pl.BlockSpec((t_blk, heads, rope), lambda i, off: (i, 0, 0))
    fixed = pl.BlockSpec((length, kvr + rope), lambda i, off: (0, 0))
    n_mine = n_ctx // 2 if n_ctx % 2 == 0 else n_ctx
    n_theirs = n_ctx // 2 if n_ctx % 2 == 0 else 1
    mine_blocks = pl.BlockSpec((n_mine, block_len, kvr + rope), lambda i, off: (0, 0, 0))
    their_blocks = pl.BlockSpec((n_theirs, block_len, kvr + rope), lambda i, off: (0, 0, 0))
    att, lqg, rqg, mine, theirs = pl.pallas_call(
        attention_kernel,
        grid_spec=pltpu.PrefetchScalarGridSpec(
            num_scalar_prefetch=1,
            grid=(block_len // t_blk,),
            in_specs=[by_rows, rope_rows, fixed, by_rows],
            out_specs=[by_rows, by_rows, rope_rows, mine_blocks, their_blocks],
            scratch_shapes=[
                pltpu.VMEM((length, kvr), jnp.float32),
                pltpu.VMEM((length, rope), jnp.float32),
            ],
        ),
        out_shape=[
            jax.ShapeDtypeStruct((block_len, heads, kvr), jnp.bfloat16),
            jax.ShapeDtypeStruct((block_len, heads, kvr), jnp.bfloat16),
            jax.ShapeDtypeStruct((block_len, heads, rope), jnp.bfloat16),
            jax.ShapeDtypeStruct((n_mine, block_len, kvr + rope), jnp.bfloat16),
            jax.ShapeDtypeStruct((n_theirs, block_len, kvr + rope), jnp.bfloat16),
        ],
        compiler_params=pltpu.CompilerParams(dimension_semantics=("arbitrary",)),
    )(offset, query_latent[0], qr, whole_keys, output_grad[0])
    attended = att[None]
    latent_qgrad = lqg[None]
    rope_qgrad = jnp.transpose(rqg, (1, 2, 0))[None]
    total = causal_reduce_ctx(mine, theirs, n_ctx)
    total = butterfly_sum_ep(total, n_ctx, n_ep).astype(jnp.bfloat16)
    latent_kgrad = total[None, :, :kvr]
    rope_kgrad = total[:, kvr:].T[None]
    return (attended, latent_qgrad, rope_qgrad, latent_kgrad, rope_kgrad)


def solution(mesh):
    placed = (
        P(None, "ctx", "ep", None),
        P(None, "ep", None, "ctx"),
        P(None, "ctx", None),
        P(None, None, "ctx"),
        P(None, "ctx", "ep", None),
    )
    return jax.shard_map(
        body,
        mesh=mesh,
        in_specs=placed,
        out_specs=(
            P(None, "ctx", "ep", None),
            P(None, "ctx", "ep", None),
            P(None, "ep", None, "ctx"),
            P(None, "ctx", None),
            P(None, None, "ctx"),
        ),
        check_vma=False,
    )
```

```python
import jax
import jax.numpy as jnp
from jax import lax
from jax.experimental import pallas as pl
from jax.experimental.pallas import tpu as pltpu
from jax.sharding import PartitionSpec as P

scale_factor = 192.0 ** (-0.5)


def causal_reduce_ctx(blocks, theirs, n_ctx):
    here = lax.axis_index("ctx")
    if n_ctx % 2:
        total = jnp.take(blocks, here, axis=0).astype(jnp.float32)
        for shift in range(1, n_ctx):
            sent = jnp.take(blocks, jnp.maximum(here - shift, 0), axis=0)
            got = lax.ppermute(sent, "ctx", [(i, i - shift) for i in range(shift, n_ctx)])
            total = total + got.astype(jnp.float32)
        return total
    pairs = n_ctx // 2
    mine = blocks
    got = lax.ppermute(theirs, "ctx", [(i, i ^ 1) for i in range(n_ctx)])
    summed = (mine.astype(jnp.float32) + got.astype(jnp.float32)).astype(jnp.bfloat16)
    total = jnp.take(summed, here // 2, axis=0).astype(jnp.float32)
    for shift in range(1, pairs):
        sent = jnp.take(summed, jnp.maximum(here // 2 - shift, 0), axis=0)
        got = lax.ppermute(sent, "ctx", [(i, i - 2 * shift) for i in range(2 * shift, n_ctx)])
        total = total + got.astype(jnp.float32)
    return total


def causal_gather_ctx(local, n_ctx):
    if n_ctx % 2:
        return lax.all_gather(local, "ctx", axis=0, tiled=True)
    here = lax.axis_index("ctx")
    partner = here + 1 - 2 * (here % 2)
    pairs = n_ctx // 2
    cross = [
        lax.ppermute(local, "ctx", [(i, i + 2 * s) for i in range(n_ctx - 2 * s)])
        for s in range(1, pairs)
    ]
    on_chip = lax.ppermute(local, "ctx", [(2 * p, 2 * p + 1) for p in range(pairs)])
    if cross:
        swapped = lax.ppermute(jnp.stack(cross), "ctx", [(i, i ^ 1) for i in range(n_ctx)])
    zero = jnp.zeros_like(local)
    slots = []
    for m in range(n_ctx):
        piece = jnp.where(m == here, local, zero)
        piece = jnp.where((here % 2 == 1) & (m == here - 1), on_chip, piece)
        for s in range(1, pairs):
            piece = jnp.where(m == here - 2 * s, cross[s - 1], piece)
            piece = jnp.where(m == partner - 2 * s, swapped[s - 1], piece)
        slots.append(piece)
    return jnp.concatenate(slots, axis=0)


def butterfly_sum_ep(total, n_ctx, n_ep):
    if n_ep & (n_ep - 1):
        return lax.psum(total.astype(jnp.bfloat16), "ep").astype(jnp.float32)
    bits = [1 << k for k in range(n_ep.bit_length() - 1)]
    orders = [bits, bits[-1:] + bits[:-1]]
    for step in range(len(bits)):
        pairs = [
            (c * n_ep + e, c * n_ep + (e ^ orders[c % 2][step]))
            for c in range(n_ctx)
            for e in range(n_ep)
        ]
        mine = total.astype(jnp.bfloat16)
        theirs = lax.ppermute(mine, ("ctx", "ep"), pairs)
        total = mine.astype(jnp.float32) + theirs.astype(jnp.float32)
    return total


def attention_kernel(offset_ref, ql_ref, qr_ref, keys_ref, do_ref,
                     att_ref, lqg_ref, rqg_ref, mine_ref, theirs_ref, lt_acc, rt_acc):
    step = pl.program_id(0)
    t_blk, heads, kvr = ql_ref.shape
    rope = qr_ref.shape[2]
    rows = t_blk * heads
    f32 = jnp.float32
    nt = (((1,), (1,)), ((), ()))
    tn = (((0,), (0,)), ((), ()))
    q = ql_ref[...].reshape(rows, kvr)
    qr = qr_ref[...].reshape(rows, rope)
    k = keys_ref[:, :kvr]
    kr = keys_ref[:, kvr:]
    dout = do_ref[...].reshape(rows, kvr)
    length = k.shape[0]
    scores = lax.dot_general(q, k, nt, preferred_element_type=f32)
    scores = scores + lax.dot_general(qr, kr, nt, preferred_element_type=f32)
    row = lax.broadcasted_iota(jnp.int32, (rows, 1), 0)
    last_key = offset_ref[0] + step * t_blk + row // heads
    col = lax.broadcasted_iota(jnp.int32, (1, length), 1)
    scores = jnp.where(col <= last_key, scores * scale_factor, f32(-1e30))
    row_max = jnp.max(scores, axis=-1, keepdims=True)
    powers = jnp.exp(scores - row_max)
    weights = powers * (1.0 / jnp.sum(powers, axis=-1, keepdims=True))
    rounded = weights.astype(jnp.bfloat16)
    att = jnp.dot(rounded, k, preferred_element_type=f32).astype(jnp.bfloat16)
    att_ref[...] = att.reshape(t_blk, heads, kvr)
    row_dots = jnp.sum(dout.astype(f32) * att.astype(f32), axis=-1, keepdims=True)
    weight_grad = lax.dot_general(dout, k, nt, preferred_element_type=f32)
    score_grad = (weights * (weight_grad - row_dots)).astype(jnp.bfloat16)
    lqg = scale_factor * jnp.dot(score_grad, k, preferred_element_type=f32)
    lqg_ref[...] = lqg.astype(jnp.bfloat16).reshape(t_blk, heads, kvr)
    rqg = scale_factor * jnp.dot(score_grad, kr, preferred_element_type=f32)
    rqg_ref[...] = rqg.astype(jnp.bfloat16).reshape(t_blk, heads, rope)
    lt = scale_factor * lax.dot_general(score_grad, q, tn, preferred_element_type=f32)
    lt = lt + lax.dot_general(rounded, dout, tn, preferred_element_type=f32)
    rt = scale_factor * lax.dot_general(score_grad, qr, tn, preferred_element_type=f32)

    @pl.when(step == 0)
    def _():
        lt_acc[...] = lt
        rt_acc[...] = rt

    @pl.when(step > 0)
    def _():
        lt_acc[...] += lt
        rt_acc[...] += rt

    @pl.when(step == pl.num_programs(0) - 1)
    def _():
        block_len = mine_ref.shape[1]
        n_blocks = lt_acc.shape[0] // block_len
        even = n_blocks % 2 == 0
        side = (offset_ref[0] // block_len) % 2 if even else 0
        for slot in range(mine_ref.shape[0]):
            start = (2 * slot + side) * block_len if even else slot * block_len
            start = pl.multiple_of(start, block_len)
            mine_ref[slot, :, :kvr] = lt_acc[pl.ds(start, block_len), :].astype(jnp.bfloat16)
            mine_ref[slot, :, kvr:] = rt_acc[pl.ds(start, block_len), :].astype(jnp.bfloat16)
        for slot in range(theirs_ref.shape[0]):
            if even:
                start = pl.multiple_of((2 * slot + 1 - side) * block_len, block_len)
                theirs_ref[slot, :, :kvr] = lt_acc[pl.ds(start, block_len), :].astype(jnp.bfloat16)
                theirs_ref[slot, :, kvr:] = rt_acc[pl.ds(start, block_len), :].astype(jnp.bfloat16)
            else:
                theirs_ref[slot] = jnp.zeros(theirs_ref.shape[1:], jnp.bfloat16)


def body(query_latent, query_rope, key_latent, key_rope, output_grad):
    n_ctx = lax.axis_size("ctx")
    n_ep = lax.axis_size("ep")
    _, block_len, heads, kvr = query_latent.shape
    rope = query_rope.shape[2]
    local_keys = jnp.concatenate([key_latent[0], key_rope[0].T], axis=1)
    whole_keys = causal_gather_ctx(local_keys, n_ctx)
    length = whole_keys.shape[0]
    offset = (lax.axis_index("ctx") * block_len).astype(jnp.int32).reshape(1)
    qr = jnp.transpose(query_rope[0], (2, 0, 1))
    t_blk = max(1, min(block_len, 1024 // heads))
    while block_len % t_blk:
        t_blk -= 1
    by_rows = pl.BlockSpec((t_blk, heads, kvr), lambda i, off: (i, 0, 0))
    rope_rows = pl.BlockSpec((t_blk, heads, rope), lambda i, off: (i, 0, 0))
    fixed = pl.BlockSpec((length, kvr + rope), lambda i, off: (0, 0))
    n_mine = n_ctx // 2 if n_ctx % 2 == 0 else n_ctx
    n_theirs = n_ctx // 2 if n_ctx % 2 == 0 else 1
    mine_blocks = pl.BlockSpec((n_mine, block_len, kvr + rope), lambda i, off: (0, 0, 0))
    their_blocks = pl.BlockSpec((n_theirs, block_len, kvr + rope), lambda i, off: (0, 0, 0))
    att, lqg, rqg, mine, theirs = pl.pallas_call(
        attention_kernel,
        grid_spec=pltpu.PrefetchScalarGridSpec(
            num_scalar_prefetch=1,
            grid=(block_len // t_blk,),
            in_specs=[by_rows, rope_rows, fixed, by_rows],
            out_specs=[by_rows, by_rows, rope_rows, mine_blocks, their_blocks],
            scratch_shapes=[
                pltpu.VMEM((length, kvr), jnp.float32),
                pltpu.VMEM((length, rope), jnp.float32),
            ],
        ),
        out_shape=[
            jax.ShapeDtypeStruct((block_len, heads, kvr), jnp.bfloat16),
            jax.ShapeDtypeStruct((block_len, heads, kvr), jnp.bfloat16),
            jax.ShapeDtypeStruct((block_len, heads, rope), jnp.bfloat16),
            jax.ShapeDtypeStruct((n_mine, block_len, kvr + rope), jnp.bfloat16),
            jax.ShapeDtypeStruct((n_theirs, block_len, kvr + rope), jnp.bfloat16),
        ],
        compiler_params=pltpu.CompilerParams(dimension_semantics=("arbitrary",)),
    )(offset, query_latent[0], qr, whole_keys, output_grad[0])
    attended = att[None]
    latent_qgrad = lqg[None]
    rope_qgrad = jnp.transpose(rqg, (1, 2, 0))[None]
    total = causal_reduce_ctx(mine, theirs, n_ctx)
    total = butterfly_sum_ep(total, n_ctx, n_ep).astype(jnp.bfloat16)
    latent_kgrad = total[None, :, :kvr]
    rope_kgrad = total[:, kvr:].T[None]
    return (attended, latent_qgrad, rope_qgrad, latent_kgrad, rope_kgrad)


def solution(mesh):
    placed = (
        P(None, "ctx", "ep", None),
        P(None, "ep", None, "ctx"),
        P(None, "ctx", None),
        P(None, None, "ctx"),
        P(None, "ctx", "ep", None),
    )
    return jax.shard_map(
        body,
        mesh=mesh,
        in_specs=placed,
        out_specs=(
            P(None, "ctx", "ep", None),
            P(None, "ctx", "ep", None),
            P(None, "ep", None, "ctx"),
            P(None, "ctx", None),
            P(None, None, "ctx"),
        ),
        check_vma=False,
    )
```

```python
import jax
import jax.numpy as jnp
from jax import lax
from jax.experimental import pallas as pl
from jax.experimental.pallas import tpu as pltpu
from jax.sharding import PartitionSpec as P

scale_factor = 192.0 ** (-0.5)


def causal_reduce_ctx(blocks, theirs, n_ctx):
    here = lax.axis_index("ctx")
    if n_ctx % 2:
        total = jnp.take(blocks, here, axis=0).astype(jnp.float32)
        for shift in range(1, n_ctx):
            sent = jnp.take(blocks, jnp.maximum(here - shift, 0), axis=0)
            got = lax.ppermute(sent, "ctx", [(i, i - shift) for i in range(shift, n_ctx)])
            total = total + got.astype(jnp.float32)
        return total
    pairs = n_ctx // 2
    mine = blocks
    got = lax.ppermute(theirs, "ctx", [(i, i ^ 1) for i in range(n_ctx)])
    summed = (mine.astype(jnp.float32) + got.astype(jnp.float32)).astype(jnp.bfloat16)
    total = jnp.take(summed, here // 2, axis=0).astype(jnp.float32)
    for shift in range(1, pairs):
        sent = jnp.take(summed, jnp.maximum(here // 2 - shift, 0), axis=0)
        got = lax.ppermute(sent, "ctx", [(i, i - 2 * shift) for i in range(2 * shift, n_ctx)])
        total = total + got.astype(jnp.float32)
    return total


def butterfly_sum_ep(total, n_ctx, n_ep):
    if n_ep & (n_ep - 1):
        return lax.psum(total.astype(jnp.bfloat16), "ep").astype(jnp.float32)
    bits = [1 << k for k in range(n_ep.bit_length() - 1)]
    orders = [bits, bits[-1:] + bits[:-1]]
    for step in range(len(bits)):
        pairs = [
            (c * n_ep + e, c * n_ep + (e ^ orders[c % 2][step]))
            for c in range(n_ctx)
            for e in range(n_ep)
        ]
        mine = total.astype(jnp.bfloat16)
        theirs = lax.ppermute(mine, ("ctx", "ep"), pairs)
        total = mine.astype(jnp.float32) + theirs.astype(jnp.float32)
    return total


def attention_kernel(offset_ref, ql_ref, qr_ref, keys_ref, do_ref,
                     att_ref, lqg_ref, rqg_ref, mine_ref, theirs_ref, lt_acc, rt_acc):
    step = pl.program_id(0)
    t_blk, heads, kvr = ql_ref.shape
    rope = qr_ref.shape[2]
    rows = t_blk * heads
    f32 = jnp.float32
    nt = (((1,), (1,)), ((), ()))
    tn = (((0,), (0,)), ((), ()))
    q = ql_ref[...].reshape(rows, kvr)
    qr = qr_ref[...].reshape(rows, rope)
    k = keys_ref[:, :kvr]
    kr = keys_ref[:, kvr:]
    dout = do_ref[...].reshape(rows, kvr)
    length = k.shape[0]
    scores = lax.dot_general(q, k, nt, preferred_element_type=f32)
    scores = scores + lax.dot_general(qr, kr, nt, preferred_element_type=f32)
    row = lax.broadcasted_iota(jnp.int32, (rows, 1), 0)
    last_key = offset_ref[0] + step * t_blk + row // heads
    col = lax.broadcasted_iota(jnp.int32, (1, length), 1)
    scores = jnp.where(col <= last_key, scores * scale_factor, f32(-1e30))
    row_max = jnp.max(scores, axis=-1, keepdims=True)
    powers = jnp.exp(scores - row_max)
    weights = powers * (1.0 / jnp.sum(powers, axis=-1, keepdims=True))
    rounded = weights.astype(jnp.bfloat16)
    att = jnp.dot(rounded, k, preferred_element_type=f32).astype(jnp.bfloat16)
    att_ref[...] = att.reshape(t_blk, heads, kvr)
    row_dots = jnp.sum(dout.astype(f32) * att.astype(f32), axis=-1, keepdims=True)
    weight_grad = lax.dot_general(dout, k, nt, preferred_element_type=f32)
    score_grad = (weights * (weight_grad - row_dots)).astype(jnp.bfloat16)
    lqg = scale_factor * jnp.dot(score_grad, k, preferred_element_type=f32)
    lqg_ref[...] = lqg.astype(jnp.bfloat16).reshape(t_blk, heads, kvr)
    rqg = scale_factor * jnp.dot(score_grad, kr, preferred_element_type=f32)
    rqg_ref[...] = rqg.astype(jnp.bfloat16).reshape(t_blk, heads, rope)
    lt = scale_factor * lax.dot_general(score_grad, q, tn, preferred_element_type=f32)
    lt = lt + lax.dot_general(rounded, dout, tn, preferred_element_type=f32)
    rt = scale_factor * lax.dot_general(score_grad, qr, tn, preferred_element_type=f32)

    @pl.when(step == 0)
    def _():
        lt_acc[...] = lt
        rt_acc[...] = rt

    @pl.when(step > 0)
    def _():
        lt_acc[...] += lt
        rt_acc[...] += rt

    @pl.when(step == pl.num_programs(0) - 1)
    def _():
        block_len = mine_ref.shape[1]
        n_blocks = lt_acc.shape[0] // block_len
        even = n_blocks % 2 == 0
        side = (offset_ref[0] // block_len) % 2 if even else 0
        for slot in range(mine_ref.shape[0]):
            start = (2 * slot + side) * block_len if even else slot * block_len
            start = pl.multiple_of(start, block_len)
            mine_ref[slot, :, :kvr] = lt_acc[pl.ds(start, block_len), :].astype(jnp.bfloat16)
            mine_ref[slot, :, kvr:] = rt_acc[pl.ds(start, block_len), :].astype(jnp.bfloat16)
        for slot in range(theirs_ref.shape[0]):
            if even:
                start = pl.multiple_of((2 * slot + 1 - side) * block_len, block_len)
                theirs_ref[slot, :, :kvr] = lt_acc[pl.ds(start, block_len), :].astype(jnp.bfloat16)
                theirs_ref[slot, :, kvr:] = rt_acc[pl.ds(start, block_len), :].astype(jnp.bfloat16)
            else:
                theirs_ref[slot] = jnp.zeros(theirs_ref.shape[1:], jnp.bfloat16)


def body(query_latent, query_rope, key_latent, key_rope, output_grad):
    n_ctx = lax.axis_size("ctx")
    n_ep = lax.axis_size("ep")
    _, block_len, heads, kvr = query_latent.shape
    rope = query_rope.shape[2]
    local_keys = jnp.concatenate([key_latent[0], key_rope[0].T], axis=1)
    whole_keys = lax.all_gather(local_keys, "ctx", axis=0, tiled=True)
    length = whole_keys.shape[0]
    offset = (lax.axis_index("ctx") * block_len).astype(jnp.int32).reshape(1)
    qr = jnp.transpose(query_rope[0], (2, 0, 1))
    t_blk = max(1, min(block_len, 2048 // heads))
    while block_len % t_blk:
        t_blk -= 1
    by_rows = pl.BlockSpec((t_blk, heads, kvr), lambda i, off: (i, 0, 0))
    rope_rows = pl.BlockSpec((t_blk, heads, rope), lambda i, off: (i, 0, 0))
    fixed = pl.BlockSpec((length, kvr + rope), lambda i, off: (0, 0))
    n_mine = n_ctx // 2 if n_ctx % 2 == 0 else n_ctx
    n_theirs = n_ctx // 2 if n_ctx % 2 == 0 else 1
    mine_blocks = pl.BlockSpec((n_mine, block_len, kvr + rope), lambda i, off: (0, 0, 0))
    their_blocks = pl.BlockSpec((n_theirs, block_len, kvr + rope), lambda i, off: (0, 0, 0))
    att, lqg, rqg, mine, theirs = pl.pallas_call(
        attention_kernel,
        grid_spec=pltpu.PrefetchScalarGridSpec(
            num_scalar_prefetch=1,
            grid=(block_len // t_blk,),
            in_specs=[by_rows, rope_rows, fixed, by_rows],
            out_specs=[by_rows, by_rows, rope_rows, mine_blocks, their_blocks],
            scratch_shapes=[
                pltpu.VMEM((length, kvr), jnp.float32),
                pltpu.VMEM((length, rope), jnp.float32),
            ],
        ),
        out_shape=[
            jax.ShapeDtypeStruct((block_len, heads, kvr), jnp.bfloat16),
            jax.ShapeDtypeStruct((block_len, heads, kvr), jnp.bfloat16),
            jax.ShapeDtypeStruct((block_len, heads, rope), jnp.bfloat16),
            jax.ShapeDtypeStruct((n_mine, block_len, kvr + rope), jnp.bfloat16),
            jax.ShapeDtypeStruct((n_theirs, block_len, kvr + rope), jnp.bfloat16),
        ],
        compiler_params=pltpu.CompilerParams(dimension_semantics=("arbitrary",)),
    )(offset, query_latent[0], qr, whole_keys, output_grad[0])
    attended = att[None]
    latent_qgrad = lqg[None]
    rope_qgrad = jnp.transpose(rqg, (1, 2, 0))[None]
    total = causal_reduce_ctx(mine, theirs, n_ctx)
    total = butterfly_sum_ep(total, n_ctx, n_ep).astype(jnp.bfloat16)
    latent_kgrad = total[None, :, :kvr]
    rope_kgrad = total[:, kvr:].T[None]
    return (attended, latent_qgrad, rope_qgrad, latent_kgrad, rope_kgrad)


def solution(mesh):
    placed = (
        P(None, "ctx", "ep", None),
        P(None, "ep", None, "ctx"),
        P(None, "ctx", None),
        P(None, None, "ctx"),
        P(None, "ctx", "ep", None),
    )
    return jax.shard_map(
        body,
        mesh=mesh,
        in_specs=placed,
        out_specs=(
            P(None, "ctx", "ep", None),
            P(None, "ctx", "ep", None),
            P(None, "ep", None, "ctx"),
            P(None, "ctx", None),
            P(None, None, "ctx"),
        ),
        check_vma=False,
    )
```

```python
import jax
import jax.numpy as jnp
from jax import lax
from jax.experimental import pallas as pl
from jax.experimental.pallas import tpu as pltpu
from jax.sharding import PartitionSpec as P

scale_factor = 192.0 ** (-0.5)


def causal_reduce_ctx(blocks, theirs, n_ctx):
    here = lax.axis_index("ctx")
    if n_ctx % 2:
        total = jnp.take(blocks, here, axis=0).astype(jnp.float32)
        for shift in range(1, n_ctx):
            sent = jnp.take(blocks, jnp.maximum(here - shift, 0), axis=0)
            got = lax.ppermute(sent, "ctx", [(i, i - shift) for i in range(shift, n_ctx)])
            total = total + got.astype(jnp.float32)
        return total
    pairs = n_ctx // 2
    mine = blocks
    got = lax.ppermute(theirs, "ctx", [(i, i ^ 1) for i in range(n_ctx)])
    summed = (mine.astype(jnp.float32) + got.astype(jnp.float32)).astype(jnp.bfloat16)
    total = jnp.take(summed, here // 2, axis=0).astype(jnp.float32)
    for shift in range(1, pairs):
        sent = jnp.take(summed, jnp.maximum(here // 2 - shift, 0), axis=0)
        got = lax.ppermute(sent, "ctx", [(i, i - 2 * shift) for i in range(2 * shift, n_ctx)])
        total = total + got.astype(jnp.float32)
    return total


def butterfly_sum_ep(total, n_ctx, n_ep):
    if n_ep & (n_ep - 1):
        return lax.psum(total.astype(jnp.bfloat16), "ep").astype(jnp.float32)
    bits = [1 << k for k in range(n_ep.bit_length() - 1)]
    orders = [bits, bits[-1:] + bits[:-1]]
    for step in range(len(bits)):
        pairs = [
            (c * n_ep + e, c * n_ep + (e ^ orders[c % 2][step]))
            for c in range(n_ctx)
            for e in range(n_ep)
        ]
        mine = total.astype(jnp.bfloat16)
        theirs = lax.ppermute(mine, ("ctx", "ep"), pairs)
        total = mine.astype(jnp.float32) + theirs.astype(jnp.float32)
    return total


def attention_kernel(offset_ref, ql_ref, qr_ref, keys_ref, do_ref,
                     att_ref, lqg_ref, rqg_ref, mine_ref, theirs_ref, lt_acc, rt_acc):
    step = pl.program_id(0)
    t_blk, heads, kvr = ql_ref.shape
    rope = qr_ref.shape[2]
    rows = t_blk * heads
    f32 = jnp.float32
    nt = (((1,), (1,)), ((), ()))
    tn = (((0,), (0,)), ((), ()))
    q = ql_ref[...].reshape(rows, kvr)
    qr = qr_ref[...].reshape(rows, rope)
    k = keys_ref[:, :kvr]
    kr = keys_ref[:, kvr:]
    dout = do_ref[...].reshape(rows, kvr)
    length = k.shape[0]
    scores = lax.dot_general(q, k, nt, preferred_element_type=f32)
    scores = scores + lax.dot_general(qr, kr, nt, preferred_element_type=f32)
    row = lax.broadcasted_iota(jnp.int32, (rows, 1), 0)
    last_key = offset_ref[0] + step * t_blk + row // heads
    col = lax.broadcasted_iota(jnp.int32, (1, length), 1)
    scores = jnp.where(col <= last_key, scores * scale_factor, f32(-1e30))
    row_max = jnp.max(scores, axis=-1, keepdims=True)
    powers = jnp.exp(scores - row_max)
    weights = powers * (1.0 / jnp.sum(powers, axis=-1, keepdims=True))
    rounded = weights.astype(jnp.bfloat16)
    att = jnp.dot(rounded, k, preferred_element_type=f32).astype(jnp.bfloat16)
    att_ref[...] = att.reshape(t_blk, heads, kvr)
    row_dots = jnp.sum(dout.astype(f32) * att.astype(f32), axis=-1, keepdims=True)
    weight_grad = lax.dot_general(dout, k, nt, preferred_element_type=f32)
    score_grad = (weights * (weight_grad - row_dots)).astype(jnp.bfloat16)
    lqg = scale_factor * jnp.dot(score_grad, k, preferred_element_type=f32)
    lqg_ref[...] = lqg.astype(jnp.bfloat16).reshape(t_blk, heads, kvr)
    rqg = scale_factor * jnp.dot(score_grad, kr, preferred_element_type=f32)
    rqg_ref[...] = rqg.astype(jnp.bfloat16).reshape(t_blk, heads, rope)
    lt = scale_factor * lax.dot_general(score_grad, q, tn, preferred_element_type=f32)
    lt = lt + lax.dot_general(rounded, dout, tn, preferred_element_type=f32)
    rt = scale_factor * lax.dot_general(score_grad, qr, tn, preferred_element_type=f32)

    block_len = mine_ref.shape[1]
    n_blocks = length // block_len
    even = n_blocks % 2 == 0
    if pl.num_programs(0) == 1 and even:
        side = (offset_ref[0] // block_len) % 2
        for slot in range(n_blocks):
            low, high = 2 * (slot // 2), 2 * (slot // 2) + 1
            if slot % 2 == 0:
                pick = side == 0
                dest = mine_ref
            else:
                pick = side == 1
                dest = theirs_ref
            for acc, cols in ((lt, slice(None, kvr)), (rt, slice(kvr, None))):
                block = jnp.where(
                    pick,
                    acc[low * block_len:(low + 1) * block_len],
                    acc[high * block_len:(high + 1) * block_len],
                )
                dest[slot // 2, :, cols] = block.astype(jnp.bfloat16)
        return

    @pl.when(step == 0)
    def _():
        lt_acc[...] = lt
        rt_acc[...] = rt

    @pl.when(step > 0)
    def _():
        lt_acc[...] += lt
        rt_acc[...] += rt

    @pl.when(step == pl.num_programs(0) - 1)
    def _():
        side = (offset_ref[0] // block_len) % 2 if even else 0
        for slot in range(mine_ref.shape[0]):
            start = (2 * slot + side) * block_len if even else slot * block_len
            start = pl.multiple_of(start, block_len)
            mine_ref[slot, :, :kvr] = lt_acc[pl.ds(start, block_len), :].astype(jnp.bfloat16)
            mine_ref[slot, :, kvr:] = rt_acc[pl.ds(start, block_len), :].astype(jnp.bfloat16)
        for slot in range(theirs_ref.shape[0]):
            if even:
                start = pl.multiple_of((2 * slot + 1 - side) * block_len, block_len)
                theirs_ref[slot, :, :kvr] = lt_acc[pl.ds(start, block_len), :].astype(jnp.bfloat16)
                theirs_ref[slot, :, kvr:] = rt_acc[pl.ds(start, block_len), :].astype(jnp.bfloat16)
            else:
                theirs_ref[slot] = jnp.zeros(theirs_ref.shape[1:], jnp.bfloat16)


def body(query_latent, query_rope, key_latent, key_rope, output_grad):
    n_ctx = lax.axis_size("ctx")
    n_ep = lax.axis_size("ep")
    _, block_len, heads, kvr = query_latent.shape
    rope = query_rope.shape[2]
    local_keys = jnp.concatenate([key_latent[0], key_rope[0].T], axis=1)
    whole_keys = lax.all_gather(local_keys, "ctx", axis=0, tiled=True)
    length = whole_keys.shape[0]
    offset = (lax.axis_index("ctx") * block_len).astype(jnp.int32).reshape(1)
    qr = jnp.transpose(query_rope[0], (2, 0, 1))
    t_blk = max(1, min(block_len, 2048 // heads))
    while block_len % t_blk:
        t_blk -= 1
    by_rows = pl.BlockSpec((t_blk, heads, kvr), lambda i, off: (i, 0, 0))
    rope_rows = pl.BlockSpec((t_blk, heads, rope), lambda i, off: (i, 0, 0))
    fixed = pl.BlockSpec((length, kvr + rope), lambda i, off: (0, 0))
    n_mine = n_ctx // 2 if n_ctx % 2 == 0 else n_ctx
    n_theirs = n_ctx // 2 if n_ctx % 2 == 0 else 1
    mine_blocks = pl.BlockSpec((n_mine, block_len, kvr + rope), lambda i, off: (0, 0, 0))
    their_blocks = pl.BlockSpec((n_theirs, block_len, kvr + rope), lambda i, off: (0, 0, 0))
    att, lqg, rqg, mine, theirs = pl.pallas_call(
        attention_kernel,
        grid_spec=pltpu.PrefetchScalarGridSpec(
            num_scalar_prefetch=1,
            grid=(block_len // t_blk,),
            in_specs=[by_rows, rope_rows, fixed, by_rows],
            out_specs=[by_rows, by_rows, rope_rows, mine_blocks, their_blocks],
            scratch_shapes=[
                pltpu.VMEM((length, kvr), jnp.float32),
                pltpu.VMEM((length, rope), jnp.float32),
            ],
        ),
        out_shape=[
            jax.ShapeDtypeStruct((block_len, heads, kvr), jnp.bfloat16),
            jax.ShapeDtypeStruct((block_len, heads, kvr), jnp.bfloat16),
            jax.ShapeDtypeStruct((block_len, heads, rope), jnp.bfloat16),
            jax.ShapeDtypeStruct((n_mine, block_len, kvr + rope), jnp.bfloat16),
            jax.ShapeDtypeStruct((n_theirs, block_len, kvr + rope), jnp.bfloat16),
        ],
        compiler_params=pltpu.CompilerParams(dimension_semantics=("arbitrary",)),
    )(offset, query_latent[0], qr, whole_keys, output_grad[0])
    attended = att[None]
    latent_qgrad = lqg[None]
    rope_qgrad = jnp.transpose(rqg, (1, 2, 0))[None]
    total = causal_reduce_ctx(mine, theirs, n_ctx)
    total = butterfly_sum_ep(total, n_ctx, n_ep).astype(jnp.bfloat16)
    latent_kgrad = total[None, :, :kvr]
    rope_kgrad = total[:, kvr:].T[None]
    return (attended, latent_qgrad, rope_qgrad, latent_kgrad, rope_kgrad)


def solution(mesh):
    placed = (
        P(None, "ctx", "ep", None),
        P(None, "ep", None, "ctx"),
        P(None, "ctx", None),
        P(None, None, "ctx"),
        P(None, "ctx", "ep", None),
    )
    return jax.shard_map(
        body,
        mesh=mesh,
        in_specs=placed,
        out_specs=(
            P(None, "ctx", "ep", None),
            P(None, "ctx", "ep", None),
            P(None, "ep", None, "ctx"),
            P(None, "ctx", None),
            P(None, None, "ctx"),
        ),
        check_vma=False,
    )
```

```python
import jax
import jax.numpy as jnp
from jax import lax
from jax.experimental import pallas as pl
from jax.experimental.pallas import tpu as pltpu
from jax.sharding import PartitionSpec as P

scale_factor = 192.0 ** (-0.5)


def causal_reduce_ctx(blocks, theirs, n_ctx):
    here = lax.axis_index("ctx")
    if n_ctx % 2:
        total = jnp.take(blocks, here, axis=0).astype(jnp.float32)
        for shift in range(1, n_ctx):
            sent = jnp.take(blocks, jnp.maximum(here - shift, 0), axis=0)
            got = lax.ppermute(sent, "ctx", [(i, i - shift) for i in range(shift, n_ctx)])
            total = total + got.astype(jnp.float32)
        return total
    pairs = n_ctx // 2
    mine = blocks
    got = lax.ppermute(theirs, "ctx", [(i, i ^ 1) for i in range(n_ctx)])
    summed = (mine.astype(jnp.float32) + got.astype(jnp.float32)).astype(jnp.bfloat16)
    total = jnp.take(summed, here // 2, axis=0).astype(jnp.float32)
    for shift in range(1, pairs):
        sent = jnp.take(summed, jnp.maximum(here // 2 - shift, 0), axis=0)
        got = lax.ppermute(sent, "ctx", [(i, i - 2 * shift) for i in range(2 * shift, n_ctx)])
        total = total + got.astype(jnp.float32)
    return total


def butterfly_sum_ep(total, n_ctx, n_ep):
    if n_ep & (n_ep - 1):
        return lax.psum(total.astype(jnp.bfloat16), "ep").astype(jnp.float32)
    bits = [1 << k for k in range(n_ep.bit_length() - 1)]
    orders = [bits, bits[-1:] + bits[:-1]]
    for step in range(len(bits)):
        pairs = [
            (c * n_ep + e, c * n_ep + (e ^ orders[c % 2][step]))
            for c in range(n_ctx)
            for e in range(n_ep)
        ]
        mine = total.astype(jnp.bfloat16)
        theirs = lax.ppermute(mine, ("ctx", "ep"), pairs)
        total = mine.astype(jnp.float32) + theirs.astype(jnp.float32)
    return total


def attention_kernel(offset_ref, ql_ref, qr_ref, keys_ref, do_ref,
                     att_hbm, lqg_ref, rqg_ref, mine_ref, theirs_ref, lt_acc, rt_acc,
                     att_ref, att_sem):
    step = pl.program_id(0)
    t_blk, heads, kvr = ql_ref.shape
    rope = qr_ref.shape[2]
    rows = t_blk * heads
    f32 = jnp.float32
    nt = (((1,), (1,)), ((), ()))
    tn = (((0,), (0,)), ((), ()))
    q = ql_ref[...].reshape(rows, kvr)
    qr = qr_ref[...].reshape(rows, rope)
    k = keys_ref[:, :kvr]
    kr = keys_ref[:, kvr:]
    dout = do_ref[...].reshape(rows, kvr)
    length = k.shape[0]
    scores = lax.dot_general(q, k, nt, preferred_element_type=f32)
    scores = scores + lax.dot_general(qr, kr, nt, preferred_element_type=f32)
    row = lax.broadcasted_iota(jnp.int32, (rows, 1), 0)
    last_key = offset_ref[0] + step * t_blk + row // heads
    col = lax.broadcasted_iota(jnp.int32, (1, length), 1)
    scores = jnp.where(col <= last_key, scores * scale_factor, f32(-1e30))
    row_max = jnp.max(scores, axis=-1, keepdims=True)
    powers = jnp.exp(scores - row_max)
    weights = powers * (1.0 / jnp.sum(powers, axis=-1, keepdims=True))
    rounded = weights.astype(jnp.bfloat16)
    att = jnp.dot(rounded, k, preferred_element_type=f32).astype(jnp.bfloat16)
    att_ref[...] = att.reshape(t_blk, heads, kvr)
    att_copy = pltpu.make_async_copy(att_ref, att_hbm.at[pl.ds(step * t_blk, t_blk)], att_sem)
    att_copy.start()
    row_dots = jnp.sum(dout.astype(f32) * att.astype(f32), axis=-1, keepdims=True)
    weight_grad = lax.dot_general(dout, k, nt, preferred_element_type=f32)
    score_grad = (weights * (weight_grad - row_dots)).astype(jnp.bfloat16)
    lqg = scale_factor * jnp.dot(score_grad, k, preferred_element_type=f32)
    lqg_ref[...] = lqg.astype(jnp.bfloat16).reshape(t_blk, heads, kvr)
    rqg = scale_factor * jnp.dot(score_grad, kr, preferred_element_type=f32)
    rqg_ref[...] = rqg.astype(jnp.bfloat16).reshape(t_blk, heads, rope)
    lt = scale_factor * lax.dot_general(score_grad, q, tn, preferred_element_type=f32)
    lt = lt + lax.dot_general(rounded, dout, tn, preferred_element_type=f32)
    rt = scale_factor * lax.dot_general(score_grad, qr, tn, preferred_element_type=f32)

    block_len = mine_ref.shape[1]
    n_blocks = length // block_len
    even = n_blocks % 2 == 0
    if pl.num_programs(0) == 1 and even:
        side = (offset_ref[0] // block_len) % 2
        for slot in range(n_blocks):
            low, high = 2 * (slot // 2), 2 * (slot // 2) + 1
            if slot % 2 == 0:
                pick = side == 0
                dest = mine_ref
            else:
                pick = side == 1
                dest = theirs_ref
            for acc, cols in ((lt, slice(None, kvr)), (rt, slice(kvr, None))):
                block = jnp.where(
                    pick,
                    acc[low * block_len:(low + 1) * block_len],
                    acc[high * block_len:(high + 1) * block_len],
                )
                dest[slot // 2, :, cols] = block.astype(jnp.bfloat16)
        att_copy.wait()
        return
    att_copy.wait()

    @pl.when(step == 0)
    def _():
        lt_acc[...] = lt
        rt_acc[...] = rt

    @pl.when(step > 0)
    def _():
        lt_acc[...] += lt
        rt_acc[...] += rt

    @pl.when(step == pl.num_programs(0) - 1)
    def _():
        side = (offset_ref[0] // block_len) % 2 if even else 0
        for slot in range(mine_ref.shape[0]):
            start = (2 * slot + side) * block_len if even else slot * block_len
            start = pl.multiple_of(start, block_len)
            mine_ref[slot, :, :kvr] = lt_acc[pl.ds(start, block_len), :].astype(jnp.bfloat16)
            mine_ref[slot, :, kvr:] = rt_acc[pl.ds(start, block_len), :].astype(jnp.bfloat16)
        for slot in range(theirs_ref.shape[0]):
            if even:
                start = pl.multiple_of((2 * slot + 1 - side) * block_len, block_len)
                theirs_ref[slot, :, :kvr] = lt_acc[pl.ds(start, block_len), :].astype(jnp.bfloat16)
                theirs_ref[slot, :, kvr:] = rt_acc[pl.ds(start, block_len), :].astype(jnp.bfloat16)
            else:
                theirs_ref[slot] = jnp.zeros(theirs_ref.shape[1:], jnp.bfloat16)


def body(query_latent, query_rope, key_latent, key_rope, output_grad):
    n_ctx = lax.axis_size("ctx")
    n_ep = lax.axis_size("ep")
    _, block_len, heads, kvr = query_latent.shape
    rope = query_rope.shape[2]
    local_keys = jnp.concatenate([key_latent[0], key_rope[0].T], axis=1)
    whole_keys = lax.all_gather(local_keys, "ctx", axis=0, tiled=True)
    length = whole_keys.shape[0]
    offset = (lax.axis_index("ctx") * block_len).astype(jnp.int32).reshape(1)
    qr = jnp.transpose(query_rope[0], (2, 0, 1))
    t_blk = max(1, min(block_len, 2048 // heads))
    while block_len % t_blk:
        t_blk -= 1
    by_rows = pl.BlockSpec((t_blk, heads, kvr), lambda i, off: (i, 0, 0))
    rope_rows = pl.BlockSpec((t_blk, heads, rope), lambda i, off: (i, 0, 0))
    fixed = pl.BlockSpec((length, kvr + rope), lambda i, off: (0, 0))
    n_mine = n_ctx // 2 if n_ctx % 2 == 0 else n_ctx
    n_theirs = n_ctx // 2 if n_ctx % 2 == 0 else 1
    mine_blocks = pl.BlockSpec((n_mine, block_len, kvr + rope), lambda i, off: (0, 0, 0))
    their_blocks = pl.BlockSpec((n_theirs, block_len, kvr + rope), lambda i, off: (0, 0, 0))
    att, lqg, rqg, mine, theirs = pl.pallas_call(
        attention_kernel,
        grid_spec=pltpu.PrefetchScalarGridSpec(
            num_scalar_prefetch=1,
            grid=(block_len // t_blk,),
            in_specs=[by_rows, rope_rows, fixed, by_rows],
            out_specs=[
                pl.BlockSpec(memory_space=pl.ANY),
                by_rows,
                rope_rows,
                mine_blocks,
                their_blocks,
            ],
            scratch_shapes=[
                pltpu.VMEM((length, kvr), jnp.float32),
                pltpu.VMEM((length, rope), jnp.float32),
                pltpu.VMEM((t_blk, heads, kvr), jnp.bfloat16),
                pltpu.SemaphoreType.DMA,
            ],
        ),
        out_shape=[
            jax.ShapeDtypeStruct((block_len, heads, kvr), jnp.bfloat16),
            jax.ShapeDtypeStruct((block_len, heads, kvr), jnp.bfloat16),
            jax.ShapeDtypeStruct((block_len, heads, rope), jnp.bfloat16),
            jax.ShapeDtypeStruct((n_mine, block_len, kvr + rope), jnp.bfloat16),
            jax.ShapeDtypeStruct((n_theirs, block_len, kvr + rope), jnp.bfloat16),
        ],
        compiler_params=pltpu.CompilerParams(dimension_semantics=("arbitrary",)),
    )(offset, query_latent[0], qr, whole_keys, output_grad[0])
    attended = att[None]
    latent_qgrad = lqg[None]
    rope_qgrad = jnp.transpose(rqg, (1, 2, 0))[None]
    total = causal_reduce_ctx(mine, theirs, n_ctx)
    total = butterfly_sum_ep(total, n_ctx, n_ep).astype(jnp.bfloat16)
    latent_kgrad = total[None, :, :kvr]
    rope_kgrad = total[:, kvr:].T[None]
    return (attended, latent_qgrad, rope_qgrad, latent_kgrad, rope_kgrad)


def solution(mesh):
    placed = (
        P(None, "ctx", "ep", None),
        P(None, "ep", None, "ctx"),
        P(None, "ctx", None),
        P(None, None, "ctx"),
        P(None, "ctx", "ep", None),
    )
    return jax.shard_map(
        body,
        mesh=mesh,
        in_specs=placed,
        out_specs=(
            P(None, "ctx", "ep", None),
            P(None, "ctx", "ep", None),
            P(None, "ep", None, "ctx"),
            P(None, "ctx", None),
            P(None, None, "ctx"),
        ),
        check_vma=False,
    )
```

```python
import jax
import jax.numpy as jnp
from jax import lax
from jax.experimental import pallas as pl
from jax.experimental.pallas import tpu as pltpu
from jax.sharding import PartitionSpec as P

scale_factor = 192.0 ** (-0.5)


def causal_reduce_ctx(blocks, theirs, n_ctx):
    here = lax.axis_index("ctx")
    if n_ctx % 2:
        total = jnp.take(blocks, here, axis=0).astype(jnp.float32)
        for shift in range(1, n_ctx):
            sent = jnp.take(blocks, jnp.maximum(here - shift, 0), axis=0)
            got = lax.ppermute(sent, "ctx", [(i, i - shift) for i in range(shift, n_ctx)])
            total = total + got.astype(jnp.float32)
        return total
    pairs = n_ctx // 2
    mine = blocks
    got = lax.ppermute(theirs, "ctx", [(i, i ^ 1) for i in range(n_ctx)])
    summed = (mine.astype(jnp.float32) + got.astype(jnp.float32)).astype(jnp.bfloat16)
    total = jnp.take(summed, here // 2, axis=0).astype(jnp.float32)
    for shift in range(1, pairs):
        sent = jnp.take(summed, jnp.maximum(here // 2 - shift, 0), axis=0)
        got = lax.ppermute(sent, "ctx", [(i, i - 2 * shift) for i in range(2 * shift, n_ctx)])
        total = total + got.astype(jnp.float32)
    return total


def butterfly_sum_ep(total, n_ctx, n_ep):
    if n_ep & (n_ep - 1):
        return lax.psum(total.astype(jnp.bfloat16), "ep").astype(jnp.float32)
    bits = [1 << k for k in range(n_ep.bit_length() - 1)]
    orders = [bits[1:2] + bits[:1] + bits[2:], bits[:1] + bits[2:] + bits[1:2]]
    for step in range(len(bits)):
        pairs = [
            (c * n_ep + e, c * n_ep + (e ^ orders[c % 2][step]))
            for c in range(n_ctx)
            for e in range(n_ep)
        ]
        mine = total.astype(jnp.bfloat16)
        theirs = lax.ppermute(mine, ("ctx", "ep"), pairs)
        total = mine.astype(jnp.float32) + theirs.astype(jnp.float32)
    return total


def attention_kernel(offset_ref, ql_ref, qr_ref, keys_ref, do_ref,
                     att_ref, lqg_ref, rqg_ref, mine_ref, theirs_ref, lt_acc, rt_acc):
    step = pl.program_id(0)
    t_blk, heads, kvr = ql_ref.shape
    rope = qr_ref.shape[2]
    rows = t_blk * heads
    f32 = jnp.float32
    nt = (((1,), (1,)), ((), ()))
    tn = (((0,), (0,)), ((), ()))
    q = ql_ref[...].reshape(rows, kvr)
    qr = qr_ref[...].reshape(rows, rope)
    k = keys_ref[:, :kvr]
    kr = keys_ref[:, kvr:]
    dout = do_ref[...].reshape(rows, kvr)
    length = k.shape[0]
    scores = lax.dot_general(q, k, nt, preferred_element_type=f32)
    scores = scores + lax.dot_general(qr, kr, nt, preferred_element_type=f32)
    row = lax.broadcasted_iota(jnp.int32, (rows, 1), 0)
    last_key = offset_ref[0] + step * t_blk + row // heads
    col = lax.broadcasted_iota(jnp.int32, (1, length), 1)
    scores = jnp.where(col <= last_key, scores * scale_factor, f32(-1e30))
    row_max = jnp.max(scores, axis=-1, keepdims=True)
    powers = jnp.exp(scores - row_max)
    weights = powers * (1.0 / jnp.sum(powers, axis=-1, keepdims=True))
    rounded = weights.astype(jnp.bfloat16)
    att = jnp.dot(rounded, k, preferred_element_type=f32).astype(jnp.bfloat16)
    att_ref[...] = att.reshape(t_blk, heads, kvr)
    row_dots = jnp.sum(dout.astype(f32) * att.astype(f32), axis=-1, keepdims=True)
    weight_grad = lax.dot_general(dout, k, nt, preferred_element_type=f32)
    score_grad = (weights * (weight_grad - row_dots)).astype(jnp.bfloat16)
    lqg = scale_factor * jnp.dot(score_grad, k, preferred_element_type=f32)
    lqg_ref[...] = lqg.astype(jnp.bfloat16).reshape(t_blk, heads, kvr)
    rqg = scale_factor * jnp.dot(score_grad, kr, preferred_element_type=f32)
    rqg_ref[...] = rqg.astype(jnp.bfloat16).reshape(t_blk, heads, rope)
    lt = scale_factor * lax.dot_general(score_grad, q, tn, preferred_element_type=f32)
    lt = lt + lax.dot_general(rounded, dout, tn, preferred_element_type=f32)
    rt = scale_factor * lax.dot_general(score_grad, qr, tn, preferred_element_type=f32)

    block_len = mine_ref.shape[1]
    n_blocks = length // block_len
    even = n_blocks % 2 == 0
    if pl.num_programs(0) == 1 and even:
        side = (offset_ref[0] // block_len) % 2
        for slot in range(n_blocks):
            low, high = 2 * (slot // 2), 2 * (slot // 2) + 1
            if slot % 2 == 0:
                pick = side == 0
                dest = mine_ref
            else:
                pick = side == 1
                dest = theirs_ref
            for acc, cols in ((lt, slice(None, kvr)), (rt, slice(kvr, None))):
                block = jnp.where(
                    pick,
                    acc[low * block_len:(low + 1) * block_len],
                    acc[high * block_len:(high + 1) * block_len],
                )
                dest[slot // 2, :, cols] = block.astype(jnp.bfloat16)
        return

    @pl.when(step == 0)
    def _():
        lt_acc[...] = lt
        rt_acc[...] = rt

    @pl.when(step > 0)
    def _():
        lt_acc[...] += lt
        rt_acc[...] += rt

    @pl.when(step == pl.num_programs(0) - 1)
    def _():
        side = (offset_ref[0] // block_len) % 2 if even else 0
        for slot in range(mine_ref.shape[0]):
            start = (2 * slot + side) * block_len if even else slot * block_len
            start = pl.multiple_of(start, block_len)
            mine_ref[slot, :, :kvr] = lt_acc[pl.ds(start, block_len), :].astype(jnp.bfloat16)
            mine_ref[slot, :, kvr:] = rt_acc[pl.ds(start, block_len), :].astype(jnp.bfloat16)
        for slot in range(theirs_ref.shape[0]):
            if even:
                start = pl.multiple_of((2 * slot + 1 - side) * block_len, block_len)
                theirs_ref[slot, :, :kvr] = lt_acc[pl.ds(start, block_len), :].astype(jnp.bfloat16)
                theirs_ref[slot, :, kvr:] = rt_acc[pl.ds(start, block_len), :].astype(jnp.bfloat16)
            else:
                theirs_ref[slot] = jnp.zeros(theirs_ref.shape[1:], jnp.bfloat16)


def body(query_latent, query_rope, key_latent, key_rope, output_grad):
    n_ctx = lax.axis_size("ctx")
    n_ep = lax.axis_size("ep")
    _, block_len, heads, kvr = query_latent.shape
    rope = query_rope.shape[2]
    local_keys = jnp.concatenate([key_latent[0], key_rope[0].T], axis=1)
    whole_keys = lax.all_gather(local_keys, "ctx", axis=0, tiled=True)
    length = whole_keys.shape[0]
    offset = (lax.axis_index("ctx") * block_len).astype(jnp.int32).reshape(1)
    qr = jnp.transpose(query_rope[0], (2, 0, 1))
    t_blk = max(1, min(block_len, 2048 // heads))
    while block_len % t_blk:
        t_blk -= 1
    by_rows = pl.BlockSpec((t_blk, heads, kvr), lambda i, off: (i, 0, 0))
    rope_rows = pl.BlockSpec((t_blk, heads, rope), lambda i, off: (i, 0, 0))
    fixed = pl.BlockSpec((length, kvr + rope), lambda i, off: (0, 0))
    n_mine = n_ctx // 2 if n_ctx % 2 == 0 else n_ctx
    n_theirs = n_ctx // 2 if n_ctx % 2 == 0 else 1
    mine_blocks = pl.BlockSpec((n_mine, block_len, kvr + rope), lambda i, off: (0, 0, 0))
    their_blocks = pl.BlockSpec((n_theirs, block_len, kvr + rope), lambda i, off: (0, 0, 0))
    att, lqg, rqg, mine, theirs = pl.pallas_call(
        attention_kernel,
        grid_spec=pltpu.PrefetchScalarGridSpec(
            num_scalar_prefetch=1,
            grid=(block_len // t_blk,),
            in_specs=[by_rows, rope_rows, fixed, by_rows],
            out_specs=[by_rows, by_rows, rope_rows, mine_blocks, their_blocks],
            scratch_shapes=[
                pltpu.VMEM((length, kvr), jnp.float32),
                pltpu.VMEM((length, rope), jnp.float32),
            ],
        ),
        out_shape=[
            jax.ShapeDtypeStruct((block_len, heads, kvr), jnp.bfloat16),
            jax.ShapeDtypeStruct((block_len, heads, kvr), jnp.bfloat16),
            jax.ShapeDtypeStruct((block_len, heads, rope), jnp.bfloat16),
            jax.ShapeDtypeStruct((n_mine, block_len, kvr + rope), jnp.bfloat16),
            jax.ShapeDtypeStruct((n_theirs, block_len, kvr + rope), jnp.bfloat16),
        ],
        compiler_params=pltpu.CompilerParams(dimension_semantics=("arbitrary",)),
    )(offset, query_latent[0], qr, whole_keys, output_grad[0])
    attended = att[None]
    latent_qgrad = lqg[None]
    rope_qgrad = jnp.transpose(rqg, (1, 2, 0))[None]
    total = causal_reduce_ctx(mine, theirs, n_ctx)
    total = butterfly_sum_ep(total, n_ctx, n_ep).astype(jnp.bfloat16)
    latent_kgrad = total[None, :, :kvr]
    rope_kgrad = total[:, kvr:].T[None]
    return (attended, latent_qgrad, rope_qgrad, latent_kgrad, rope_kgrad)


def solution(mesh):
    placed = (
        P(None, "ctx", "ep", None),
        P(None, "ep", None, "ctx"),
        P(None, "ctx", None),
        P(None, None, "ctx"),
        P(None, "ctx", "ep", None),
    )
    return jax.shard_map(
        body,
        mesh=mesh,
        in_specs=placed,
        out_specs=(
            P(None, "ctx", "ep", None),
            P(None, "ctx", "ep", None),
            P(None, "ep", None, "ctx"),
            P(None, "ctx", None),
            P(None, None, "ctx"),
        ),
        check_vma=False,
    )
```
